32 devices in a mesh: src: 8 (over z, x), tgt: 4 (over y, core).
Axes of the slice: x: 2, y: 2, z: 4, core: 2. Of those that a mesh axis runs over, the one named last changes fastest.
Arguments:
- src_emb: bfloat16 [64, 16384], P(None, 'src'), may hold values from -2.75 to 2.75
- tgt_emb: bfloat16 [64, 32768], P(None, 'tgt'), may hold values from -2.75 to 2.75
- target_features: bfloat16 [128, 32768], P(None, 'tgt'), may hold values from -6 to 6
- src_mass: float32 [16384], P('src'), may hold values from 1 to 10
- tgt_mass: float32 [32768], P('tgt'), may hold values from 1 to 10
- kept_blocks: int32 [64, 32], P('src', 'tgt'), may hold values from 0 to 31, as said below
- kept_count: int32 [64, 4], P('src', 'tgt'), may hold values from 1 to 8
Outputs:
- projected: float32 [16384, 128], P(('src', 'tgt'))
- src_potential: float32 [16384], P('src')
- tgt_potential: float32 [32768], P('tgt')
The draws below stay inside these ranges and needn't reach their ends.
Inputs may be any that keep to these rules, and one draw needn't show every extreme that they name: `kept_blocks`: entry [r, t * 8 + k] is a block number within target shard t; the 8 entries of one group are distinct; the first kept_count[r, t] of them are kept, the others are unused; every target block is kept by some source block row.
All inputs are finite; a program needn't handle non-finite values.
Results may differ from the reference program's by a relative error of at most 0.00075.
Values sent between devices are 32-bit elements; how exact they have to be, the bound alone decides.
No kernel may reach another device: no remote copies, remote signals or barrier semaphores. Data moves between devices by JAX's collectives and lax.ppermute only.
A program may use at most 64 MiB of HBM per device.

```python
import math
import jax
import jax.numpy as jnp
from jax import lax

DIM = 64
FEAT = 128
BLOCK = 256
KSH = 8
ITERS = 2
TGT_DEV = 8192
NS = 16384
NT = 32768
NSB = 64
TBD = 32
N_TGT = 4


def embedding_pair(key):
    base = jax.random.fold_in(key, 37)
    keys = jax.random.split(base, 7)
    src_values = 0.125 * jnp.clip(jax.random.normal(keys[0], (DIM, NS), jnp.float32), -4.0, 4.0)
    tgt_values = 0.125 * jnp.clip(jax.random.normal(keys[1], (DIM, NT), jnp.float32), -4.0, 4.0)
    strength = jax.random.uniform(keys[5], (1, NS), jnp.float32, 1.0, 1.5)
    signs = jnp.where(jax.random.uniform(keys[6], (1, NS), jnp.float32) < 0.5, -1.0, 1.0)
    far_cells = (jnp.arange(NS, dtype=jnp.int32) % 16 == 7)[None, :]
    src_values = jnp.where(far_cells, src_values + strength * signs, src_values)
    src_values = jnp.clip(src_values, -2.75, 2.75)
    tgt_values = jnp.clip(tgt_values, -2.75, 2.75)
    return (src_values, tgt_values)


def draw_src_emb(key, part):
    return embedding_pair(key)[0].astype(jnp.bfloat16)


def draw_tgt_emb(key, part):
    return embedding_pair(key)[1].astype(jnp.bfloat16)


def draw_kept_blocks(key, part):
    base = jax.random.fold_in(key, 11)
    shards = NT // TGT_DEV
    scores = jax.random.randint(base, (NSB, shards, TBD - 1), 0, 1 << 20, jnp.int32) * (TBD - 1)
    scores = scores + jnp.arange(TBD - 1, dtype=jnp.int32)
    order = (jnp.argsort(scores, axis=-1)[:, :, :KSH - 1] + 1).astype(jnp.int32)
    block_displacements = jnp.concatenate([jnp.zeros((NSB, shards, 1), jnp.int32), order], axis=-1)
    rows = jnp.arange(NSB, dtype=jnp.int32)
    blocks = (rows[:, None, None] + block_displacements) % TBD
    return blocks.reshape(NSB, shards * KSH).astype(jnp.int32)


def draw_kept_count(key, part):
    base = jax.random.fold_in(key, 23)
    keys = jax.random.split(base, 3)
    shards = NT // TGT_DEV
    shape = (NSB, shards)
    lower = jnp.minimum(jax.random.randint(keys[0], shape, 0, KSH, jnp.int32), jax.random.randint(keys[1], shape, 0, KSH, jnp.int32)) + 1
    heavy = jax.random.randint(keys[2], shape, 0, 4, jnp.int32) == 0
    leading = (jnp.arange(NSB, dtype=jnp.int32)[:, None] == 0) & (jnp.arange(shards, dtype=jnp.int32)[None, :] == 0)
    return jnp.where(heavy | leading, KSH, lower).astype(jnp.int32)


def block_levels(own_key, dims, cuts, least, top_value):
    factor_of = 1.0
    for axis_at, parts in cuts:
        draws = jax.random.uniform(jax.random.fold_in(jax.random.fold_in(own_key, 6), axis_at), (parts,), jnp.float32, least / len(cuts), top_value / len(cuts))
        factor_of = factor_of * jnp.repeat(jnp.exp(draws), dims[axis_at] // parts).reshape((-1,) + (1,) * (len(dims) - 1 - axis_at))
    return factor_of


def gaussian(own_key, shape, spread, bound, cuts=(), kind=jnp.bfloat16):
    values = jax.random.normal(own_key, shape, jnp.float32) * spread
    if len(cuts) > 0:
        values = block_levels(own_key, shape, cuts, -0.22, 0.18) * values
    return jnp.clip(values, min=-bound, max=bound).astype(kind)


def setup_inputs(seed: int = 0) -> dict:
    streams_of = jax.random.split(jax.random.key(seed), 8)
    src_emb = draw_src_emb(jax.random.fold_in(streams_of[7], 71), 0)
    tgt_emb = draw_tgt_emb(jax.random.fold_in(streams_of[7], 71), 0)
    target_features = gaussian(streams_of[2], (FEAT, NT), 1.0, 6.0, ((1, 4),))
    src_mass = jnp.clip(jnp.exp(math.log(10.0) - 2.3025851 * jax.random.uniform(streams_of[3], (NS,), jnp.float32) ** block_levels(streams_of[3], (NS,), ((0, 8),), -0.2, 0.2)), 1.0, 10.0)
    tgt_mass = jnp.clip(jnp.exp(math.log(10.0) - 2.3025851 * jax.random.uniform(streams_of[4], (NT,), jnp.float32) ** block_levels(streams_of[4], (NT,), ((0, 4),), -0.2, 0.2)), 1.0, 10.0)
    kept_blocks = draw_kept_blocks(jax.random.fold_in(streams_of[7], 71), 0)
    kept_count = draw_kept_count(jax.random.fold_in(streams_of[7], 71), 0)
    return {"src_emb": src_emb, "tgt_emb": tgt_emb, "target_features": target_features, "src_mass": src_mass, "tgt_mass": tgt_mass, "kept_blocks": kept_blocks, "kept_count": kept_count}


SENTINEL = -1.0e30
EPSILON = 0.1


def reference(src_emb, tgt_emb, target_features, src_mass, tgt_mass, kept_blocks, kept_count):
    every_block_list = N_TGT * TBD
    src_float = src_emb.astype(jnp.float32)
    tgt_float = tgt_emb.astype(jnp.float32)
    src_tiles = src_float.reshape(DIM, NSB, BLOCK).transpose(1, 0, 2)
    src_norm = jnp.sum(jnp.square(src_float), axis=0).reshape(NSB, BLOCK)
    tgt_tiles = tgt_float.reshape(DIM, every_block_list, BLOCK)
    target_norm = jnp.sum(jnp.square(tgt_float), axis=0).reshape(every_block_list, BLOCK)
    feat_tiles = target_features.astype(jnp.float32).reshape(FEAT, every_block_list, BLOCK)
    slot_ids = jnp.arange(N_TGT * KSH, dtype=jnp.int32)
    global_index = (kept_blocks + (slot_ids // KSH) * TBD).astype(jnp.int32)
    live_slot = (slot_ids % KSH)[None, :] < jnp.repeat(kept_count, KSH, axis=1)
    packets = (src_tiles, src_norm, global_index, live_slot)

    def distances(packet):
        products = jnp.einsum("dr,dkc->krc", packet[0], jnp.take(tgt_tiles, packet[2], axis=1))
        return packet[1][None, :, None] + jnp.take(target_norm, packet[2], axis=0)[:, None, :] - 2.0 * products

    def row_scaled(potential_tiles, packet):
        scaled = (jnp.take(potential_tiles, packet[2], axis=0)[:, None, :] - distances(packet)) / EPSILON
        return jnp.where(packet[3][:, None, None], scaled, SENTINEL)

    def row_pass(potential):
        potential_tiles = potential.reshape(every_block_list, BLOCK)

        def per_block(packet):
            scaled = row_scaled(potential_tiles, packet)
            highest = jnp.max(scaled, axis=(0, 2))
            totals = jnp.sum(jnp.where(packet[3][:, None, None], jnp.exp(scaled - highest[None, :, None]), 0.0), axis=(0, 2))
            return highest + jnp.log(totals)

        return lax.map(per_block, packets).reshape(NS)

    def column_pass(potential):
        potential_tiles = potential.reshape(NSB, BLOCK)

        def per_block(carry, packet):
            block_top, block_sum = carry
            scaled = (packet[4][None, :, None] - distances(packet)) / EPSILON
            scaled = jnp.where(packet[3][:, None, None], scaled, SENTINEL)
            highest = jnp.max(scaled, axis=1)
            totals = jnp.sum(jnp.where(packet[3][:, None, None], jnp.exp(scaled - highest[:, None, :]), 0.0), axis=1)
            new_top = block_top.at[packet[2]].max(highest)
            rescaled = block_sum * jnp.exp(block_top - new_top)
            added = rescaled.at[packet[2]].add(totals * jnp.exp(highest - jnp.take(new_top, packet[2], axis=0)))
            return (new_top, added), None

        start = (jnp.full((every_block_list, BLOCK), SENTINEL, jnp.float32), jnp.zeros((every_block_list, BLOCK), jnp.float32))
        (block_top, block_sum), discarded_value = lax.scan(per_block, start, packets + (potential_tiles,))
        return (block_top + jnp.log(block_sum)).reshape(NT)

    tgt_potential = jnp.zeros((NT,), jnp.float32)
    src_potential = jnp.zeros((NS,), jnp.float32)
    for iteration in range(ITERS):
        src_potential = EPSILON * jnp.log(src_mass) - EPSILON * row_pass(tgt_potential)
        tgt_potential = EPSILON * jnp.log(tgt_mass) - EPSILON * column_pass(src_potential)

    final_tiles = tgt_potential.reshape(every_block_list, BLOCK)

    def plan_block(packet):
        scaled = row_scaled(final_tiles, packet).reshape(N_TGT, KSH, BLOCK, BLOCK)
        live = packet[3].reshape(N_TGT, KSH)
        shard_top = jnp.max(scaled, axis=(1, 3))
        weights = jnp.where(live[:, :, None, None], jnp.exp(scaled - shard_top[:, None, :, None]), 0.0)
        rounded_count = lax.optimization_barrier(weights.astype(jnp.bfloat16)).astype(jnp.float32)
        feature_matrix = jnp.take(feat_tiles, packet[2], axis=1).reshape(FEAT, N_TGT, KSH, BLOCK)
        partial_numerator = jnp.einsum("pmsx,hpmx->psh", rounded_count, feature_matrix)
        shard_den = jnp.sum(rounded_count, axis=(1, 3))
        top = jnp.max(shard_top, axis=0)
        factor = jnp.exp(shard_top - top[None, :])
        numerator = jnp.sum(partial_numerator * factor[:, :, None], axis=0)
        denominator = jnp.sum(shard_den * factor, axis=0)
        return numerator / denominator[:, None]

    projected = lax.map(plan_block, packets).reshape(NS, FEAT)
    return projected, src_potential, tgt_potential
```

```python
import jax
import jax.numpy as jnp
from jax import lax
from jax.sharding import PartitionSpec as P

BLOCK = 256
ITERS = 2


SENTINEL = -1e30
EPSILON = 0.1


def pair_distance(src_tile, norm_tile, tgt_chosen, tgt_norm_chosen):
    products = jnp.einsum("dr,dkc->krc", src_tile, tgt_chosen, preferred_element_type=jnp.float32)
    return norm_tile[None, :, None] + tgt_norm_chosen[:, None, :] - 2.0 * products


def lse_pair(top, total, other_top, other_total):
    overall = jnp.maximum(top, other_top)
    return (overall, total * jnp.exp(top - overall) + other_total * jnp.exp(other_top - overall))


def butterfly_lse(highest, totals, axis):
    size = lax.axis_size(axis)
    step = 1
    while step < size:
        pairs = [(i, i ^ step) for i in range(size)]
        other = lax.ppermute(jnp.stack([highest, totals]), axis, pairs)
        highest, totals = lse_pair(highest, totals, other[0], other[1])
        step *= 2
    return (highest, totals)


def merge_rows(highest, totals):
    return butterfly_lse(highest, totals, "tgt")


def merge_columns(block_top, block_sum):
    return butterfly_lse(block_top, block_sum, "src")


def halving_merge(top, numerator, denominator, axis):
    size = lax.axis_size(axis)
    me = lax.axis_index(axis)
    rows = top.shape[0] // size
    top = top.reshape(size, rows)
    denominator = denominator.reshape(size, rows)
    numerator = numerator.reshape(size, rows, numerator.shape[-1])
    step = 1
    while step < size:
        pairs = [(i, i ^ step) for i in range(size)]
        keep = (me // step) % 2
        count = top.shape[0] // 2

        def split(x):
            x = x.reshape((count, 2) + x.shape[1:])
            return (
                lax.dynamic_index_in_dim(x, keep, axis=1, keepdims=False),
                lax.dynamic_index_in_dim(x, 1 - keep, axis=1, keepdims=False),
            )

        top_keep, top_send = split(top)
        den_keep, den_send = split(denominator)
        num_keep, num_send = split(numerator)
        small = lax.ppermute(jnp.stack([top_send, den_send]), axis, pairs)
        num_other = lax.ppermute(num_send, axis, pairs)
        overall = jnp.maximum(top_keep, small[0])
        mine = jnp.exp(top_keep - overall)
        theirs = jnp.exp(small[0] - overall)
        numerator = num_keep * mine[..., None] + num_other * theirs[..., None]
        denominator = den_keep * mine + small[1] * theirs
        top = overall
        step *= 2
    return (numerator.reshape(rows, -1), denominator.reshape(rows))


def shards(src_emb, tgt_emb, target_features, src_mass, tgt_mass, kept_blocks, kept_count):
    emb_width = src_emb.shape[0]
    src_rows = src_emb.shape[1]
    tgt_rows = tgt_emb.shape[1]
    src_blocks = src_rows // BLOCK
    tgt_blocks = tgt_rows // BLOCK
    slot_count = kept_blocks.shape[1]
    src_tiles = src_emb.reshape(emb_width, src_blocks, BLOCK).transpose(1, 0, 2)
    src_norm = jnp.sum(jnp.square(src_emb.astype(jnp.float32)), axis=0).reshape(src_blocks, BLOCK)
    tgt_tiles = tgt_emb.reshape(emb_width, tgt_blocks, BLOCK)
    target_norm = jnp.sum(jnp.square(tgt_emb.astype(jnp.float32)), axis=0).reshape(
        tgt_blocks, BLOCK
    )
    feat_tiles = target_features.reshape(target_features.shape[0], tgt_blocks, BLOCK)
    live_slot = lax.broadcasted_iota(jnp.int32, (src_blocks, slot_count), 1) < kept_count
    packets = (src_tiles, src_norm, kept_blocks, live_slot)
    flat_index = kept_blocks.reshape(-1)
    member = (
        lax.broadcasted_iota(jnp.int32, (tgt_blocks, flat_index.shape[0]), 0) == flat_index[None, :]
    )

    def distances(packet):
        return pair_distance(
            packet[0],
            packet[1],
            jnp.take(tgt_tiles, packet[2], axis=1),
            jnp.take(target_norm, packet[2], axis=0),
        )

    def row_scaled(potential_tiles, packet):
        scaled = (
            jnp.take(potential_tiles, packet[2], axis=0)[:, None, :] - distances(packet)
        ) / EPSILON
        return jnp.where(packet[3][:, None, None], scaled, SENTINEL)

    tgt_potential = jnp.zeros((tgt_rows,), jnp.float32)
    src_potential = jnp.zeros((src_rows,), jnp.float32)
    for iteration in range(ITERS):
        row_potential_tiles = tgt_potential.reshape(tgt_blocks, BLOCK)

        def row_per_block(packet):
            scaled = row_scaled(row_potential_tiles, packet)
            highest = jnp.max(scaled, axis=(0, 2))
            totals = jnp.sum(
                jnp.where(packet[3][:, None, None], jnp.exp(scaled - highest[None, :, None]), 0.0),
                axis=(0, 2),
            )
            return (highest, totals)

        highest, totals = lax.map(row_per_block, packets)
        highest, totals = merge_rows(*(highest.reshape(src_rows), totals.reshape(src_rows)))
        src_potential = EPSILON * jnp.log(src_mass) - EPSILON * (highest + jnp.log(totals))
        column_potential_tiles = src_potential.reshape(src_blocks, BLOCK)

        def column_per_block(packet):
            scaled = (packet[4][None, :, None] - distances(packet)) / EPSILON
            scaled = jnp.where(packet[3][:, None, None], scaled, SENTINEL)
            highest = jnp.max(scaled, axis=1)
            totals = jnp.sum(
                jnp.where(packet[3][:, None, None], jnp.exp(scaled - highest[:, None, :]), 0.0),
                axis=1,
            )
            return (highest, totals)

        slot_top, slot_sum = lax.map(column_per_block, packets + (column_potential_tiles,))
        slot_top = slot_top.reshape(src_blocks * slot_count, BLOCK)
        slot_sum = slot_sum.reshape(src_blocks * slot_count, BLOCK)
        block_top = jnp.max(jnp.where(member[:, :, None], slot_top[None, :, :], SENTINEL), axis=1)
        scaled_sum = slot_sum * jnp.exp(slot_top - jnp.take(block_top, flat_index, axis=0))
        block_sum = jnp.dot(member.astype(jnp.float32), scaled_sum, precision=lax.Precision.HIGHEST)
        block_top, block_sum = merge_columns(
            *(block_top.reshape(tgt_rows), block_sum.reshape(tgt_rows))
        )
        tgt_potential = EPSILON * jnp.log(tgt_mass) - EPSILON * (block_top + jnp.log(block_sum))
    final_tiles = tgt_potential.reshape(tgt_blocks, BLOCK)

    def local_peak(packet):
        return jnp.max(row_scaled(final_tiles, packet), axis=(0, 2))

    local_top = lax.map(local_peak, packets)

    def weigh(packet):
        scaled = row_scaled(final_tiles, packet)
        weights = jnp.where(
            packet[3][:, None, None], jnp.exp(scaled - packet[4][None, :, None]), 0.0
        )
        rounded_count = lax.optimization_barrier(weights.astype(jnp.bfloat16))
        numerator = jnp.einsum(
            "krc,fkc->rf",
            rounded_count,
            jnp.take(feat_tiles, packet[2], axis=1),
            preferred_element_type=jnp.float32,
        )
        return (numerator, jnp.sum(rounded_count.astype(jnp.float32), axis=(0, 2)))

    numerator, denominator = lax.map(weigh, packets + (local_top,))
    numerator = numerator.reshape(src_rows, target_features.shape[0])
    denominator = denominator.reshape(src_rows)
    local_top = local_top.reshape(src_rows)
    numerator, denominator = halving_merge(local_top, numerator, denominator, "tgt")
    projected = numerator / denominator[:, None]
    return (projected, src_potential, tgt_potential)


def solution(mesh):
    return jax.shard_map(
        shards,
        mesh=mesh,
        in_specs=(
            P(None, "src"),
            P(None, "tgt"),
            P(None, "tgt"),
            P("src"),
            P("tgt"),
            P("src", "tgt"),
            P("src", "tgt"),
        ),
        out_specs=(P(("src", "tgt"), None), P("src"), P("tgt")),
        check_vma=False,
    )
```

```python
import functools

import jax
import jax.numpy as jnp
from jax import lax
from jax.experimental import pallas as pl
from jax.experimental.pallas import tpu as pltpu
from jax.sharding import PartitionSpec as P

BLOCK = 256
ITERS = 2


SENTINEL = -1e30
EPSILON = 0.1
SCALE = 1.0 / EPSILON


def lse_pair(top, total, other_top, other_total):
    overall = jnp.maximum(top, other_top)
    return (overall, total * jnp.exp(top - overall) + other_total * jnp.exp(other_top - overall))


def butterfly_lse(highest, totals, axis):
    size = lax.axis_size(axis)
    step = 1
    while step < size:
        pairs = [(i, i ^ step) for i in range(size)]
        other = lax.ppermute(jnp.stack([highest, totals]), axis, pairs)
        highest, totals = lse_pair(highest, totals, other[0], other[1])
        step *= 2
    return (highest, totals)


def halving_merge(top, numerator, denominator, axis):
    size = lax.axis_size(axis)
    me = lax.axis_index(axis)
    rows = top.shape[0] // size
    top = top.reshape(size, rows)
    denominator = denominator.reshape(size, rows)
    numerator = numerator.reshape(size, rows, numerator.shape[-1])
    step = 1
    while step < size:
        pairs = [(i, i ^ step) for i in range(size)]
        keep = (me // step) % 2
        count = top.shape[0] // 2

        def split(x):
            x = x.reshape((count, 2) + x.shape[1:])
            return (
                lax.dynamic_index_in_dim(x, keep, axis=1, keepdims=False),
                lax.dynamic_index_in_dim(x, 1 - keep, axis=1, keepdims=False),
            )

        top_keep, top_send = split(top)
        den_keep, den_send = split(denominator)
        num_keep, num_send = split(numerator)
        small = lax.ppermute(jnp.stack([top_send, den_send]), axis, pairs)
        num_other = lax.ppermute(num_send, axis, pairs)
        overall = jnp.maximum(top_keep, small[0])
        mine = jnp.exp(top_keep - overall)
        theirs = jnp.exp(small[0] - overall)
        numerator = num_keep * mine[..., None] + num_other * theirs[..., None]
        denominator = den_keep * mine + small[1] * theirs
        top = overall
        step *= 2
    return (numerator.reshape(rows, -1), denominator.reshape(rows))


def tile_cost(src_ref, snorm_ref, tgt_ref, tnorm_ref, b):
    products = jnp.dot(src_ref[...], tgt_ref[b], preferred_element_type=jnp.float32)
    return (snorm_ref[...] + tnorm_ref[b]) - 2.0 * products


def row_kernel(blocks_ref, count_ref, src_ref, snorm_ref, tgt_ref, tnorm_ref, tpot_ref,
               high_ref, total_ref, held, top_acc, sum_acc):
    r = pl.program_id(0)
    slots = held.shape[0]
    live = count_ref[r, 0]

    def scaled_of(k):
        b = blocks_ref[r, k]
        cost = tile_cost(src_ref, snorm_ref, tgt_ref, tnorm_ref, b)
        return (tpot_ref[b] - cost) * SCALE

    first = scaled_of(0)
    held[0] = first
    top_acc[...] = first
    for k in range(1, slots):
        @pl.when(k < live)
        def _():
            scaled = scaled_of(k)
            held[k] = scaled
            top_acc[...] = jnp.maximum(top_acc[...], scaled)

    highest = jnp.max(top_acc[...], axis=1, keepdims=True)
    sum_acc[...] = jnp.exp(held[0] - highest)
    for k in range(1, slots):
        @pl.when(k < live)
        def _():
            sum_acc[...] += jnp.exp(held[k] - highest)

    high_ref[...] = highest
    total_ref[...] = jnp.sum(sum_acc[...], axis=1, keepdims=True)


def column_kernel(blocks_ref, count_ref, src_ref, snorm_ref, spot_ref, tgt_ref, tnorm_ref,
                  top_ref, sum_ref):
    r = pl.program_id(0)
    slots = blocks_ref.shape[1]
    live = count_ref[r, 0]

    @pl.when(r == 0)
    def _():
        top_ref[...] = jnp.full(top_ref.shape, SENTINEL, jnp.float32)
        sum_ref[...] = jnp.zeros(sum_ref.shape, jnp.float32)

    def merge(k):
        b = blocks_ref[r, k]
        cost = tile_cost(src_ref, snorm_ref, tgt_ref, tnorm_ref, b)
        scaled = (spot_ref[...] - cost) * SCALE
        highest = jnp.max(scaled, axis=0, keepdims=True)
        totals = jnp.sum(jnp.exp(scaled - highest), axis=0, keepdims=True)
        old_top = top_ref[b]
        new_top = jnp.maximum(old_top, highest)
        sum_ref[b] = sum_ref[b] * jnp.exp(old_top - new_top) + totals * jnp.exp(highest - new_top)
        top_ref[b] = new_top

    merge(0)
    for k in range(1, slots):
        @pl.when(k < live)
        def _():
            merge(k)


def project_kernel(blocks_ref, count_ref, src_ref, snorm_ref, tgt_ref, tnorm_ref, tpot_ref,
                   feat_ref, top_ref, num_ref, den_ref, held, top_acc, den_acc):
    r = pl.program_id(0)
    slots = held.shape[0]
    live = count_ref[r, 0]

    def scaled_of(k):
        b = blocks_ref[r, k]
        cost = tile_cost(src_ref, snorm_ref, tgt_ref, tnorm_ref, b)
        return (tpot_ref[b] - cost) * SCALE

    first = scaled_of(0)
    held[0] = first
    top_acc[...] = first
    for k in range(1, slots):
        @pl.when(k < live)
        def _():
            scaled = scaled_of(k)
            held[k] = scaled
            top_acc[...] = jnp.maximum(top_acc[...], scaled)

    highest = jnp.max(top_acc[...], axis=1, keepdims=True)

    def weigh(k):
        b = blocks_ref[r, k]
        weights = jnp.exp(held[k] - highest).astype(jnp.bfloat16)
        part = lax.dot_general(weights, feat_ref[b], (((1,), (1,)), ((), ())),
                               preferred_element_type=jnp.float32)
        return part, weights.astype(jnp.float32)

    part, weights = weigh(0)
    num_ref[...] = part
    den_acc[...] = weights
    for k in range(1, slots):
        @pl.when(k < live)
        def _():
            part, weights = weigh(k)
            num_ref[...] += part
            den_acc[...] += weights

    top_ref[...] = highest
    den_ref[...] = jnp.sum(den_acc[...], axis=1, keepdims=True)


def whole(shape):
    return pl.BlockSpec(shape, lambda r, *_: (0,) * len(shape))


def per_row(width):
    return pl.BlockSpec((BLOCK, width), lambda r, *_: (r, 0))


def row_pass(blocks, counts, src_t, snorm, tgt_t, tnorm, tpot):
    rows = src_t.shape[0]
    slots = blocks.shape[1]
    spec = pltpu.PrefetchScalarGridSpec(
        num_scalar_prefetch=2,
        grid=(rows // BLOCK,),
        in_specs=[per_row(src_t.shape[1]), per_row(1), whole(tgt_t.shape), whole(tnorm.shape),
                  whole(tpot.shape)],
        out_specs=[per_row(1), per_row(1)],
        scratch_shapes=[pltpu.VMEM((slots, BLOCK, BLOCK), jnp.float32),
                        pltpu.VMEM((BLOCK, BLOCK), jnp.float32),
                        pltpu.VMEM((BLOCK, BLOCK), jnp.float32)],
    )
    return pl.pallas_call(
        row_kernel,
        grid_spec=spec,
        out_shape=[jax.ShapeDtypeStruct((rows, 1), jnp.float32)] * 2,
        compiler_params=pltpu.CompilerParams(dimension_semantics=("arbitrary",)),
    )(blocks, counts, src_t, snorm, tgt_t, tnorm, tpot)


def column_pass(blocks, counts, src_t, snorm, spot, tgt_t, tnorm):
    rows = src_t.shape[0]
    spec = pltpu.PrefetchScalarGridSpec(
        num_scalar_prefetch=2,
        grid=(rows // BLOCK,),
        in_specs=[per_row(src_t.shape[1]), per_row(1), per_row(1), whole(tgt_t.shape),
                  whole(tnorm.shape)],
        out_specs=[whole(tnorm.shape), whole(tnorm.shape)],
    )
    return pl.pallas_call(
        column_kernel,
        grid_spec=spec,
        out_shape=[jax.ShapeDtypeStruct(tnorm.shape, jnp.float32)] * 2,
        compiler_params=pltpu.CompilerParams(dimension_semantics=("arbitrary",)),
    )(blocks, counts, src_t, snorm, spot, tgt_t, tnorm)


def project_pass(blocks, counts, src_t, snorm, tgt_t, tnorm, tpot, feat_t):
    rows = src_t.shape[0]
    slots = blocks.shape[1]
    feats = feat_t.shape[1]
    spec = pltpu.PrefetchScalarGridSpec(
        num_scalar_prefetch=2,
        grid=(rows // BLOCK,),
        in_specs=[per_row(src_t.shape[1]), per_row(1), whole(tgt_t.shape), whole(tnorm.shape),
                  whole(tpot.shape), whole(feat_t.shape)],
        out_specs=[per_row(1), per_row(feats), per_row(1)],
        scratch_shapes=[pltpu.VMEM((slots, BLOCK, BLOCK), jnp.float32),
                        pltpu.VMEM((BLOCK, BLOCK), jnp.float32),
                        pltpu.VMEM((BLOCK, BLOCK), jnp.float32)],
    )
    return pl.pallas_call(
        project_kernel,
        grid_spec=spec,
        out_shape=[jax.ShapeDtypeStruct((rows, 1), jnp.float32),
                   jax.ShapeDtypeStruct((rows, feats), jnp.float32),
                   jax.ShapeDtypeStruct((rows, 1), jnp.float32)],
        compiler_params=pltpu.CompilerParams(dimension_semantics=("arbitrary",)),
    )(blocks, counts, src_t, snorm, tgt_t, tnorm, tpot, feat_t)


def shards(src_emb, tgt_emb, target_features, src_mass, tgt_mass, kept_blocks, kept_count):
    emb_width = src_emb.shape[0]
    src_rows = src_emb.shape[1]
    tgt_rows = tgt_emb.shape[1]
    tgt_blocks = tgt_rows // BLOCK
    feats = target_features.shape[0]
    src_t = src_emb.T
    snorm = jnp.sum(jnp.square(src_emb.astype(jnp.float32)), axis=0).reshape(src_rows, 1)
    tgt_t = tgt_emb.reshape(emb_width, tgt_blocks, BLOCK).transpose(1, 0, 2)
    tnorm = jnp.sum(jnp.square(tgt_emb.astype(jnp.float32)), axis=0).reshape(tgt_blocks, 1, BLOCK)
    feat_t = target_features.reshape(feats, tgt_blocks, BLOCK).transpose(1, 0, 2)
    counts = kept_count.reshape(-1, 1)

    tgt_potential = jnp.zeros((tgt_rows,), jnp.float32)
    src_potential = jnp.zeros((src_rows,), jnp.float32)
    for iteration in range(ITERS):
        tpot = tgt_potential.reshape(tgt_blocks, 1, BLOCK)
        highest, totals = row_pass(kept_blocks, counts, src_t, snorm, tgt_t, tnorm, tpot)
        highest, totals = butterfly_lse(highest.reshape(src_rows), totals.reshape(src_rows), "tgt")
        src_potential = EPSILON * jnp.log(src_mass) - EPSILON * (highest + jnp.log(totals))
        block_top, block_sum = column_pass(
            kept_blocks, counts, src_t, snorm, src_potential.reshape(src_rows, 1), tgt_t, tnorm
        )
        block_top, block_sum = butterfly_lse(
            block_top.reshape(tgt_rows), block_sum.reshape(tgt_rows), "src"
        )
        tgt_potential = EPSILON * jnp.log(tgt_mass) - EPSILON * (block_top + jnp.log(block_sum))

    tpot = tgt_potential.reshape(tgt_blocks, 1, BLOCK)
    local_top, numerator, denominator = project_pass(
        kept_blocks, counts, src_t, snorm, tgt_t, tnorm, tpot, feat_t
    )
    numerator, denominator = halving_merge(
        local_top.reshape(src_rows), numerator, denominator.reshape(src_rows), "tgt"
    )
    projected = numerator / denominator[:, None]
    return (projected, src_potential, tgt_potential)


def solution(mesh):
    return jax.shard_map(
        shards,
        mesh=mesh,
        in_specs=(
            P(None, "src"),
            P(None, "tgt"),
            P(None, "tgt"),
            P("src"),
            P("tgt"),
            P("src", "tgt"),
            P("src", "tgt"),
        ),
        out_specs=(P(("src", "tgt"), None), P("src"), P("tgt")),
        check_vma=False,
    )
```

```python
import functools

import jax
import jax.numpy as jnp
from jax import lax
from jax.experimental import pallas as pl
from jax.experimental.pallas import tpu as pltpu
from jax.sharding import PartitionSpec as P

BLOCK = 256
ITERS = 2


SENTINEL = -1e30
EPSILON = 0.1
SCALE = 1.0 / EPSILON


def lse_pair(top, total, other_top, other_total):
    overall = jnp.maximum(top, other_top)
    return (overall, total * jnp.exp(top - overall) + other_total * jnp.exp(other_top - overall))


def butterfly_lse(highest, totals, axis):
    size = lax.axis_size(axis)
    step = 1
    while step < size:
        pairs = [(i, i ^ step) for i in range(size)]
        other = lax.ppermute(jnp.stack([highest, totals]), axis, pairs)
        highest, totals = lse_pair(highest, totals, other[0], other[1])
        step *= 2
    return (highest, totals)


def halving_merge(top, numerator, denominator, axis):
    size = lax.axis_size(axis)
    me = lax.axis_index(axis)
    rows = top.shape[0] // size
    top = top.reshape(size, rows)
    denominator = denominator.reshape(size, rows)
    numerator = numerator.reshape(size, rows, numerator.shape[-1])
    step = 1
    while step < size:
        pairs = [(i, i ^ step) for i in range(size)]
        keep = (me // step) % 2
        count = top.shape[0] // 2

        def split(x):
            x = x.reshape((count, 2) + x.shape[1:])
            return (
                lax.dynamic_index_in_dim(x, keep, axis=1, keepdims=False),
                lax.dynamic_index_in_dim(x, 1 - keep, axis=1, keepdims=False),
            )

        top_keep, top_send = split(top)
        den_keep, den_send = split(denominator)
        num_keep, num_send = split(numerator)
        small = lax.ppermute(jnp.stack([top_send, den_send]), axis, pairs)
        num_other = lax.ppermute(num_send, axis, pairs)
        overall = jnp.maximum(top_keep, small[0])
        mine = jnp.exp(top_keep - overall)
        theirs = jnp.exp(small[0] - overall)
        numerator = num_keep * mine[..., None] + num_other * theirs[..., None]
        denominator = den_keep * mine + small[1] * theirs
        top = overall
        step *= 2
    return (numerator.reshape(rows, -1), denominator.reshape(rows))


CHUNK = 64


def tile_slice(ref, b):
    return ref[:, pl.ds(pl.multiple_of(b * BLOCK, BLOCK), BLOCK)]


def doubled_source(src_ref):
    exact = src_ref[...].astype(jnp.float32)
    return (exact * 2.0).astype(jnp.bfloat16), jnp.sum(exact * exact, axis=1, keepdims=True)


def as_row(column, scratch):
    scratch[...] = jnp.broadcast_to(column, scratch.shape)
    return jnp.transpose(scratch[...])[0:1, :]


def as_column(row, scratch):
    scratch[...] = jnp.broadcast_to(row, scratch.shape)
    return jnp.transpose(scratch[...])[:, 0:1]


def fill_shifted(blocks_ref, r, live, doubled, tgt_ref, tnorm_ref, tpot_ref, held):
    def fill(k):
        b = blocks_ref[r, k]
        shift = tile_slice(tpot_ref, b) - tile_slice(tnorm_ref, b)
        held[k] = jnp.dot(doubled, tile_slice(tgt_ref, b), preferred_element_type=jnp.float32) + shift

    fill(0)
    lax.fori_loop(1, live, lambda k, c: (fill(k), c)[1], 0)


def chunk_peak(held, live, rows):
    peak = lax.fori_loop(1, live, lambda k, m: jnp.maximum(m, held[k, rows, :]), held[0, rows, :])
    return jnp.max(peak, axis=1, keepdims=True)


def row_kernel(blocks_ref, count_ref, src_ref, tgt_ref, tnorm_ref, tpot_ref,
               high_ref, total_ref, held, high_col, total_col, wide):
    r = pl.program_id(0)
    live = count_ref[r, 0]
    doubled, snorm = doubled_source(src_ref)
    fill_shifted(blocks_ref, r, live, doubled, tgt_ref, tnorm_ref, tpot_ref, held)
    for chunk in range(BLOCK // CHUNK):
        rows = pl.ds(chunk * CHUNK, CHUNK)
        peak = chunk_peak(held, live, rows)

        def add(k, acc):
            return acc + jnp.exp((held[k, rows, :] - peak) * SCALE)

        acc = lax.fori_loop(1, live, add, jnp.exp((held[0, rows, :] - peak) * SCALE))
        high_col[rows, :] = peak
        total_col[rows, :] = jnp.sum(acc, axis=1, keepdims=True)
    high_ref[...] = as_row((high_col[...] - snorm) * SCALE, wide)
    total_ref[...] = as_row(total_col[...], wide)


def column_kernel(blocks_ref, count_ref, src_ref, spot_ref, tgt_ref, tnorm_ref,
                  top_ref, sum_ref, tall):
    r = pl.program_id(0)
    live = count_ref[r, 0]

    @pl.when(r == 0)
    def _():
        top_ref[...] = jnp.full(top_ref.shape, SENTINEL, jnp.float32)
        sum_ref[...] = jnp.zeros(sum_ref.shape, jnp.float32)

    doubled, snorm = doubled_source(src_ref)
    shift = as_column(spot_ref[...], tall) - snorm

    def merge(k, c):
        b = blocks_ref[r, k]
        lanes = pl.ds(pl.multiple_of(b * BLOCK, BLOCK), BLOCK)
        shifted = jnp.dot(doubled, tile_slice(tgt_ref, b), preferred_element_type=jnp.float32) + shift
        peak = jnp.max(shifted, axis=0, keepdims=True)
        totals = jnp.sum(jnp.exp((shifted - peak) * SCALE), axis=0, keepdims=True)
        highest = (peak - tnorm_ref[:, lanes]) * SCALE
        old_top = top_ref[:, lanes]
        new_top = jnp.maximum(old_top, highest)
        sum_ref[:, lanes] = (sum_ref[:, lanes] * jnp.exp(old_top - new_top)
                             + totals * jnp.exp(highest - new_top))
        top_ref[:, lanes] = new_top
        return c

    lax.fori_loop(0, live, merge, 0)


def project_kernel(blocks_ref, count_ref, src_ref, tgt_ref, tnorm_ref, tpot_ref, feat_ref,
                   top_ref, num_ref, den_ref, held, weights, high_col, den_col, wide):
    r = pl.program_id(0)
    live = count_ref[r, 0]
    doubled, snorm = doubled_source(src_ref)
    fill_shifted(blocks_ref, r, live, doubled, tgt_ref, tnorm_ref, tpot_ref, held)
    for chunk in range(BLOCK // CHUNK):
        rows = pl.ds(chunk * CHUNK, CHUNK)
        peak = chunk_peak(held, live, rows)

        def weigh(k, acc):
            rounded = jnp.exp((held[k, rows, :] - peak) * SCALE).astype(jnp.bfloat16)
            weights[k, rows, :] = rounded
            return acc + rounded.astype(jnp.float32)

        acc = lax.fori_loop(0, live, weigh, jnp.zeros((CHUNK, BLOCK), jnp.float32))
        high_col[rows, :] = peak
        den_col[rows, :] = jnp.sum(acc, axis=1, keepdims=True)

    def part(k):
        return lax.dot_general(weights[k], tile_slice(feat_ref, blocks_ref[r, k]),
                               (((1,), (1,)), ((), ())), preferred_element_type=jnp.float32)

    num_ref[...] = part(0)

    def add(k, c):
        num_ref[...] += part(k)
        return c

    lax.fori_loop(1, live, add, 0)
    top_ref[...] = as_row((high_col[...] - snorm) * SCALE, wide)
    den_ref[...] = as_row(den_col[...], wide)


def whole(shape):
    return pl.BlockSpec(shape, lambda r, *_: (0,) * len(shape))


def per_row(width):
    return pl.BlockSpec((BLOCK, width), lambda r, *_: (r, 0))


def lane_row():
    return pl.BlockSpec((1, BLOCK), lambda r, *_: (0, r))


def column_scratch():
    return pltpu.VMEM((BLOCK, 1), jnp.float32)


def row_pass(blocks, counts, src_t, tgt, tnorm, tpot):
    rows = src_t.shape[0]
    slots = blocks.shape[1]
    spec = pltpu.PrefetchScalarGridSpec(
        num_scalar_prefetch=2,
        grid=(rows // BLOCK,),
        in_specs=[per_row(src_t.shape[1]), whole(tgt.shape), whole(tnorm.shape), whole(tpot.shape)],
        out_specs=[lane_row(), lane_row()],
        scratch_shapes=[pltpu.VMEM((slots, BLOCK, BLOCK), jnp.float32), column_scratch(),
                        column_scratch(), pltpu.VMEM((BLOCK, 128), jnp.float32)],
    )
    return pl.pallas_call(
        row_kernel,
        grid_spec=spec,
        out_shape=[jax.ShapeDtypeStruct((1, rows), jnp.float32)] * 2,
        compiler_params=pltpu.CompilerParams(dimension_semantics=("arbitrary",)),
    )(blocks, counts, src_t, tgt, tnorm, tpot)


def column_pass(blocks, counts, src_t, spot, tgt, tnorm):
    rows = src_t.shape[0]
    spec = pltpu.PrefetchScalarGridSpec(
        num_scalar_prefetch=2,
        grid=(rows // BLOCK,),
        in_specs=[per_row(src_t.shape[1]), lane_row(), whole(tgt.shape), whole(tnorm.shape)],
        out_specs=[whole(tnorm.shape), whole(tnorm.shape)],
        scratch_shapes=[pltpu.VMEM((128, BLOCK), jnp.float32)],
    )
    return pl.pallas_call(
        column_kernel,
        grid_spec=spec,
        out_shape=[jax.ShapeDtypeStruct(tnorm.shape, jnp.float32)] * 2,
        compiler_params=pltpu.CompilerParams(dimension_semantics=("arbitrary",)),
    )(blocks, counts, src_t, spot, tgt, tnorm)


def project_pass(blocks, counts, src_t, tgt, tnorm, tpot, feat):
    rows = src_t.shape[0]
    slots = blocks.shape[1]
    feats = feat.shape[0]
    spec = pltpu.PrefetchScalarGridSpec(
        num_scalar_prefetch=2,
        grid=(rows // BLOCK,),
        in_specs=[per_row(src_t.shape[1]), whole(tgt.shape), whole(tnorm.shape),
                  whole(tpot.shape), whole(feat.shape)],
        out_specs=[lane_row(), per_row(feats), lane_row()],
        scratch_shapes=[pltpu.VMEM((slots, BLOCK, BLOCK), jnp.float32),
                        pltpu.VMEM((slots, BLOCK, BLOCK), jnp.bfloat16),
                        column_scratch(), column_scratch(), pltpu.VMEM((BLOCK, 128), jnp.float32)],
    )
    return pl.pallas_call(
        project_kernel,
        grid_spec=spec,
        out_shape=[jax.ShapeDtypeStruct((1, rows), jnp.float32),
                   jax.ShapeDtypeStruct((rows, feats), jnp.float32),
                   jax.ShapeDtypeStruct((1, rows), jnp.float32)],
        compiler_params=pltpu.CompilerParams(dimension_semantics=("arbitrary",)),
    )(blocks, counts, src_t, tgt, tnorm, tpot, feat)


def shards(src_emb, tgt_emb, target_features, src_mass, tgt_mass, kept_blocks, kept_count):
    src_rows = src_emb.shape[1]
    tgt_rows = tgt_emb.shape[1]
    src_t = src_emb.T
    tnorm = jnp.sum(jnp.square(tgt_emb.astype(jnp.float32)), axis=0).reshape(1, tgt_rows)
    counts = kept_count.reshape(-1, 1)

    tgt_potential = jnp.zeros((tgt_rows,), jnp.float32)
    src_potential = jnp.zeros((src_rows,), jnp.float32)
    for iteration in range(ITERS):
        tpot = tgt_potential.reshape(1, tgt_rows)
        highest, totals = row_pass(kept_blocks, counts, src_t, tgt_emb, tnorm, tpot)
        highest, totals = butterfly_lse(highest.reshape(src_rows), totals.reshape(src_rows), "tgt")
        src_potential = EPSILON * jnp.log(src_mass) - EPSILON * (highest + jnp.log(totals))
        block_top, block_sum = column_pass(
            kept_blocks, counts, src_t, src_potential.reshape(1, src_rows), tgt_emb, tnorm
        )
        block_top, block_sum = butterfly_lse(
            block_top.reshape(tgt_rows), block_sum.reshape(tgt_rows), "src"
        )
        tgt_potential = EPSILON * jnp.log(tgt_mass) - EPSILON * (block_top + jnp.log(block_sum))

    tpot = tgt_potential.reshape(1, tgt_rows)
    local_top, numerator, denominator = project_pass(
        kept_blocks, counts, src_t, tgt_emb, tnorm, tpot, target_features
    )
    numerator, denominator = halving_merge(
        local_top.reshape(src_rows), numerator, denominator.reshape(src_rows), "tgt"
    )
    projected = numerator / denominator[:, None]
    return (projected, src_potential, tgt_potential)


def solution(mesh):
    return jax.shard_map(
        shards,
        mesh=mesh,
        in_specs=(
            P(None, "src"),
            P(None, "tgt"),
            P(None, "tgt"),
            P("src"),
            P("tgt"),
            P("src", "tgt"),
            P("src", "tgt"),
        ),
        out_specs=(P(("src", "tgt"), None), P("src"), P("tgt")),
        check_vma=False,
    )
```

```python
import functools

import jax
import jax.numpy as jnp
from jax import lax
from jax.experimental import pallas as pl
from jax.experimental.pallas import tpu as pltpu
from jax.sharding import PartitionSpec as P

BLOCK = 256
ITERS = 2


SENTINEL = -1e30
EPSILON = 0.1
SCALE = 1.0 / EPSILON


def lse_pair(top, total, other_top, other_total):
    overall = jnp.maximum(top, other_top)
    return (overall, total * jnp.exp(top - overall) + other_total * jnp.exp(other_top - overall))


def butterfly_lse(highest, totals, axis):
    size = lax.axis_size(axis)
    step = 1
    while step < size:
        pairs = [(i, i ^ step) for i in range(size)]
        other = lax.ppermute(jnp.stack([highest, totals]), axis, pairs)
        highest, totals = lse_pair(highest, totals, other[0], other[1])
        step *= 2
    return (highest, totals)


def halving_merge(top, numerator, denominator, axis):
    size = lax.axis_size(axis)
    me = lax.axis_index(axis)
    rows = top.shape[0] // size
    top = top.reshape(size, rows)
    denominator = denominator.reshape(size, rows)
    numerator = numerator.reshape(size, rows, numerator.shape[-1])
    step = 1
    while step < size:
        pairs = [(i, i ^ step) for i in range(size)]
        keep = (me // step) % 2
        count = top.shape[0] // 2

        def split(x):
            x = x.reshape((count, 2) + x.shape[1:])
            return (
                lax.dynamic_index_in_dim(x, keep, axis=1, keepdims=False),
                lax.dynamic_index_in_dim(x, 1 - keep, axis=1, keepdims=False),
            )

        top_keep, top_send = split(top)
        den_keep, den_send = split(denominator)
        num_keep, num_send = split(numerator)
        small = lax.ppermute(jnp.stack([top_send, den_send]), axis, pairs)
        num_other = lax.ppermute(num_send, axis, pairs)
        overall = jnp.maximum(top_keep, small[0])
        mine = jnp.exp(top_keep - overall)
        theirs = jnp.exp(small[0] - overall)
        numerator = num_keep * mine[..., None] + num_other * theirs[..., None]
        denominator = den_keep * mine + small[1] * theirs
        top = overall
        step *= 2
    return (numerator.reshape(rows, -1), denominator.reshape(rows))


CHUNK = 64


def tile_slice(ref, b):
    return ref[:, pl.ds(pl.multiple_of(b * BLOCK, BLOCK), BLOCK)]


def doubled_source(src_ref):
    exact = src_ref[...].astype(jnp.float32)
    return (exact * 2.0).astype(jnp.bfloat16), jnp.sum(exact * exact, axis=1, keepdims=True)


def as_row(column, scratch):
    scratch[...] = jnp.broadcast_to(column, scratch.shape)
    return jnp.transpose(scratch[...])[0:1, :]


def as_column(row, scratch):
    scratch[...] = jnp.broadcast_to(row, scratch.shape)
    return jnp.transpose(scratch[...])[:, 0:1]


def by_count(live, slots, body):
    for count in range(1, slots + 1):
        pl.when(live == count)(functools.partial(body, count))


def fill_shifted(blocks_ref, r, count, doubled, tgt_ref, tnorm_ref, tpot_ref, held):
    for k in range(count):
        b = blocks_ref[r, k]
        shift = tile_slice(tpot_ref, b) - tile_slice(tnorm_ref, b)
        held[k] = jnp.dot(doubled, tile_slice(tgt_ref, b), preferred_element_type=jnp.float32) + shift


def chunk_peak(held, count, rows):
    peak = held[0, rows, :]
    for k in range(1, count):
        peak = jnp.maximum(peak, held[k, rows, :])
    return jnp.max(peak, axis=1, keepdims=True)


def row_kernel(blocks_ref, count_ref, src_ref, tgt_ref, tnorm_ref, tpot_ref,
               high_ref, total_ref, held, high_col, total_col, wide):
    r = pl.program_id(0)
    doubled, snorm = doubled_source(src_ref)

    def body(count):
        fill_shifted(blocks_ref, r, count, doubled, tgt_ref, tnorm_ref, tpot_ref, held)
        for chunk in range(BLOCK // CHUNK):
            rows = pl.ds(chunk * CHUNK, CHUNK)
            peak = chunk_peak(held, count, rows)
            acc = jnp.exp((held[0, rows, :] - peak) * SCALE)
            for k in range(1, count):
                acc = acc + jnp.exp((held[k, rows, :] - peak) * SCALE)
            high_col[rows, :] = peak
            total_col[rows, :] = jnp.sum(acc, axis=1, keepdims=True)

    by_count(count_ref[r, 0], held.shape[0], body)
    high_ref[...] = as_row((high_col[...] - snorm) * SCALE, wide)
    total_ref[...] = as_row(total_col[...], wide)


def column_kernel(blocks_ref, count_ref, src_ref, spot_ref, tgt_ref, tnorm_ref,
                  top_ref, sum_ref, tall):
    r = pl.program_id(0)

    @pl.when(r == 0)
    def _():
        top_ref[...] = jnp.full(top_ref.shape, SENTINEL, jnp.float32)
        sum_ref[...] = jnp.zeros(sum_ref.shape, jnp.float32)

    doubled, snorm = doubled_source(src_ref)
    shift = as_column(spot_ref[...], tall) - snorm

    def body(count):
        for k in range(count):
            b = blocks_ref[r, k]
            lanes = pl.ds(pl.multiple_of(b * BLOCK, BLOCK), BLOCK)
            shifted = jnp.dot(doubled, tile_slice(tgt_ref, b),
                              preferred_element_type=jnp.float32) + shift
            peak = jnp.max(shifted, axis=0, keepdims=True)
            totals = jnp.sum(jnp.exp((shifted - peak) * SCALE), axis=0, keepdims=True)
            highest = (peak - tnorm_ref[:, lanes]) * SCALE
            old_top = top_ref[:, lanes]
            new_top = jnp.maximum(old_top, highest)
            sum_ref[:, lanes] = (sum_ref[:, lanes] * jnp.exp(old_top - new_top)
                                 + totals * jnp.exp(highest - new_top))
            top_ref[:, lanes] = new_top

    by_count(count_ref[r, 0], blocks_ref.shape[1], body)


def project_kernel(blocks_ref, count_ref, src_ref, tgt_ref, tnorm_ref, tpot_ref, feat_ref,
                   top_ref, num_ref, den_ref, held, weights, high_col, den_col, wide):
    r = pl.program_id(0)
    doubled, snorm = doubled_source(src_ref)

    def body(count):
        fill_shifted(blocks_ref, r, count, doubled, tgt_ref, tnorm_ref, tpot_ref, held)
        for chunk in range(BLOCK // CHUNK):
            rows = pl.ds(chunk * CHUNK, CHUNK)
            peak = chunk_peak(held, count, rows)
            acc = jnp.zeros((CHUNK, BLOCK), jnp.float32)
            for k in range(count):
                rounded = jnp.exp((held[k, rows, :] - peak) * SCALE).astype(jnp.bfloat16)
                weights[k, rows, :] = rounded
                acc = acc + rounded.astype(jnp.float32)
            high_col[rows, :] = peak
            den_col[rows, :] = jnp.sum(acc, axis=1, keepdims=True)
        total = None
        for k in range(count):
            part = lax.dot_general(weights[k], tile_slice(feat_ref, blocks_ref[r, k]),
                                   (((1,), (1,)), ((), ())), preferred_element_type=jnp.float32)
            total = part if total is None else total + part
        num_ref[...] = total

    by_count(count_ref[r, 0], held.shape[0], body)
    top_ref[...] = as_row((high_col[...] - snorm) * SCALE, wide)
    den_ref[...] = as_row(den_col[...], wide)


def whole(shape):
    return pl.BlockSpec(shape, lambda r, *_: (0,) * len(shape))


def per_row(width):
    return pl.BlockSpec((BLOCK, width), lambda r, *_: (r, 0))


def lane_row():
    return pl.BlockSpec((1, BLOCK), lambda r, *_: (0, r))


def column_scratch():
    return pltpu.VMEM((BLOCK, 1), jnp.float32)


def row_pass(blocks, counts, src_t, tgt, tnorm, tpot):
    rows = src_t.shape[0]
    slots = blocks.shape[1]
    spec = pltpu.PrefetchScalarGridSpec(
        num_scalar_prefetch=2,
        grid=(rows // BLOCK,),
        in_specs=[per_row(src_t.shape[1]), whole(tgt.shape), whole(tnorm.shape), whole(tpot.shape)],
        out_specs=[lane_row(), lane_row()],
        scratch_shapes=[pltpu.VMEM((slots, BLOCK, BLOCK), jnp.float32), column_scratch(),
                        column_scratch(), pltpu.VMEM((BLOCK, 128), jnp.float32)],
    )
    return pl.pallas_call(
        row_kernel,
        grid_spec=spec,
        out_shape=[jax.ShapeDtypeStruct((1, rows), jnp.float32)] * 2,
        compiler_params=pltpu.CompilerParams(dimension_semantics=("arbitrary",)),
    )(blocks, counts, src_t, tgt, tnorm, tpot)


def column_pass(blocks, counts, src_t, spot, tgt, tnorm):
    rows = src_t.shape[0]
    spec = pltpu.PrefetchScalarGridSpec(
        num_scalar_prefetch=2,
        grid=(rows // BLOCK,),
        in_specs=[per_row(src_t.shape[1]), lane_row(), whole(tgt.shape), whole(tnorm.shape)],
        out_specs=[whole(tnorm.shape), whole(tnorm.shape)],
        scratch_shapes=[pltpu.VMEM((128, BLOCK), jnp.float32)],
    )
    return pl.pallas_call(
        column_kernel,
        grid_spec=spec,
        out_shape=[jax.ShapeDtypeStruct(tnorm.shape, jnp.float32)] * 2,
        compiler_params=pltpu.CompilerParams(dimension_semantics=("arbitrary",)),
    )(blocks, counts, src_t, spot, tgt, tnorm)


def project_pass(blocks, counts, src_t, tgt, tnorm, tpot, feat):
    rows = src_t.shape[0]
    slots = blocks.shape[1]
    feats = feat.shape[0]
    spec = pltpu.PrefetchScalarGridSpec(
        num_scalar_prefetch=2,
        grid=(rows // BLOCK,),
        in_specs=[per_row(src_t.shape[1]), whole(tgt.shape), whole(tnorm.shape),
                  whole(tpot.shape), whole(feat.shape)],
        out_specs=[lane_row(), per_row(feats), lane_row()],
        scratch_shapes=[pltpu.VMEM((slots, BLOCK, BLOCK), jnp.float32),
                        pltpu.VMEM((slots, BLOCK, BLOCK), jnp.bfloat16),
                        column_scratch(), column_scratch(), pltpu.VMEM((BLOCK, 128), jnp.float32)],
    )
    return pl.pallas_call(
        project_kernel,
        grid_spec=spec,
        out_shape=[jax.ShapeDtypeStruct((1, rows), jnp.float32),
                   jax.ShapeDtypeStruct((rows, feats), jnp.float32),
                   jax.ShapeDtypeStruct((1, rows), jnp.float32)],
        compiler_params=pltpu.CompilerParams(dimension_semantics=("arbitrary",)),
    )(blocks, counts, src_t, tgt, tnorm, tpot, feat)


def shards(src_emb, tgt_emb, target_features, src_mass, tgt_mass, kept_blocks, kept_count):
    src_rows = src_emb.shape[1]
    tgt_rows = tgt_emb.shape[1]
    src_t = src_emb.T
    tnorm = jnp.sum(jnp.square(tgt_emb.astype(jnp.float32)), axis=0).reshape(1, tgt_rows)
    counts = kept_count.reshape(-1, 1)

    tgt_potential = jnp.zeros((tgt_rows,), jnp.float32)
    src_potential = jnp.zeros((src_rows,), jnp.float32)
    for iteration in range(ITERS):
        tpot = tgt_potential.reshape(1, tgt_rows)
        highest, totals = row_pass(kept_blocks, counts, src_t, tgt_emb, tnorm, tpot)
        highest, totals = butterfly_lse(highest.reshape(src_rows), totals.reshape(src_rows), "tgt")
        src_potential = EPSILON * jnp.log(src_mass) - EPSILON * (highest + jnp.log(totals))
        block_top, block_sum = column_pass(
            kept_blocks, counts, src_t, src_potential.reshape(1, src_rows), tgt_emb, tnorm
        )
        block_top, block_sum = butterfly_lse(
            block_top.reshape(tgt_rows), block_sum.reshape(tgt_rows), "src"
        )
        tgt_potential = EPSILON * jnp.log(tgt_mass) - EPSILON * (block_top + jnp.log(block_sum))

    tpot = tgt_potential.reshape(1, tgt_rows)
    local_top, numerator, denominator = project_pass(
        kept_blocks, counts, src_t, tgt_emb, tnorm, tpot, target_features
    )
    numerator, denominator = halving_merge(
        local_top.reshape(src_rows), numerator, denominator.reshape(src_rows), "tgt"
    )
    projected = numerator / denominator[:, None]
    return (projected, src_potential, tgt_potential)


def solution(mesh):
    return jax.shard_map(
        shards,
        mesh=mesh,
        in_specs=(
            P(None, "src"),
            P(None, "tgt"),
            P(None, "tgt"),
            P("src"),
            P("tgt"),
            P("src", "tgt"),
            P("src", "tgt"),
        ),
        out_specs=(P(("src", "tgt"), None), P("src"), P("tgt")),
        check_vma=False,
    )
```

```python
import functools

import jax
import jax.numpy as jnp
from jax import lax
from jax.experimental import pallas as pl
from jax.experimental.pallas import tpu as pltpu
from jax.sharding import PartitionSpec as P

BLOCK = 256
ITERS = 2


SENTINEL = -1e30
EPSILON = 0.1
SCALE = 1.0 / EPSILON


def lse_pair(top, total, other_top, other_total):
    overall = jnp.maximum(top, other_top)
    return (overall, total * jnp.exp(top - overall) + other_total * jnp.exp(other_top - overall))


def butterfly_lse(highest, totals, axis):
    size = lax.axis_size(axis)
    step = 1
    while step < size:
        pairs = [(i, i ^ step) for i in range(size)]
        other = lax.ppermute(jnp.stack([highest, totals]), axis, pairs)
        highest, totals = lse_pair(highest, totals, other[0], other[1])
        step *= 2
    return (highest, totals)


def halving_merge(top, numerator, denominator, axis):
    size = lax.axis_size(axis)
    me = lax.axis_index(axis)
    rows = top.shape[0] // size
    top = top.reshape(size, rows)
    denominator = denominator.reshape(size, rows)
    numerator = numerator.reshape(size, rows, numerator.shape[-1])
    step = 1
    while step < size:
        pairs = [(i, i ^ step) for i in range(size)]
        keep = (me // step) % 2
        count = top.shape[0] // 2

        def split(x):
            x = x.reshape((count, 2) + x.shape[1:])
            return (
                lax.dynamic_index_in_dim(x, keep, axis=1, keepdims=False),
                lax.dynamic_index_in_dim(x, 1 - keep, axis=1, keepdims=False),
            )

        top_keep, top_send = split(top)
        den_keep, den_send = split(denominator)
        num_keep, num_send = split(numerator)
        small = lax.ppermute(jnp.stack([top_send, den_send]), axis, pairs)
        num_other = lax.ppermute(num_send, axis, pairs)
        overall = jnp.maximum(top_keep, small[0])
        mine = jnp.exp(top_keep - overall)
        theirs = jnp.exp(small[0] - overall)
        numerator = num_keep * mine[..., None] + num_other * theirs[..., None]
        denominator = den_keep * mine + small[1] * theirs
        top = overall
        step *= 2
    return (numerator.reshape(rows, -1), denominator.reshape(rows))


CHUNK = 64


def tile_slice(ref, b):
    return ref[:, pl.ds(pl.multiple_of(b * BLOCK, BLOCK), BLOCK)]


def row_slice(ref, r):
    return ref[pl.ds(pl.multiple_of(r * BLOCK, BLOCK), BLOCK), :]


def doubled_source(src_ref, r):
    exact = tile_slice(src_ref, r).astype(jnp.float32)
    return (exact * 2.0).astype(jnp.bfloat16), jnp.sum(exact * exact, axis=0, keepdims=True)


def products(doubled, tgt_ref, b):
    return lax.dot_general(doubled, tile_slice(tgt_ref, b), (((0,), (0,)), ((), ())),
                           preferred_element_type=jnp.float32)


def as_row(column, scratch):
    scratch[...] = jnp.broadcast_to(column, scratch.shape)
    return jnp.transpose(scratch[...])[0:1, :]


def as_column(row, scratch):
    scratch[...] = jnp.broadcast_to(row, scratch.shape)
    return jnp.transpose(scratch[...])[:, 0:1]


def by_count(live, slots, body):
    for count in range(1, slots + 1):
        pl.when(live == count)(functools.partial(body, count))


def over_rows(rows, body):
    lax.fori_loop(0, rows, lambda r, c: (body(r), c)[1], 0)


def fill_shifted(blocks_ref, r, count, doubled, tgt_ref, tnorm_ref, tpot_ref, held):
    for k in range(count):
        b = blocks_ref[r, k]
        shift = tile_slice(tpot_ref, b) - tile_slice(tnorm_ref, b)
        held[k] = products(doubled, tgt_ref, b) + shift


def chunk_peak(held, count, rows):
    peak = held[0, rows, :]
    for k in range(1, count):
        peak = jnp.maximum(peak, held[k, rows, :])
    return jnp.max(peak, axis=1, keepdims=True)


def row_kernel(blocks_ref, count_ref, src_ref, tgt_ref, tnorm_ref, tpot_ref,
               high_ref, total_ref, held, high_col, total_col, wide):
    def per_row(r):
        doubled, snorm = doubled_source(src_ref, r)

        def body(count):
            fill_shifted(blocks_ref, r, count, doubled, tgt_ref, tnorm_ref, tpot_ref, held)
            for chunk in range(BLOCK // CHUNK):
                rows = pl.ds(chunk * CHUNK, CHUNK)
                peak = chunk_peak(held, count, rows)
                acc = jnp.exp((held[0, rows, :] - peak) * SCALE)
                for k in range(1, count):
                    acc = acc + jnp.exp((held[k, rows, :] - peak) * SCALE)
                high_col[rows, :] = peak
                total_col[rows, :] = jnp.sum(acc, axis=1, keepdims=True)

        by_count(count_ref[r], held.shape[0], body)
        lanes = pl.ds(pl.multiple_of(r * BLOCK, BLOCK), BLOCK)
        high_ref[:, lanes] = (as_row(high_col[...], wide) - snorm) * SCALE
        total_ref[:, lanes] = as_row(total_col[...], wide)

    over_rows(count_ref.shape[0], per_row)


def column_kernel(blocks_ref, count_ref, src_ref, spot_ref, tgt_ref, tnorm_ref,
                  top_ref, sum_ref, tall):
    top_ref[...] = jnp.full(top_ref.shape, SENTINEL, jnp.float32)
    sum_ref[...] = jnp.zeros(sum_ref.shape, jnp.float32)

    def per_row(r):
        doubled, snorm = doubled_source(src_ref, r)
        shift = as_column(tile_slice(spot_ref, r) - snorm, tall)

        def body(count):
            for k in range(count):
                b = blocks_ref[r, k]
                lanes = pl.ds(pl.multiple_of(b * BLOCK, BLOCK), BLOCK)
                shifted = products(doubled, tgt_ref, b) + shift
                peak = jnp.max(shifted, axis=0, keepdims=True)
                totals = jnp.sum(jnp.exp((shifted - peak) * SCALE), axis=0, keepdims=True)
                highest = (peak - tnorm_ref[:, lanes]) * SCALE
                old_top = top_ref[:, lanes]
                new_top = jnp.maximum(old_top, highest)
                sum_ref[:, lanes] = (sum_ref[:, lanes] * jnp.exp(old_top - new_top)
                                     + totals * jnp.exp(highest - new_top))
                top_ref[:, lanes] = new_top

        by_count(count_ref[r], blocks_ref.shape[1], body)

    over_rows(count_ref.shape[0], per_row)


def project_kernel(blocks_ref, count_ref, src_ref, tgt_ref, tnorm_ref, tpot_ref, feat_ref,
                   top_ref, num_ref, den_ref, held, weights, high_col, den_col, wide):
    def per_row(r):
        doubled, snorm = doubled_source(src_ref, r)

        def body(count):
            fill_shifted(blocks_ref, r, count, doubled, tgt_ref, tnorm_ref, tpot_ref, held)
            for chunk in range(BLOCK // CHUNK):
                rows = pl.ds(chunk * CHUNK, CHUNK)
                peak = chunk_peak(held, count, rows)
                acc = jnp.zeros((CHUNK, BLOCK), jnp.float32)
                for k in range(count):
                    rounded = jnp.exp((held[k, rows, :] - peak) * SCALE).astype(jnp.bfloat16)
                    weights[k, rows, :] = rounded
                    acc = acc + rounded.astype(jnp.float32)
                high_col[rows, :] = peak
                den_col[rows, :] = jnp.sum(acc, axis=1, keepdims=True)
            total = None
            for k in range(count):
                part = lax.dot_general(weights[k], tile_slice(feat_ref, blocks_ref[r, k]),
                                       (((1,), (1,)), ((), ())),
                                       preferred_element_type=jnp.float32)
                total = part if total is None else total + part
            num_ref[pl.ds(pl.multiple_of(r * BLOCK, BLOCK), BLOCK), :] = total

        by_count(count_ref[r], held.shape[0], body)
        lanes = pl.ds(pl.multiple_of(r * BLOCK, BLOCK), BLOCK)
        top_ref[:, lanes] = (as_row(high_col[...], wide) - snorm) * SCALE
        den_ref[:, lanes] = as_row(den_col[...], wide)

    over_rows(count_ref.shape[0], per_row)


def whole(shape):
    return pl.BlockSpec(shape, lambda r, *_: (0,) * len(shape))


def column_scratch():
    return pltpu.VMEM((BLOCK, 1), jnp.float32)


def local_call(kernel, operands, outs, scratch):
    spec = pltpu.PrefetchScalarGridSpec(
        num_scalar_prefetch=2,
        grid=(1,),
        in_specs=[whole(x.shape) for x in operands[2:]],
        out_specs=[whole(o.shape) for o in outs],
        scratch_shapes=scratch,
    )
    return pl.pallas_call(kernel, grid_spec=spec, out_shape=outs)(*operands)


def row_pass(blocks, counts, src, tgt, tnorm, tpot):
    rows = src.shape[1]
    slots = blocks.shape[1]
    return local_call(
        row_kernel, (blocks, counts, src, tgt, tnorm, tpot),
        [jax.ShapeDtypeStruct((1, rows), jnp.float32)] * 2,
        [pltpu.VMEM((slots, BLOCK, BLOCK), jnp.float32), column_scratch(), column_scratch(),
         pltpu.VMEM((BLOCK, 128), jnp.float32)],
    )


def column_pass(blocks, counts, src, spot, tgt, tnorm):
    return local_call(
        column_kernel, (blocks, counts, src, spot, tgt, tnorm),
        [jax.ShapeDtypeStruct(tnorm.shape, jnp.float32)] * 2,
        [pltpu.VMEM((128, BLOCK), jnp.float32)],
    )


def project_pass(blocks, counts, src, tgt, tnorm, tpot, feat):
    rows = src.shape[1]
    slots = blocks.shape[1]
    return local_call(
        project_kernel, (blocks, counts, src, tgt, tnorm, tpot, feat),
        [jax.ShapeDtypeStruct((1, rows), jnp.float32),
         jax.ShapeDtypeStruct((rows, feat.shape[0]), jnp.float32),
         jax.ShapeDtypeStruct((1, rows), jnp.float32)],
        [pltpu.VMEM((slots, BLOCK, BLOCK), jnp.float32),
         pltpu.VMEM((slots, BLOCK, BLOCK), jnp.bfloat16),
         column_scratch(), column_scratch(), pltpu.VMEM((BLOCK, 128), jnp.float32)],
    )


def shards(src_emb, tgt_emb, target_features, src_mass, tgt_mass, kept_blocks, kept_count):
    src_rows = src_emb.shape[1]
    tgt_rows = tgt_emb.shape[1]
    src_t = src_emb
    tnorm = jnp.sum(jnp.square(tgt_emb.astype(jnp.float32)), axis=0).reshape(1, tgt_rows)
    counts = kept_count.reshape(-1)

    tgt_potential = jnp.zeros((tgt_rows,), jnp.float32)
    src_potential = jnp.zeros((src_rows,), jnp.float32)
    for iteration in range(ITERS):
        tpot = tgt_potential.reshape(1, tgt_rows)
        highest, totals = row_pass(kept_blocks, counts, src_t, tgt_emb, tnorm, tpot)
        highest, totals = butterfly_lse(highest.reshape(src_rows), totals.reshape(src_rows), "tgt")
        src_potential = EPSILON * jnp.log(src_mass) - EPSILON * (highest + jnp.log(totals))
        block_top, block_sum = column_pass(
            kept_blocks, counts, src_t, src_potential.reshape(1, src_rows), tgt_emb, tnorm
        )
        block_top, block_sum = butterfly_lse(
            block_top.reshape(tgt_rows), block_sum.reshape(tgt_rows), "src"
        )
        tgt_potential = EPSILON * jnp.log(tgt_mass) - EPSILON * (block_top + jnp.log(block_sum))

    tpot = tgt_potential.reshape(1, tgt_rows)
    local_top, numerator, denominator = project_pass(
        kept_blocks, counts, src_t, tgt_emb, tnorm, tpot, target_features
    )
    numerator, denominator = halving_merge(
        local_top.reshape(src_rows), numerator, denominator.reshape(src_rows), "tgt"
    )
    projected = numerator / denominator[:, None]
    return (projected, src_potential, tgt_potential)


def solution(mesh):
    return jax.shard_map(
        shards,
        mesh=mesh,
        in_specs=(
            P(None, "src"),
            P(None, "tgt"),
            P(None, "tgt"),
            P("src"),
            P("tgt"),
            P("src", "tgt"),
            P("src", "tgt"),
        ),
        out_specs=(P(("src", "tgt"), None), P("src"), P("tgt")),
        check_vma=False,
    )
```

```python
import functools
import math

import jax
import jax.numpy as jnp
from jax import lax
from jax.experimental import pallas as pl
from jax.experimental.pallas import tpu as pltpu
from jax.sharding import PartitionSpec as P

BLOCK = 256
ITERS = 2


SENTINEL = -1e30
EPSILON = 0.1
SCALE = 1.0 / EPSILON
BASE2 = SCALE / math.log(2.0)


def lse_pair(top, total, other_top, other_total):
    overall = jnp.maximum(top, other_top)
    return (overall, total * jnp.exp(top - overall) + other_total * jnp.exp(other_top - overall))


def butterfly_lse(highest, totals, axis):
    size = lax.axis_size(axis)
    step = 1
    while step < size:
        pairs = [(i, i ^ step) for i in range(size)]
        other = lax.ppermute(jnp.stack([highest, totals]), axis, pairs)
        highest, totals = lse_pair(highest, totals, other[0], other[1])
        step *= 2
    return (highest, totals)


def halving_merge(top, numerator, denominator, axis):
    size = lax.axis_size(axis)
    me = lax.axis_index(axis)
    rows = top.shape[0] // size
    top = top.reshape(size, rows)
    denominator = denominator.reshape(size, rows)
    numerator = numerator.reshape(size, rows, numerator.shape[-1])
    step = 1
    while step < size:
        pairs = [(i, i ^ step) for i in range(size)]
        keep = (me // step) % 2
        count = top.shape[0] // 2

        def split(x):
            x = x.reshape((count, 2) + x.shape[1:])
            return (
                lax.dynamic_index_in_dim(x, keep, axis=1, keepdims=False),
                lax.dynamic_index_in_dim(x, 1 - keep, axis=1, keepdims=False),
            )

        top_keep, top_send = split(top)
        den_keep, den_send = split(denominator)
        num_keep, num_send = split(numerator)
        small = lax.ppermute(jnp.stack([top_send, den_send]), axis, pairs)
        num_other = lax.ppermute(num_send, axis, pairs)
        overall = jnp.maximum(top_keep, small[0])
        mine = jnp.exp(top_keep - overall)
        theirs = jnp.exp(small[0] - overall)
        numerator = num_keep * mine[..., None] + num_other * theirs[..., None]
        denominator = den_keep * mine + small[1] * theirs
        top = overall
        step *= 2
    return (numerator.reshape(rows, -1), denominator.reshape(rows))


CHUNK = 64
EXTRA = 16


def tile_slice(ref, b):
    return ref[:, pl.ds(pl.multiple_of(b * BLOCK, BLOCK), BLOCK)]


def row_slice(ref, r):
    return ref[pl.ds(pl.multiple_of(r * BLOCK, BLOCK), BLOCK), :]


def doubled_source(src_ref, r):
    exact = tile_slice(src_ref, r).astype(jnp.float32)
    return (exact * 2.0).astype(jnp.bfloat16), jnp.sum(exact * exact, axis=0, keepdims=True)


def products(doubled, tgt_ref, b):
    return lax.dot_general(doubled, tile_slice(tgt_ref, b), (((0,), (0,)), ((), ())),
                           preferred_element_type=jnp.float32)


def as_row(column, scratch):
    scratch[...] = jnp.broadcast_to(column, scratch.shape)
    return jnp.transpose(scratch[...])[0:1, :]


def as_column(row, scratch):
    scratch[...] = jnp.broadcast_to(row, scratch.shape)
    return jnp.transpose(scratch[...])[:, 0:1]


def by_count(live, slots, body):
    for count in range(1, slots + 1):
        pl.when(live == count)(functools.partial(body, count))


def over_rows(rows, body):
    lax.fori_loop(0, rows, lambda r, c: (body(r), c)[1], 0)


def fill_shifted(blocks_ref, r, count, doubled, tgt_ref, tnorm_ref, tpot_ref, held):
    for k in range(count):
        b = blocks_ref[r, k]
        shift = tile_slice(tpot_ref, b) - tile_slice(tnorm_ref, b)
        held[k] = products(doubled, tgt_ref, b) + shift


def chunk_peak(held, count, rows):
    peak = held[0, rows, :]
    for k in range(1, count):
        peak = jnp.maximum(peak, held[k, rows, :])
    return jnp.max(peak, axis=1, keepdims=True)


def row_kernel(blocks_ref, count_ref, src_ref, tgt_ref, tnorm_ref, tpot_ref,
               high_ref, total_ref, held, high_col, total_col, wide):
    def per_row(r):
        doubled, snorm = doubled_source(src_ref, r)

        def body(count):
            fill_shifted(blocks_ref, r, count, doubled, tgt_ref, tnorm_ref, tpot_ref, held)
            for chunk in range(BLOCK // CHUNK):
                rows = pl.ds(chunk * CHUNK, CHUNK)
                peak = chunk_peak(held, count, rows)
                acc = jnp.exp2((held[0, rows, :] - peak) * BASE2)
                for k in range(1, count):
                    acc = acc + jnp.exp2((held[k, rows, :] - peak) * BASE2)
                high_col[rows, :] = peak
                total_col[rows, :] = jnp.sum(acc, axis=1, keepdims=True)

        by_count(count_ref[r], held.shape[0], body)
        lanes = pl.ds(pl.multiple_of(r * BLOCK, BLOCK), BLOCK)
        high_ref[:, lanes] = (as_row(high_col[...], wide) - snorm) * SCALE
        total_ref[:, lanes] = as_row(total_col[...], wide)

    over_rows(count_ref.shape[0], per_row)


def split_rows(row, ones):
    high = row.astype(jnp.bfloat16).astype(jnp.float32)
    middle = (row - high).astype(jnp.bfloat16).astype(jnp.float32)
    low = row - high - middle
    index = lax.broadcasted_iota(jnp.int32, (EXTRA, row.shape[1]), 0)
    if ones:
        rows = jnp.where(index < 3, 1.0, 0.0)
    else:
        rows = jnp.where(index == 0, high, jnp.where(index == 1, middle,
                                                     jnp.where(index == 2, low, 0.0)))
    return rows.astype(jnp.bfloat16)


def column_kernel(blocks_ref, count_ref, src_ref, spot_ref, tgt_ref, tnorm_ref,
                  top_ref, sum_ref, lhs):
    top_ref[...] = jnp.full(top_ref.shape, SENTINEL, jnp.float32)
    sum_ref[...] = jnp.zeros(sum_ref.shape, jnp.float32)
    width = src_ref.shape[0]

    def per_row(r):
        doubled, snorm = doubled_source(src_ref, r)
        lhs[0:width, :] = doubled
        lhs[width:, :] = split_rows(tile_slice(spot_ref, r) - snorm, False)
        augmented = lhs[...]

        def body(count):
            for k in range(count):
                b = blocks_ref[r, k]
                lanes = pl.ds(pl.multiple_of(b * BLOCK, BLOCK), BLOCK)
                shifted = products(augmented, tgt_ref, b)
                peak = jnp.max(shifted, axis=0, keepdims=True)
                totals = jnp.sum(jnp.exp2((shifted - peak) * BASE2), axis=0, keepdims=True)
                highest = (peak - tnorm_ref[:, lanes]) * SCALE
                old_top = top_ref[:, lanes]
                new_top = jnp.maximum(old_top, highest)
                sum_ref[:, lanes] = (sum_ref[:, lanes] * jnp.exp(old_top - new_top)
                                     + totals * jnp.exp(highest - new_top))
                top_ref[:, lanes] = new_top

        by_count(count_ref[r], blocks_ref.shape[1], body)

    over_rows(count_ref.shape[0], per_row)


def project_kernel(blocks_ref, count_ref, src_ref, tgt_ref, tnorm_ref, tpot_ref, feat_ref,
                   top_ref, num_ref, den_ref, held, weights, high_col, den_col, wide):
    def per_row(r):
        doubled, snorm = doubled_source(src_ref, r)

        def body(count):
            fill_shifted(blocks_ref, r, count, doubled, tgt_ref, tnorm_ref, tpot_ref, held)
            for chunk in range(BLOCK // CHUNK):
                rows = pl.ds(chunk * CHUNK, CHUNK)
                peak = chunk_peak(held, count, rows)
                acc = jnp.zeros((CHUNK, BLOCK), jnp.float32)
                for k in range(count):
                    rounded = jnp.exp2((held[k, rows, :] - peak) * BASE2).astype(jnp.bfloat16)
                    weights[k, rows, :] = rounded
                    acc = acc + rounded.astype(jnp.float32)
                high_col[rows, :] = peak
                den_col[rows, :] = jnp.sum(acc, axis=1, keepdims=True)
            total = None
            for k in range(count):
                part = lax.dot_general(weights[k], tile_slice(feat_ref, blocks_ref[r, k]),
                                       (((1,), (1,)), ((), ())),
                                       preferred_element_type=jnp.float32)
                total = part if total is None else total + part
            num_ref[pl.ds(pl.multiple_of(r * BLOCK, BLOCK), BLOCK), :] = total

        by_count(count_ref[r], held.shape[0], body)
        lanes = pl.ds(pl.multiple_of(r * BLOCK, BLOCK), BLOCK)
        top_ref[:, lanes] = (as_row(high_col[...], wide) - snorm) * SCALE
        den_ref[:, lanes] = as_row(den_col[...], wide)

    over_rows(count_ref.shape[0], per_row)


def whole(shape):
    return pl.BlockSpec(shape, lambda r, *_: (0,) * len(shape))


def column_scratch():
    return pltpu.VMEM((BLOCK, 1), jnp.float32)


def local_call(kernel, operands, outs, scratch):
    spec = pltpu.PrefetchScalarGridSpec(
        num_scalar_prefetch=2,
        grid=(1,),
        in_specs=[whole(x.shape) for x in operands[2:]],
        out_specs=[whole(o.shape) for o in outs],
        scratch_shapes=scratch,
    )
    return pl.pallas_call(kernel, grid_spec=spec, out_shape=outs)(*operands)


def row_pass(blocks, counts, src, tgt, tnorm, tpot):
    rows = src.shape[1]
    slots = blocks.shape[1]
    return local_call(
        row_kernel, (blocks, counts, src, tgt, tnorm, tpot),
        [jax.ShapeDtypeStruct((1, rows), jnp.float32)] * 2,
        [pltpu.VMEM((slots, BLOCK, BLOCK), jnp.float32), column_scratch(), column_scratch(),
         pltpu.VMEM((BLOCK, 128), jnp.float32)],
    )


def column_pass(blocks, counts, src, spot, tgt_ones, tnorm):
    return local_call(
        column_kernel, (blocks, counts, src, spot, tgt_ones, tnorm),
        [jax.ShapeDtypeStruct(tnorm.shape, jnp.float32)] * 2,
        [pltpu.VMEM((src.shape[0] + EXTRA, BLOCK), jnp.bfloat16)],
    )


def project_pass(blocks, counts, src, tgt, tnorm, tpot, feat):
    rows = src.shape[1]
    slots = blocks.shape[1]
    return local_call(
        project_kernel, (blocks, counts, src, tgt, tnorm, tpot, feat),
        [jax.ShapeDtypeStruct((1, rows), jnp.float32),
         jax.ShapeDtypeStruct((rows, feat.shape[0]), jnp.float32),
         jax.ShapeDtypeStruct((1, rows), jnp.float32)],
        [pltpu.VMEM((slots, BLOCK, BLOCK), jnp.float32),
         pltpu.VMEM((slots, BLOCK, BLOCK), jnp.bfloat16),
         column_scratch(), column_scratch(), pltpu.VMEM((BLOCK, 128), jnp.float32)],
    )


def shards(src_emb, tgt_emb, target_features, src_mass, tgt_mass, kept_blocks, kept_count):
    src_rows = src_emb.shape[1]
    tgt_rows = tgt_emb.shape[1]
    src_t = src_emb
    tnorm = jnp.sum(jnp.square(tgt_emb.astype(jnp.float32)), axis=0).reshape(1, tgt_rows)
    counts = kept_count.reshape(-1)
    tgt_ones = jnp.concatenate(
        [tgt_emb, split_rows(jnp.zeros((1, tgt_rows), jnp.float32), True)], axis=0
    )

    tgt_potential = jnp.zeros((tgt_rows,), jnp.float32)
    src_potential = jnp.zeros((src_rows,), jnp.float32)
    for iteration in range(ITERS):
        tpot = tgt_potential.reshape(1, tgt_rows)
        highest, totals = row_pass(kept_blocks, counts, src_t, tgt_emb, tnorm, tpot)
        highest, totals = butterfly_lse(highest.reshape(src_rows), totals.reshape(src_rows), "tgt")
        src_potential = EPSILON * jnp.log(src_mass) - EPSILON * (highest + jnp.log(totals))
        block_top, block_sum = column_pass(
            kept_blocks, counts, src_t, src_potential.reshape(1, src_rows), tgt_ones, tnorm
        )
        block_top, block_sum = butterfly_lse(
            block_top.reshape(tgt_rows), block_sum.reshape(tgt_rows), "src"
        )
        tgt_potential = EPSILON * jnp.log(tgt_mass) - EPSILON * (block_top + jnp.log(block_sum))

    tpot = tgt_potential.reshape(1, tgt_rows)
    local_top, numerator, denominator = project_pass(
        kept_blocks, counts, src_t, tgt_emb, tnorm, tpot, target_features
    )
    numerator, denominator = halving_merge(
        local_top.reshape(src_rows), numerator, denominator.reshape(src_rows), "tgt"
    )
    projected = numerator / denominator[:, None]
    return (projected, src_potential, tgt_potential)


def solution(mesh):
    return jax.shard_map(
        shards,
        mesh=mesh,
        in_specs=(
            P(None, "src"),
            P(None, "tgt"),
            P(None, "tgt"),
            P("src"),
            P("tgt"),
            P("src", "tgt"),
            P("src", "tgt"),
        ),
        out_specs=(P(("src", "tgt"), None), P("src"), P("tgt")),
        check_vma=False,
    )
```

```python
import functools
import math

import jax
import jax.numpy as jnp
from jax import lax
from jax.experimental import pallas as pl
from jax.experimental.pallas import tpu as pltpu
from jax.sharding import PartitionSpec as P

BLOCK = 256
ITERS = 2


SENTINEL = -1e30
EPSILON = 0.1
SCALE = 1.0 / EPSILON
BASE2 = SCALE / math.log(2.0)


def lse_pair(top, total, other_top, other_total):
    overall = jnp.maximum(top, other_top)
    return (overall, total * jnp.exp(top - overall) + other_total * jnp.exp(other_top - overall))


def butterfly_lse(highest, totals, axis):
    size = lax.axis_size(axis)
    step = 1
    while step < size:
        pairs = [(i, i ^ step) for i in range(size)]
        other = lax.ppermute(jnp.stack([highest, totals]), axis, pairs)
        highest, totals = lse_pair(highest, totals, other[0], other[1])
        step *= 2
    return (highest, totals)


def halving_merge(top, numerator, denominator, axis):
    size = lax.axis_size(axis)
    me = lax.axis_index(axis)
    rows = top.shape[0] // size
    top = top.reshape(size, rows)
    denominator = denominator.reshape(size, rows)
    numerator = numerator.reshape(size, rows, numerator.shape[-1])
    step = 1
    while step < size:
        pairs = [(i, i ^ step) for i in range(size)]
        keep = (me // step) % 2
        count = top.shape[0] // 2

        def split(x):
            x = x.reshape((count, 2) + x.shape[1:])
            return (
                lax.dynamic_index_in_dim(x, keep, axis=1, keepdims=False),
                lax.dynamic_index_in_dim(x, 1 - keep, axis=1, keepdims=False),
            )

        top_keep, top_send = split(top)
        den_keep, den_send = split(denominator)
        num_keep, num_send = split(numerator)
        small = lax.ppermute(jnp.stack([top_send, den_send]), axis, pairs)
        num_other = lax.ppermute(num_send, axis, pairs)
        overall = jnp.maximum(top_keep, small[0])
        mine = jnp.exp(top_keep - overall)
        theirs = jnp.exp(small[0] - overall)
        numerator = num_keep * mine[..., None] + num_other * theirs[..., None]
        denominator = den_keep * mine + small[1] * theirs
        top = overall
        step *= 2
    return (numerator.reshape(rows, -1), denominator.reshape(rows))


CHUNK = 64
EXTRA = 16
VMEM_LIMIT = 24 * 1024 * 1024


def tile_slice(ref, b):
    return ref[:, pl.ds(pl.multiple_of(b * BLOCK, BLOCK), BLOCK)]


def row_slice(ref, r):
    return ref[pl.ds(pl.multiple_of(r * BLOCK, BLOCK), BLOCK), :]


def doubled_source(src_ref, r):
    exact = tile_slice(src_ref, r).astype(jnp.float32)
    return (exact * 2.0).astype(jnp.bfloat16), jnp.sum(exact * exact, axis=0, keepdims=True)


def products(doubled, tgt_ref, b):
    return lax.dot_general(doubled, tile_slice(tgt_ref, b), (((0,), (0,)), ((), ())),
                           preferred_element_type=jnp.float32)


def as_row(column, scratch):
    scratch[...] = jnp.broadcast_to(column, scratch.shape)
    return jnp.transpose(scratch[...])[0:1, :]


def as_column(row, scratch):
    scratch[...] = jnp.broadcast_to(row, scratch.shape)
    return jnp.transpose(scratch[...])[:, 0:1]


def by_count(live, slots, body):
    for count in range(1, slots + 1):
        pl.when(live == count)(functools.partial(body, count))


def over_rows(rows, body):
    lax.fori_loop(0, rows, lambda r, c: (body(r), c)[1], 0)


def fill_shifted(blocks_ref, r, count, doubled, tgt_ref, tnorm_ref, tpot_ref, held):
    for k in range(count):
        b = blocks_ref[r, k]
        shift = tile_slice(tpot_ref, b) - tile_slice(tnorm_ref, b)
        held[k] = products(doubled, tgt_ref, b) + shift


def chunk_peak(held, count, rows):
    peak = held[0, rows, :]
    for k in range(1, count):
        peak = jnp.maximum(peak, held[k, rows, :])
    return jnp.max(peak, axis=1, keepdims=True)


def row_kernel(blocks_ref, count_ref, src_ref, tgt_ref, tnorm_ref, tpot_ref,
               high_ref, total_ref, held, high_col, total_col, wide):
    def per_row(r):
        doubled, snorm = doubled_source(src_ref, r)

        def body(count):
            fill_shifted(blocks_ref, r, count, doubled, tgt_ref, tnorm_ref, tpot_ref, held)
            for chunk in range(BLOCK // CHUNK):
                rows = pl.ds(chunk * CHUNK, CHUNK)
                peak = chunk_peak(held, count, rows)
                acc = jnp.exp2((held[0, rows, :] - peak) * BASE2)
                for k in range(1, count):
                    acc = acc + jnp.exp2((held[k, rows, :] - peak) * BASE2)
                high_col[rows, :] = peak
                total_col[rows, :] = jnp.sum(acc, axis=1, keepdims=True)

        by_count(count_ref[r], held.shape[0], body)
        lanes = pl.ds(pl.multiple_of(r * BLOCK, BLOCK), BLOCK)
        high_ref[:, lanes] = (as_row(high_col[...], wide) - snorm) * SCALE
        total_ref[:, lanes] = as_row(total_col[...], wide)

    over_rows(count_ref.shape[0], per_row)


def split_rows(row, ones):
    high = row.astype(jnp.bfloat16).astype(jnp.float32)
    middle = (row - high).astype(jnp.bfloat16).astype(jnp.float32)
    low = row - high - middle
    index = lax.broadcasted_iota(jnp.int32, (EXTRA, row.shape[1]), 0)
    if ones:
        rows = jnp.where(index < 3, 1.0, 0.0)
    else:
        rows = jnp.where(index == 0, high, jnp.where(index == 1, middle,
                                                     jnp.where(index == 2, low, 0.0)))
    return rows.astype(jnp.bfloat16)


def column_kernel(blocks_ref, count_ref, src_ref, spot_ref, tgt_ref, tnorm_ref,
                  top_ref, sum_ref, lhs):
    top_ref[...] = jnp.full(top_ref.shape, SENTINEL, jnp.float32)
    sum_ref[...] = jnp.zeros(sum_ref.shape, jnp.float32)
    width = src_ref.shape[0]

    def per_row(r):
        doubled, snorm = doubled_source(src_ref, r)
        lhs[0:width, :] = doubled
        lhs[width:, :] = split_rows(tile_slice(spot_ref, r) - snorm, False)
        augmented = lhs[...]

        def body(count):
            for k in range(count):
                b = blocks_ref[r, k]
                lanes = pl.ds(pl.multiple_of(b * BLOCK, BLOCK), BLOCK)
                shifted = products(augmented, tgt_ref, b)
                peak = jnp.max(shifted, axis=0, keepdims=True)
                totals = jnp.sum(jnp.exp2((shifted - peak) * BASE2), axis=0, keepdims=True)
                highest = (peak - tnorm_ref[:, lanes]) * SCALE
                old_top = top_ref[:, lanes]
                new_top = jnp.maximum(old_top, highest)
                sum_ref[:, lanes] = (sum_ref[:, lanes] * jnp.exp(old_top - new_top)
                                     + totals * jnp.exp(highest - new_top))
                top_ref[:, lanes] = new_top

        by_count(count_ref[r], blocks_ref.shape[1], body)

    over_rows(count_ref.shape[0], per_row)


def project_kernel(blocks_ref, count_ref, src_ref, tgt_ref, tnorm_ref, tpot_ref, feat_ref,
                   top_ref, num_ref, den_ref, held, weights, high_col, den_col, wide):
    def per_row(r):
        doubled, snorm = doubled_source(src_ref, r)

        def body(count):
            fill_shifted(blocks_ref, r, count, doubled, tgt_ref, tnorm_ref, tpot_ref, held)
            for chunk in range(BLOCK // CHUNK):
                rows = pl.ds(chunk * CHUNK, CHUNK)
                peak = chunk_peak(held, count, rows)
                acc = jnp.zeros((CHUNK, BLOCK), jnp.float32)
                for k in range(count):
                    rounded = jnp.exp2((held[k, rows, :] - peak) * BASE2).astype(jnp.bfloat16)
                    weights[k, rows, :] = rounded
                    acc = acc + rounded.astype(jnp.float32)
                high_col[rows, :] = peak
                den_col[rows, :] = jnp.sum(acc, axis=1, keepdims=True)
            total = None
            for k in range(count):
                part = lax.dot_general(weights[k], tile_slice(feat_ref, blocks_ref[r, k]),
                                       (((1,), (1,)), ((), ())),
                                       preferred_element_type=jnp.float32)
                total = part if total is None else total + part
            num_ref[pl.ds(pl.multiple_of(r * BLOCK, BLOCK), BLOCK), :] = total

        by_count(count_ref[r], held.shape[0], body)
        lanes = pl.ds(pl.multiple_of(r * BLOCK, BLOCK), BLOCK)
        top_ref[:, lanes] = (as_row(high_col[...], wide) - snorm) * SCALE
        den_ref[:, lanes] = as_row(den_col[...], wide)

    over_rows(count_ref.shape[0], per_row)


def whole(shape):
    return pl.BlockSpec(shape, lambda r, *_: (0,) * len(shape))


def column_scratch():
    return pltpu.VMEM((BLOCK, 1), jnp.float32)


def local_call(kernel, operands, outs, scratch):
    spec = pltpu.PrefetchScalarGridSpec(
        num_scalar_prefetch=2,
        grid=(1,),
        in_specs=[whole(x.shape) for x in operands[2:]],
        out_specs=[whole(o.shape) for o in outs],
        scratch_shapes=scratch,
    )
    return pl.pallas_call(
        kernel, grid_spec=spec, out_shape=outs,
        compiler_params=pltpu.CompilerParams(vmem_limit_bytes=VMEM_LIMIT),
    )(*operands)


def row_pass(blocks, counts, src, tgt, tnorm, tpot):
    rows = src.shape[1]
    slots = blocks.shape[1]
    return local_call(
        row_kernel, (blocks, counts, src, tgt, tnorm, tpot),
        [jax.ShapeDtypeStruct((1, rows), jnp.float32)] * 2,
        [pltpu.VMEM((slots, BLOCK, BLOCK), jnp.float32), column_scratch(), column_scratch(),
         pltpu.VMEM((BLOCK, 128), jnp.float32)],
    )


def column_pass(blocks, counts, src, spot, tgt_ones, tnorm):
    return local_call(
        column_kernel, (blocks, counts, src, spot, tgt_ones, tnorm),
        [jax.ShapeDtypeStruct(tnorm.shape, jnp.float32)] * 2,
        [pltpu.VMEM((src.shape[0] + EXTRA, BLOCK), jnp.bfloat16)],
    )


def project_pass(blocks, counts, src, tgt, tnorm, tpot, feat):
    rows = src.shape[1]
    slots = blocks.shape[1]
    return local_call(
        project_kernel, (blocks, counts, src, tgt, tnorm, tpot, feat),
        [jax.ShapeDtypeStruct((1, rows), jnp.float32),
         jax.ShapeDtypeStruct((rows, feat.shape[0]), jnp.float32),
         jax.ShapeDtypeStruct((1, rows), jnp.float32)],
        [pltpu.VMEM((slots, BLOCK, BLOCK), jnp.float32),
         pltpu.VMEM((slots, BLOCK, BLOCK), jnp.bfloat16),
         column_scratch(), column_scratch(), pltpu.VMEM((BLOCK, 128), jnp.float32)],
    )


def shards(src_emb, tgt_emb, target_features, src_mass, tgt_mass, kept_blocks, kept_count):
    src_rows = src_emb.shape[1]
    tgt_rows = tgt_emb.shape[1]
    src_t = src_emb
    tnorm = jnp.sum(jnp.square(tgt_emb.astype(jnp.float32)), axis=0).reshape(1, tgt_rows)
    counts = kept_count.reshape(-1)
    tgt_ones = jnp.concatenate(
        [tgt_emb, split_rows(jnp.zeros((1, tgt_rows), jnp.float32), True)], axis=0
    )

    tgt_potential = jnp.zeros((tgt_rows,), jnp.float32)
    src_potential = jnp.zeros((src_rows,), jnp.float32)
    for iteration in range(ITERS):
        tpot = tgt_potential.reshape(1, tgt_rows)
        highest, totals = row_pass(kept_blocks, counts, src_t, tgt_emb, tnorm, tpot)
        highest, totals = butterfly_lse(highest.reshape(src_rows), totals.reshape(src_rows), "tgt")
        src_potential = EPSILON * jnp.log(src_mass) - EPSILON * (highest + jnp.log(totals))
        block_top, block_sum = column_pass(
            kept_blocks, counts, src_t, src_potential.reshape(1, src_rows), tgt_ones, tnorm
        )
        block_top, block_sum = butterfly_lse(
            block_top.reshape(tgt_rows), block_sum.reshape(tgt_rows), "src"
        )
        tgt_potential = EPSILON * jnp.log(tgt_mass) - EPSILON * (block_top + jnp.log(block_sum))

    tpot = tgt_potential.reshape(1, tgt_rows)
    local_top, numerator, denominator = project_pass(
        kept_blocks, counts, src_t, tgt_emb, tnorm, tpot, target_features
    )
    numerator, denominator = halving_merge(
        local_top.reshape(src_rows), numerator, denominator.reshape(src_rows), "tgt"
    )
    projected = numerator / denominator[:, None]
    return (projected, src_potential, tgt_potential)


def solution(mesh):
    return jax.shard_map(
        shards,
        mesh=mesh,
        in_specs=(
            P(None, "src"),
            P(None, "tgt"),
            P(None, "tgt"),
            P("src"),
            P("tgt"),
            P("src", "tgt"),
            P("src", "tgt"),
        ),
        out_specs=(P(("src", "tgt"), None), P("src"), P("tgt")),
        check_vma=False,
    )
```

```python
import functools
import math

import jax
import jax.numpy as jnp
from jax import lax
from jax.experimental import pallas as pl
from jax.experimental.pallas import tpu as pltpu
from jax.sharding import PartitionSpec as P

BLOCK = 256
ITERS = 2


SENTINEL = -1e30
EPSILON = 0.1
SCALE = 1.0 / EPSILON
BASE2 = SCALE / math.log(2.0)


def lse_pair(top, total, other_top, other_total):
    overall = jnp.maximum(top, other_top)
    return (overall, total * jnp.exp(top - overall) + other_total * jnp.exp(other_top - overall))


def butterfly_lse(highest, totals, axis):
    size = lax.axis_size(axis)
    step = 1
    while step < size:
        pairs = [(i, i ^ step) for i in range(size)]
        other = lax.ppermute(jnp.stack([highest, totals]), axis, pairs)
        highest, totals = lse_pair(highest, totals, other[0], other[1])
        step *= 2
    return (highest, totals)


def halving_merge(top, numerator, denominator, axis):
    size = lax.axis_size(axis)
    me = lax.axis_index(axis)
    rows = top.shape[0] // size
    top = top.reshape(size, rows)
    denominator = denominator.reshape(size, rows)
    numerator = numerator.reshape(size, rows, numerator.shape[-1])
    step = 1
    while step < size:
        pairs = [(i, i ^ step) for i in range(size)]
        keep = (me // step) % 2
        count = top.shape[0] // 2

        def split(x):
            x = x.reshape((count, 2) + x.shape[1:])
            return (
                lax.dynamic_index_in_dim(x, keep, axis=1, keepdims=False),
                lax.dynamic_index_in_dim(x, 1 - keep, axis=1, keepdims=False),
            )

        top_keep, top_send = split(top)
        den_keep, den_send = split(denominator)
        num_keep, num_send = split(numerator)
        small = lax.ppermute(jnp.stack([top_send, den_send]), axis, pairs)
        num_other = lax.ppermute(num_send, axis, pairs)
        overall = jnp.maximum(top_keep, small[0])
        mine = jnp.exp(top_keep - overall)
        theirs = jnp.exp(small[0] - overall)
        numerator = num_keep * mine[..., None] + num_other * theirs[..., None]
        denominator = den_keep * mine + small[1] * theirs
        top = overall
        step *= 2
    return (numerator.reshape(rows, -1), denominator.reshape(rows))


CHUNK = 64
EXTRA = 16
VMEM_LIMIT = 24 * 1024 * 1024


def tile_slice(ref, b):
    return ref[:, pl.ds(pl.multiple_of(b * BLOCK, BLOCK), BLOCK)]


def row_slice(ref, r):
    return ref[pl.ds(pl.multiple_of(r * BLOCK, BLOCK), BLOCK), :]


def doubled_source(src_ref, r):
    exact = tile_slice(src_ref, r).astype(jnp.float32)
    return (exact * 2.0).astype(jnp.bfloat16), jnp.sum(exact * exact, axis=0, keepdims=True)


def products(doubled, tgt_ref, b):
    return lax.dot_general(doubled, tile_slice(tgt_ref, b), (((0,), (0,)), ((), ())),
                           preferred_element_type=jnp.float32)


def as_row(column, scratch):
    scratch[...] = jnp.broadcast_to(column, scratch.shape)
    return jnp.transpose(scratch[...])[0:1, :]


def as_column(row, scratch):
    scratch[...] = jnp.broadcast_to(row, scratch.shape)
    return jnp.transpose(scratch[...])[:, 0:1]


def by_count(live, slots, body):
    for count in range(1, slots + 1):
        pl.when(live == count)(functools.partial(body, count))


def over_rows(rows, body):
    lax.fori_loop(0, rows, lambda r, c: (body(r), c)[1], 0)


def fill_shifted(blocks_ref, r, count, doubled, tgt_ref, tnorm_ref, tpot_ref, held):
    for k in range(count):
        b = blocks_ref[r, k]
        shift = tile_slice(tpot_ref, b) - tile_slice(tnorm_ref, b)
        held[k] = products(doubled, tgt_ref, b) + shift


def chunk_peak(held, count, rows):
    peak = held[0, rows, :]
    for k in range(1, count):
        peak = jnp.maximum(peak, held[k, rows, :])
    return jnp.max(peak, axis=1, keepdims=True)


def row_kernel(blocks_ref, count_ref, src_ref, tgt_ref, tnorm_ref, tpot_ref,
               high_ref, total_ref, held, high_col, total_col, wide):
    def per_row(r):
        doubled, snorm = doubled_source(src_ref, r)

        def body(count):
            fill_shifted(blocks_ref, r, count, doubled, tgt_ref, tnorm_ref, tpot_ref, held)
            for chunk in range(BLOCK // CHUNK):
                rows = pl.ds(chunk * CHUNK, CHUNK)
                peak = chunk_peak(held, count, rows)
                acc = jnp.exp2((held[0, rows, :] - peak) * BASE2)
                for k in range(1, count):
                    acc = acc + jnp.exp2((held[k, rows, :] - peak) * BASE2)
                high_col[rows, :] = peak
                total_col[rows, :] = jnp.sum(acc, axis=1, keepdims=True)

        by_count(count_ref[r], held.shape[0], body)
        lanes = pl.ds(pl.multiple_of(r * BLOCK, BLOCK), BLOCK)
        high_ref[:, lanes] = (as_row(high_col[...], wide) - snorm) * SCALE
        total_ref[:, lanes] = as_row(total_col[...], wide)

    over_rows(count_ref.shape[0], per_row)


def split_rows(row, ones):
    high = row.astype(jnp.bfloat16).astype(jnp.float32)
    middle = (row - high).astype(jnp.bfloat16).astype(jnp.float32)
    low = row - high - middle
    index = lax.broadcasted_iota(jnp.int32, (EXTRA, row.shape[1]), 0)
    if ones:
        rows = jnp.where(index < 3, 1.0, 0.0)
    else:
        rows = jnp.where(index == 0, high, jnp.where(index == 1, middle,
                                                     jnp.where(index == 2, low, 0.0)))
    return rows.astype(jnp.bfloat16)


def column_kernel(blocks_ref, count_ref, src_ref, spot_ref, tgt_ref, tnorm_ref,
                  top_ref, sum_ref, lhs):
    top_ref[...] = jnp.full(top_ref.shape, SENTINEL, jnp.float32)
    sum_ref[...] = jnp.zeros(sum_ref.shape, jnp.float32)
    width = src_ref.shape[0]

    def per_row(r):
        doubled, snorm = doubled_source(src_ref, r)
        lhs[0:width, :] = doubled
        lhs[width:, :] = split_rows(tile_slice(spot_ref, r) - snorm, False)
        augmented = lhs[...]

        def body(count):
            for k in range(count):
                b = blocks_ref[r, k]
                lanes = pl.ds(pl.multiple_of(b * BLOCK, BLOCK), BLOCK)
                shifted = products(augmented, tgt_ref, b)
                peak = jnp.max(shifted, axis=0, keepdims=True)
                totals = jnp.sum(jnp.exp2((shifted - peak) * BASE2), axis=0, keepdims=True)
                highest = (peak - tnorm_ref[:, lanes]) * SCALE
                old_top = top_ref[:, lanes]
                new_top = jnp.maximum(old_top, highest)
                sum_ref[:, lanes] = (sum_ref[:, lanes] * jnp.exp(old_top - new_top)
                                     + totals * jnp.exp(highest - new_top))
                top_ref[:, lanes] = new_top

        by_count(count_ref[r], blocks_ref.shape[1], body)

    over_rows(count_ref.shape[0], per_row)


def project_kernel(blocks_ref, count_ref, src_ref, tgt_ref, tnorm_ref, tpot_ref, feat_ref,
                   top_ref, num_ref, den_ref, held, weights, high_col, den_col, wide):
    def per_row(r):
        doubled, snorm = doubled_source(src_ref, r)

        def body(count):
            fill_shifted(blocks_ref, r, count, doubled, tgt_ref, tnorm_ref, tpot_ref, held)
            for chunk in range(BLOCK // CHUNK):
                rows = pl.ds(chunk * CHUNK, CHUNK)
                peak = chunk_peak(held, count, rows)
                acc = jnp.zeros((CHUNK, BLOCK), jnp.float32)
                for k in range(count):
                    rounded = jnp.exp2((held[k, rows, :] - peak) * BASE2).astype(jnp.bfloat16)
                    weights[k, rows, :] = rounded
                    acc = acc + rounded.astype(jnp.float32)
                high_col[rows, :] = peak
                den_col[rows, :] = jnp.sum(acc, axis=1, keepdims=True)
            total = None
            for k in range(count):
                part = lax.dot_general(weights[k], tile_slice(feat_ref, blocks_ref[r, k]),
                                       (((1,), (1,)), ((), ())),
                                       preferred_element_type=jnp.float32)
                total = part if total is None else total + part
            num_ref[pl.ds(pl.multiple_of(r * BLOCK, BLOCK), BLOCK), :] = total

        by_count(count_ref[r], held.shape[0], body)
        lanes = pl.ds(pl.multiple_of(r * BLOCK, BLOCK), BLOCK)
        top_ref[:, lanes] = (as_row(high_col[...], wide) - snorm) * SCALE
        den_ref[:, lanes] = as_row(den_col[...], wide)

    over_rows(count_ref.shape[0], per_row)


def whole(shape):
    return pl.BlockSpec(shape, lambda r, *_: (0,) * len(shape))


def resident():
    return pl.BlockSpec(memory_space=pltpu.VMEM)


def column_scratch():
    return pltpu.VMEM((BLOCK, 1), jnp.float32)


def local_call(kernel, operands, outs, scratch):
    spec = pltpu.PrefetchScalarGridSpec(
        num_scalar_prefetch=2,
        grid=(1,),
        in_specs=[resident() for x in operands[2:]],
        out_specs=[resident() for o in outs],
        scratch_shapes=scratch,
    )
    return pl.pallas_call(
        kernel, grid_spec=spec, out_shape=outs,
        compiler_params=pltpu.CompilerParams(vmem_limit_bytes=VMEM_LIMIT),
    )(*operands)


def row_pass(blocks, counts, src, tgt, tnorm, tpot):
    rows = src.shape[1]
    slots = blocks.shape[1]
    return local_call(
        row_kernel, (blocks, counts, src, tgt, tnorm, tpot),
        [jax.ShapeDtypeStruct((1, rows), jnp.float32)] * 2,
        [pltpu.VMEM((slots, BLOCK, BLOCK), jnp.float32), column_scratch(), column_scratch(),
         pltpu.VMEM((BLOCK, 128), jnp.float32)],
    )


def column_pass(blocks, counts, src, spot, tgt_ones, tnorm):
    return local_call(
        column_kernel, (blocks, counts, src, spot, tgt_ones, tnorm),
        [jax.ShapeDtypeStruct(tnorm.shape, jnp.float32)] * 2,
        [pltpu.VMEM((src.shape[0] + EXTRA, BLOCK), jnp.bfloat16)],
    )


def project_pass(blocks, counts, src, tgt, tnorm, tpot, feat):
    rows = src.shape[1]
    slots = blocks.shape[1]
    return local_call(
        project_kernel, (blocks, counts, src, tgt, tnorm, tpot, feat),
        [jax.ShapeDtypeStruct((1, rows), jnp.float32),
         jax.ShapeDtypeStruct((rows, feat.shape[0]), jnp.float32),
         jax.ShapeDtypeStruct((1, rows), jnp.float32)],
        [pltpu.VMEM((slots, BLOCK, BLOCK), jnp.float32),
         pltpu.VMEM((slots, BLOCK, BLOCK), jnp.bfloat16),
         column_scratch(), column_scratch(), pltpu.VMEM((BLOCK, 128), jnp.float32)],
    )


def shards(src_emb, tgt_emb, target_features, src_mass, tgt_mass, kept_blocks, kept_count):
    src_rows = src_emb.shape[1]
    tgt_rows = tgt_emb.shape[1]
    src_t = src_emb
    tnorm = jnp.sum(jnp.square(tgt_emb.astype(jnp.float32)), axis=0).reshape(1, tgt_rows)
    counts = kept_count.reshape(-1)
    tgt_ones = jnp.concatenate(
        [tgt_emb, split_rows(jnp.zeros((1, tgt_rows), jnp.float32), True)], axis=0
    )

    tgt_potential = jnp.zeros((tgt_rows,), jnp.float32)
    src_potential = jnp.zeros((src_rows,), jnp.float32)
    for iteration in range(ITERS):
        tpot = tgt_potential.reshape(1, tgt_rows)
        highest, totals = row_pass(kept_blocks, counts, src_t, tgt_emb, tnorm, tpot)
        highest, totals = butterfly_lse(highest.reshape(src_rows), totals.reshape(src_rows), "tgt")
        src_potential = EPSILON * jnp.log(src_mass) - EPSILON * (highest + jnp.log(totals))
        block_top, block_sum = column_pass(
            kept_blocks, counts, src_t, src_potential.reshape(1, src_rows), tgt_ones, tnorm
        )
        block_top, block_sum = butterfly_lse(
            block_top.reshape(tgt_rows), block_sum.reshape(tgt_rows), "src"
        )
        tgt_potential = EPSILON * jnp.log(tgt_mass) - EPSILON * (block_top + jnp.log(block_sum))

    tpot = tgt_potential.reshape(1, tgt_rows)
    local_top, numerator, denominator = project_pass(
        kept_blocks, counts, src_t, tgt_emb, tnorm, tpot, target_features
    )
    numerator, denominator = halving_merge(
        local_top.reshape(src_rows), numerator, denominator.reshape(src_rows), "tgt"
    )
    projected = numerator / denominator[:, None]
    return (projected, src_potential, tgt_potential)


def solution(mesh):
    return jax.shard_map(
        shards,
        mesh=mesh,
        in_specs=(
            P(None, "src"),
            P(None, "tgt"),
            P(None, "tgt"),
            P("src"),
            P("tgt"),
            P("src", "tgt"),
            P("src", "tgt"),
        ),
        out_specs=(P(("src", "tgt"), None), P("src"), P("tgt")),
        check_vma=False,
    )
```

```python
import functools
import math

import jax
import jax.numpy as jnp
from jax import lax
from jax.experimental import pallas as pl
from jax.experimental.pallas import tpu as pltpu
from jax.sharding import PartitionSpec as P

BLOCK = 256
ITERS = 2


SENTINEL = -1e30
EPSILON = 0.1
SCALE = 1.0 / EPSILON
BASE2 = SCALE / math.log(2.0)


def lse_pair(value, other):
    overall = jnp.maximum(value, other)
    return overall + jnp.log(jnp.exp(value - overall) + jnp.exp(other - overall))


def butterfly_lse(value, axis):
    size = lax.axis_size(axis)
    step = 1
    while step < size:
        pairs = [(i, i ^ step) for i in range(size)]
        value = lse_pair(value, lax.ppermute(value, axis, pairs))
        step *= 2
    return value


def halving_merge(top, numerator, denominator, axis):
    size = lax.axis_size(axis)
    me = lax.axis_index(axis)
    rows = top.shape[0] // size
    top = top.reshape(size, rows)
    denominator = denominator.reshape(size, rows)
    numerator = numerator.reshape(size, rows, numerator.shape[-1])
    step = 1
    while step < size:
        pairs = [(i, i ^ step) for i in range(size)]
        keep = (me // step) % 2
        count = top.shape[0] // 2

        def split(x):
            x = x.reshape((count, 2) + x.shape[1:])
            return (
                lax.dynamic_index_in_dim(x, keep, axis=1, keepdims=False),
                lax.dynamic_index_in_dim(x, 1 - keep, axis=1, keepdims=False),
            )

        top_keep, top_send = split(top)
        den_keep, den_send = split(denominator)
        num_keep, num_send = split(numerator)
        small = lax.ppermute(jnp.stack([top_send, den_send]), axis, pairs)
        num_other = lax.ppermute(num_send, axis, pairs)
        overall = jnp.maximum(top_keep, small[0])
        mine = jnp.exp(top_keep - overall)
        theirs = jnp.exp(small[0] - overall)
        numerator = num_keep * mine[..., None] + num_other * theirs[..., None]
        denominator = den_keep * mine + small[1] * theirs
        top = overall
        step *= 2
    return (numerator.reshape(rows, -1), denominator.reshape(rows))


CHUNK = 64
EXTRA = 16
VMEM_LIMIT = 24 * 1024 * 1024


def tile_slice(ref, b):
    return ref[:, pl.ds(pl.multiple_of(b * BLOCK, BLOCK), BLOCK)]


def row_slice(ref, r):
    return ref[pl.ds(pl.multiple_of(r * BLOCK, BLOCK), BLOCK), :]


def doubled_source(src_ref, r):
    exact = tile_slice(src_ref, r).astype(jnp.float32)
    return (exact * 2.0).astype(jnp.bfloat16), jnp.sum(exact * exact, axis=0, keepdims=True)


def products(doubled, tgt_ref, b):
    return lax.dot_general(doubled, tile_slice(tgt_ref, b), (((0,), (0,)), ((), ())),
                           preferred_element_type=jnp.float32)


def as_row(column, scratch):
    scratch[...] = jnp.broadcast_to(column, scratch.shape)
    return jnp.transpose(scratch[...])[0:1, :]


def as_column(row, scratch):
    scratch[...] = jnp.broadcast_to(row, scratch.shape)
    return jnp.transpose(scratch[...])[:, 0:1]


def by_count(live, slots, body):
    for count in range(1, slots + 1):
        pl.when(live == count)(functools.partial(body, count))


def over_rows(rows, body):
    lax.fori_loop(0, rows, lambda r, c: (body(r), c)[1], 0)


def fill_shifted(blocks_ref, r, count, doubled, tgt_ref, tnorm_ref, tpot_ref, held):
    for k in range(count):
        b = blocks_ref[r, k]
        shift = tile_slice(tpot_ref, b) - tile_slice(tnorm_ref, b)
        held[k] = products(doubled, tgt_ref, b) + shift


def chunk_peak(held, count, rows):
    peak = held[0, rows, :]
    for k in range(1, count):
        peak = jnp.maximum(peak, held[k, rows, :])
    return jnp.max(peak, axis=1, keepdims=True)


def row_kernel(blocks_ref, count_ref, src_ref, tgt_ref, tnorm_ref, tpot_ref,
               lse_ref, held, high_col, total_col, wide):
    def per_row(r):
        doubled, snorm = doubled_source(src_ref, r)

        def body(count):
            fill_shifted(blocks_ref, r, count, doubled, tgt_ref, tnorm_ref, tpot_ref, held)
            for chunk in range(BLOCK // CHUNK):
                rows = pl.ds(chunk * CHUNK, CHUNK)
                peak = chunk_peak(held, count, rows)
                acc = jnp.exp2((held[0, rows, :] - peak) * BASE2)
                for k in range(1, count):
                    acc = acc + jnp.exp2((held[k, rows, :] - peak) * BASE2)
                high_col[rows, :] = peak
                total_col[rows, :] = jnp.sum(acc, axis=1, keepdims=True)

        by_count(count_ref[r], held.shape[0], body)
        lanes = pl.ds(pl.multiple_of(r * BLOCK, BLOCK), BLOCK)
        lse_ref[:, lanes] = ((as_row(high_col[...], wide) - snorm) * SCALE
                             + jnp.log(as_row(total_col[...], wide)))

    over_rows(count_ref.shape[0], per_row)


def split_rows(row, ones):
    high = row.astype(jnp.bfloat16).astype(jnp.float32)
    middle = (row - high).astype(jnp.bfloat16).astype(jnp.float32)
    low = row - high - middle
    index = lax.broadcasted_iota(jnp.int32, (EXTRA, row.shape[1]), 0)
    if ones:
        rows = jnp.where(index < 3, 1.0, 0.0)
    else:
        rows = jnp.where(index == 0, high, jnp.where(index == 1, middle,
                                                     jnp.where(index == 2, low, 0.0)))
    return rows.astype(jnp.bfloat16)


def column_kernel(blocks_ref, count_ref, src_ref, spot_ref, tgt_ref, tnorm_ref,
                  lse_ref, top_ref, sum_ref, lhs):
    top_ref[...] = jnp.full(top_ref.shape, SENTINEL, jnp.float32)
    sum_ref[...] = jnp.zeros(sum_ref.shape, jnp.float32)
    width = src_ref.shape[0]

    def per_row(r):
        doubled, snorm = doubled_source(src_ref, r)
        lhs[0:width, :] = doubled
        lhs[width:, :] = split_rows(tile_slice(spot_ref, r) - snorm, False)
        augmented = lhs[...]

        def body(count):
            for k in range(count):
                b = blocks_ref[r, k]
                lanes = pl.ds(pl.multiple_of(b * BLOCK, BLOCK), BLOCK)
                shifted = products(augmented, tgt_ref, b)
                peak = jnp.max(shifted, axis=0, keepdims=True)
                totals = jnp.sum(jnp.exp2((shifted - peak) * BASE2), axis=0, keepdims=True)
                highest = (peak - tnorm_ref[:, lanes]) * SCALE
                old_top = top_ref[:, lanes]
                new_top = jnp.maximum(old_top, highest)
                sum_ref[:, lanes] = (sum_ref[:, lanes] * jnp.exp(old_top - new_top)
                                     + totals * jnp.exp(highest - new_top))
                top_ref[:, lanes] = new_top

        by_count(count_ref[r], blocks_ref.shape[1], body)

    over_rows(count_ref.shape[0], per_row)
    totals = sum_ref[...]
    lse_ref[...] = jnp.where(totals > 0.0, top_ref[...] + jnp.log(totals), SENTINEL)


def project_kernel(blocks_ref, count_ref, src_ref, tgt_ref, tnorm_ref, tpot_ref, feat_ref,
                   top_ref, num_ref, den_ref, held, weights, high_col, den_col, wide):
    def per_row(r):
        doubled, snorm = doubled_source(src_ref, r)

        def body(count):
            fill_shifted(blocks_ref, r, count, doubled, tgt_ref, tnorm_ref, tpot_ref, held)
            for chunk in range(BLOCK // CHUNK):
                rows = pl.ds(chunk * CHUNK, CHUNK)
                peak = chunk_peak(held, count, rows)
                acc = jnp.zeros((CHUNK, BLOCK), jnp.float32)
                for k in range(count):
                    rounded = jnp.exp2((held[k, rows, :] - peak) * BASE2).astype(jnp.bfloat16)
                    weights[k, rows, :] = rounded
                    acc = acc + rounded.astype(jnp.float32)
                high_col[rows, :] = peak
                den_col[rows, :] = jnp.sum(acc, axis=1, keepdims=True)
            total = None
            for k in range(count):
                part = lax.dot_general(weights[k], tile_slice(feat_ref, blocks_ref[r, k]),
                                       (((1,), (1,)), ((), ())),
                                       preferred_element_type=jnp.float32)
                total = part if total is None else total + part
            num_ref[pl.ds(pl.multiple_of(r * BLOCK, BLOCK), BLOCK), :] = total

        by_count(count_ref[r], held.shape[0], body)
        lanes = pl.ds(pl.multiple_of(r * BLOCK, BLOCK), BLOCK)
        top_ref[:, lanes] = (as_row(high_col[...], wide) - snorm) * SCALE
        den_ref[:, lanes] = as_row(den_col[...], wide)

    over_rows(count_ref.shape[0], per_row)


def whole(shape):
    return pl.BlockSpec(shape, lambda r, *_: (0,) * len(shape))


def resident():
    return pl.BlockSpec(memory_space=pltpu.VMEM)


def column_scratch():
    return pltpu.VMEM((BLOCK, 1), jnp.float32)


def local_call(kernel, operands, outs, scratch):
    spec = pltpu.PrefetchScalarGridSpec(
        num_scalar_prefetch=2,
        grid=(1,),
        in_specs=[resident() for x in operands[2:]],
        out_specs=[resident() for o in outs],
        scratch_shapes=scratch,
    )
    return pl.pallas_call(
        kernel, grid_spec=spec, out_shape=outs,
        compiler_params=pltpu.CompilerParams(vmem_limit_bytes=VMEM_LIMIT),
    )(*operands)


def row_pass(blocks, counts, src, tgt, tnorm, tpot):
    rows = src.shape[1]
    slots = blocks.shape[1]
    return local_call(
        row_kernel, (blocks, counts, src, tgt, tnorm, tpot),
        [jax.ShapeDtypeStruct((1, rows), jnp.float32)],
        [pltpu.VMEM((slots, BLOCK, BLOCK), jnp.float32), column_scratch(), column_scratch(),
         pltpu.VMEM((BLOCK, 128), jnp.float32)],
    )


def column_pass(blocks, counts, src, spot, tgt_ones, tnorm):
    return local_call(
        column_kernel, (blocks, counts, src, spot, tgt_ones, tnorm),
        [jax.ShapeDtypeStruct(tnorm.shape, jnp.float32)],
        [pltpu.VMEM(tnorm.shape, jnp.float32), pltpu.VMEM(tnorm.shape, jnp.float32),
         pltpu.VMEM((src.shape[0] + EXTRA, BLOCK), jnp.bfloat16)],
    )


def project_pass(blocks, counts, src, tgt, tnorm, tpot, feat):
    rows = src.shape[1]
    slots = blocks.shape[1]
    return local_call(
        project_kernel, (blocks, counts, src, tgt, tnorm, tpot, feat),
        [jax.ShapeDtypeStruct((1, rows), jnp.float32),
         jax.ShapeDtypeStruct((rows, feat.shape[0]), jnp.float32),
         jax.ShapeDtypeStruct((1, rows), jnp.float32)],
        [pltpu.VMEM((slots, BLOCK, BLOCK), jnp.float32),
         pltpu.VMEM((slots, BLOCK, BLOCK), jnp.bfloat16),
         column_scratch(), column_scratch(), pltpu.VMEM((BLOCK, 128), jnp.float32)],
    )


def shards(src_emb, tgt_emb, target_features, src_mass, tgt_mass, kept_blocks, kept_count):
    src_rows = src_emb.shape[1]
    tgt_rows = tgt_emb.shape[1]
    src_t = src_emb
    tnorm = jnp.sum(jnp.square(tgt_emb.astype(jnp.float32)), axis=0).reshape(1, tgt_rows)
    counts = kept_count.reshape(-1)
    tgt_ones = jnp.concatenate(
        [tgt_emb, split_rows(jnp.zeros((1, tgt_rows), jnp.float32), True)], axis=0
    )

    tgt_potential = jnp.zeros((tgt_rows,), jnp.float32)
    src_potential = jnp.zeros((src_rows,), jnp.float32)
    for iteration in range(ITERS):
        tpot = tgt_potential.reshape(1, tgt_rows)
        (row_lse,) = row_pass(kept_blocks, counts, src_t, tgt_emb, tnorm, tpot)
        row_lse = butterfly_lse(row_lse.reshape(src_rows), "tgt")
        src_potential = EPSILON * jnp.log(src_mass) - EPSILON * row_lse
        (column_lse,) = column_pass(
            kept_blocks, counts, src_t, src_potential.reshape(1, src_rows), tgt_ones, tnorm
        )
        column_lse = butterfly_lse(column_lse.reshape(tgt_rows), "src")
        tgt_potential = EPSILON * jnp.log(tgt_mass) - EPSILON * column_lse

    tpot = tgt_potential.reshape(1, tgt_rows)
    local_top, numerator, denominator = project_pass(
        kept_blocks, counts, src_t, tgt_emb, tnorm, tpot, target_features
    )
    numerator, denominator = halving_merge(
        local_top.reshape(src_rows), numerator, denominator.reshape(src_rows), "tgt"
    )
    projected = numerator / denominator[:, None]
    return (projected, src_potential, tgt_potential)


def solution(mesh):
    return jax.shard_map(
        shards,
        mesh=mesh,
        in_specs=(
            P(None, "src"),
            P(None, "tgt"),
            P(None, "tgt"),
            P("src"),
            P("tgt"),
            P("src", "tgt"),
            P("src", "tgt"),
        ),
        out_specs=(P(("src", "tgt"), None), P("src"), P("tgt")),
        check_vma=False,
    )
```

```python
import functools
import math

import jax
import jax.numpy as jnp
from jax import lax
from jax.experimental import pallas as pl
from jax.experimental.pallas import tpu as pltpu
from jax.sharding import PartitionSpec as P

BLOCK = 256
ITERS = 2


SENTINEL = -1e30
EPSILON = 0.1
SCALE = 1.0 / EPSILON
BASE2 = SCALE / math.log(2.0)


def lse_pair(value, other):
    overall = jnp.maximum(value, other)
    return overall + jnp.log(jnp.exp(value - overall) + jnp.exp(other - overall))


def butterfly_lse(value, axis):
    size = lax.axis_size(axis)
    step = 1
    while step < size:
        pairs = [(i, i ^ step) for i in range(size)]
        value = lse_pair(value, lax.ppermute(value, axis, pairs))
        step *= 2
    return value


def halving_merge(small, numerator, axis):
    size = lax.axis_size(axis)
    me = lax.axis_index(axis)
    rows = small.shape[1] // size
    small = small.reshape(2, size, rows)
    numerator = numerator.reshape(size, rows, numerator.shape[-1])
    step = 1
    while step < size:
        pairs = [(i, i ^ step) for i in range(size)]
        keep = (me // step) % 2
        count = numerator.shape[0] // 2

        def split(x, axis_at):
            x = x.reshape(x.shape[:axis_at] + (count, 2) + x.shape[axis_at + 1:])
            return (
                lax.dynamic_index_in_dim(x, keep, axis=axis_at + 1, keepdims=False),
                lax.dynamic_index_in_dim(x, 1 - keep, axis=axis_at + 1, keepdims=False),
            )

        small_keep, small_send = split(small, 1)
        num_keep, num_send = split(numerator, 0)
        small_other = lax.ppermute(small_send, axis, pairs)
        num_other = lax.ppermute(num_send, axis, pairs)
        overall = jnp.maximum(small_keep[0], small_other[0])
        mine = jnp.exp(small_keep[0] - overall)
        theirs = jnp.exp(small_other[0] - overall)
        numerator = num_keep * mine[..., None] + num_other * theirs[..., None]
        small = jnp.stack([overall, small_keep[1] * mine + small_other[1] * theirs])
        step *= 2
    return (numerator.reshape(rows, -1), small[1].reshape(rows))


CHUNK = 64
EXTRA = 16
VMEM_LIMIT = 24 * 1024 * 1024


def tile_slice(ref, b):
    return ref[:, pl.ds(pl.multiple_of(b * BLOCK, BLOCK), BLOCK)]


def row_slice(ref, r):
    return ref[pl.ds(pl.multiple_of(r * BLOCK, BLOCK), BLOCK), :]


def doubled_source(src_ref, r):
    exact = tile_slice(src_ref, r).astype(jnp.float32)
    return (exact * 2.0).astype(jnp.bfloat16), jnp.sum(exact * exact, axis=0, keepdims=True)


def products(doubled, tgt_ref, b):
    return lax.dot_general(doubled, tile_slice(tgt_ref, b), (((0,), (0,)), ((), ())),
                           preferred_element_type=jnp.float32)


def as_row(column, scratch):
    scratch[...] = jnp.broadcast_to(column, scratch.shape)
    return jnp.transpose(scratch[...])[0:1, :]


def as_column(row, scratch):
    scratch[...] = jnp.broadcast_to(row, scratch.shape)
    return jnp.transpose(scratch[...])[:, 0:1]


def by_count(live, slots, body):
    for count in range(1, slots + 1):
        pl.when(live == count)(functools.partial(body, count))


def over_rows(rows, body):
    lax.fori_loop(0, rows, lambda r, c: (body(r), c)[1], 0)


def fill_shifted(blocks_ref, r, count, doubled, tgt_ref, tnorm_ref, tpot_ref, held):
    for k in range(count):
        b = blocks_ref[r, k]
        shift = tile_slice(tpot_ref, b) - tile_slice(tnorm_ref, b)
        held[k] = products(doubled, tgt_ref, b) + shift


def chunk_peak(held, count, rows):
    peak = held[0, rows, :]
    for k in range(1, count):
        peak = jnp.maximum(peak, held[k, rows, :])
    return jnp.max(peak, axis=1, keepdims=True)


def row_kernel(blocks_ref, count_ref, src_ref, tgt_ref, tnorm_ref, tpot_ref,
               lse_ref, held, high_col, total_col, wide):
    def per_row(r):
        doubled, snorm = doubled_source(src_ref, r)

        def body(count):
            fill_shifted(blocks_ref, r, count, doubled, tgt_ref, tnorm_ref, tpot_ref, held)
            for chunk in range(BLOCK // CHUNK):
                rows = pl.ds(chunk * CHUNK, CHUNK)
                peak = chunk_peak(held, count, rows)
                acc = jnp.exp2((held[0, rows, :] - peak) * BASE2)
                for k in range(1, count):
                    acc = acc + jnp.exp2((held[k, rows, :] - peak) * BASE2)
                high_col[rows, :] = peak
                total_col[rows, :] = jnp.sum(acc, axis=1, keepdims=True)

        by_count(count_ref[r], held.shape[0], body)
        lanes = pl.ds(pl.multiple_of(r * BLOCK, BLOCK), BLOCK)
        lse_ref[:, lanes] = ((as_row(high_col[...], wide) - snorm) * SCALE
                             + jnp.log(as_row(total_col[...], wide)))

    over_rows(count_ref.shape[0], per_row)


def split_rows(row, ones):
    high = row.astype(jnp.bfloat16).astype(jnp.float32)
    middle = (row - high).astype(jnp.bfloat16).astype(jnp.float32)
    low = row - high - middle
    index = lax.broadcasted_iota(jnp.int32, (EXTRA, row.shape[1]), 0)
    if ones:
        rows = jnp.where(index < 3, 1.0, 0.0)
    else:
        rows = jnp.where(index == 0, high, jnp.where(index == 1, middle,
                                                     jnp.where(index == 2, low, 0.0)))
    return rows.astype(jnp.bfloat16)


def column_kernel(blocks_ref, count_ref, src_ref, spot_ref, tgt_ref, tnorm_ref,
                  lse_ref, top_ref, sum_ref, lhs):
    top_ref[...] = jnp.full(top_ref.shape, SENTINEL, jnp.float32)
    sum_ref[...] = jnp.zeros(sum_ref.shape, jnp.float32)
    width = src_ref.shape[0]

    def per_row(r):
        doubled, snorm = doubled_source(src_ref, r)
        lhs[0:width, :] = doubled
        lhs[width:, :] = split_rows(tile_slice(spot_ref, r) - snorm, False)
        augmented = lhs[...]

        def body(count):
            for k in range(count):
                b = blocks_ref[r, k]
                lanes = pl.ds(pl.multiple_of(b * BLOCK, BLOCK), BLOCK)
                shifted = products(augmented, tgt_ref, b)
                peak = jnp.max(shifted, axis=0, keepdims=True)
                totals = jnp.sum(jnp.exp2((shifted - peak) * BASE2), axis=0, keepdims=True)
                highest = (peak - tnorm_ref[:, lanes]) * SCALE
                old_top = top_ref[:, lanes]
                new_top = jnp.maximum(old_top, highest)
                sum_ref[:, lanes] = (sum_ref[:, lanes] * jnp.exp(old_top - new_top)
                                     + totals * jnp.exp(highest - new_top))
                top_ref[:, lanes] = new_top

        by_count(count_ref[r], blocks_ref.shape[1], body)

    over_rows(count_ref.shape[0], per_row)
    totals = sum_ref[...]
    lse_ref[...] = jnp.where(totals > 0.0, top_ref[...] + jnp.log(totals), SENTINEL)


def project_kernel(blocks_ref, count_ref, src_ref, tgt_ref, tnorm_ref, tpot_ref, feat_ref,
                   small_ref, num_ref, held, weights, high_col, den_col, wide):
    def per_row(r):
        doubled, snorm = doubled_source(src_ref, r)

        def body(count):
            fill_shifted(blocks_ref, r, count, doubled, tgt_ref, tnorm_ref, tpot_ref, held)
            for chunk in range(BLOCK // CHUNK):
                rows = pl.ds(chunk * CHUNK, CHUNK)
                peak = chunk_peak(held, count, rows)
                acc = jnp.zeros((CHUNK, BLOCK), jnp.float32)
                for k in range(count):
                    rounded = jnp.exp2((held[k, rows, :] - peak) * BASE2).astype(jnp.bfloat16)
                    weights[k, rows, :] = rounded
                    acc = acc + rounded.astype(jnp.float32)
                high_col[rows, :] = peak
                den_col[rows, :] = jnp.sum(acc, axis=1, keepdims=True)
            total = None
            for k in range(count):
                part = lax.dot_general(weights[k], tile_slice(feat_ref, blocks_ref[r, k]),
                                       (((1,), (1,)), ((), ())),
                                       preferred_element_type=jnp.float32)
                total = part if total is None else total + part
            num_ref[pl.ds(pl.multiple_of(r * BLOCK, BLOCK), BLOCK), :] = total

        by_count(count_ref[r], held.shape[0], body)
        lanes = pl.ds(pl.multiple_of(r * BLOCK, BLOCK), BLOCK)
        small_ref[0:1, lanes] = (as_row(high_col[...], wide) - snorm) * SCALE
        small_ref[1:2, lanes] = as_row(den_col[...], wide)

    over_rows(count_ref.shape[0], per_row)


def whole(shape):
    return pl.BlockSpec(shape, lambda r, *_: (0,) * len(shape))


def resident():
    return pl.BlockSpec(memory_space=pltpu.VMEM)


def column_scratch():
    return pltpu.VMEM((BLOCK, 1), jnp.float32)


def local_call(kernel, operands, outs, scratch):
    spec = pltpu.PrefetchScalarGridSpec(
        num_scalar_prefetch=2,
        grid=(1,),
        in_specs=[resident() for x in operands[2:]],
        out_specs=[resident() for o in outs],
        scratch_shapes=scratch,
    )
    return pl.pallas_call(
        kernel, grid_spec=spec, out_shape=outs,
        compiler_params=pltpu.CompilerParams(vmem_limit_bytes=VMEM_LIMIT),
    )(*operands)


def row_pass(blocks, counts, src, tgt, tnorm, tpot):
    rows = src.shape[1]
    slots = blocks.shape[1]
    return local_call(
        row_kernel, (blocks, counts, src, tgt, tnorm, tpot),
        [jax.ShapeDtypeStruct((1, rows), jnp.float32)],
        [pltpu.VMEM((slots, BLOCK, BLOCK), jnp.float32), column_scratch(), column_scratch(),
         pltpu.VMEM((BLOCK, 128), jnp.float32)],
    )


def column_pass(blocks, counts, src, spot, tgt_ones, tnorm):
    return local_call(
        column_kernel, (blocks, counts, src, spot, tgt_ones, tnorm),
        [jax.ShapeDtypeStruct(tnorm.shape, jnp.float32)],
        [pltpu.VMEM(tnorm.shape, jnp.float32), pltpu.VMEM(tnorm.shape, jnp.float32),
         pltpu.VMEM((src.shape[0] + EXTRA, BLOCK), jnp.bfloat16)],
    )


def project_pass(blocks, counts, src, tgt, tnorm, tpot, feat):
    rows = src.shape[1]
    slots = blocks.shape[1]
    return local_call(
        project_kernel, (blocks, counts, src, tgt, tnorm, tpot, feat),
        [jax.ShapeDtypeStruct((2, rows), jnp.float32),
         jax.ShapeDtypeStruct((rows, feat.shape[0]), jnp.float32)],
        [pltpu.VMEM((slots, BLOCK, BLOCK), jnp.float32),
         pltpu.VMEM((slots, BLOCK, BLOCK), jnp.bfloat16),
         column_scratch(), column_scratch(), pltpu.VMEM((BLOCK, 128), jnp.float32)],
    )


def shards(src_emb, tgt_emb, target_features, src_mass, tgt_mass, kept_blocks, kept_count):
    src_rows = src_emb.shape[1]
    tgt_rows = tgt_emb.shape[1]
    src_t = src_emb
    tnorm = jnp.sum(jnp.square(tgt_emb.astype(jnp.float32)), axis=0).reshape(1, tgt_rows)
    counts = kept_count.reshape(-1)
    tgt_ones = jnp.concatenate(
        [tgt_emb, split_rows(jnp.zeros((1, tgt_rows), jnp.float32), True)], axis=0
    )

    tgt_potential = jnp.zeros((tgt_rows,), jnp.float32)
    src_potential = jnp.zeros((src_rows,), jnp.float32)
    for iteration in range(ITERS):
        tpot = tgt_potential.reshape(1, tgt_rows)
        (row_lse,) = row_pass(kept_blocks, counts, src_t, tgt_emb, tnorm, tpot)
        row_lse = butterfly_lse(row_lse.reshape(src_rows), "tgt")
        src_potential = EPSILON * jnp.log(src_mass) - EPSILON * row_lse
        (column_lse,) = column_pass(
            kept_blocks, counts, src_t, src_potential.reshape(1, src_rows), tgt_ones, tnorm
        )
        column_lse = butterfly_lse(column_lse.reshape(tgt_rows), "src")
        tgt_potential = EPSILON * jnp.log(tgt_mass) - EPSILON * column_lse

    tpot = tgt_potential.reshape(1, tgt_rows)
    small, numerator = project_pass(
        kept_blocks, counts, src_t, tgt_emb, tnorm, tpot, target_features
    )
    numerator, denominator = halving_merge(small, numerator, "tgt")
    projected = numerator / denominator[:, None]
    return (projected, src_potential, tgt_potential)


def solution(mesh):
    return jax.shard_map(
        shards,
        mesh=mesh,
        in_specs=(
            P(None, "src"),
            P(None, "tgt"),
            P(None, "tgt"),
            P("src"),
            P("tgt"),
            P("src", "tgt"),
            P("src", "tgt"),
        ),
        out_specs=(P(("src", "tgt"), None), P("src"), P("tgt")),
        check_vma=False,
    )
```

```python
import functools
import math

import jax
import jax.numpy as jnp
from jax import lax
from jax.experimental import pallas as pl
from jax.experimental.pallas import tpu as pltpu
from jax.sharding import PartitionSpec as P

BLOCK = 256
ITERS = 2


SENTINEL = -1e30
EPSILON = 0.1
SCALE = 1.0 / EPSILON
BASE2 = SCALE / math.log(2.0)


def lse_pair(value, other):
    overall = jnp.maximum(value, other)
    return overall + jnp.log(jnp.exp(value - overall) + jnp.exp(other - overall))


def butterfly_lse(value, axis):
    size = lax.axis_size(axis)
    step = 1
    while step < size:
        pairs = [(i, i ^ step) for i in range(size)]
        value = lse_pair(value, lax.ppermute(value, axis, pairs))
        step *= 2
    return value


def halving_merge(small, numerator, axis):
    size = lax.axis_size(axis)
    me = lax.axis_index(axis)
    rows = small.shape[1] // size
    small = small.reshape(2, size, rows)
    numerator = numerator.reshape(size, rows, numerator.shape[-1])
    step = 1
    while step < size:
        pairs = [(i, i ^ step) for i in range(size)]
        keep = (me // step) % 2
        count = numerator.shape[0] // 2

        def split(x, axis_at):
            x = x.reshape(x.shape[:axis_at] + (count, 2) + x.shape[axis_at + 1:])
            return (
                lax.dynamic_index_in_dim(x, keep, axis=axis_at + 1, keepdims=False),
                lax.dynamic_index_in_dim(x, 1 - keep, axis=axis_at + 1, keepdims=False),
            )

        small_keep, small_send = split(small, 1)
        num_keep, num_send = split(numerator, 0)
        small_other = lax.ppermute(small_send, axis, pairs)
        num_other = lax.ppermute(num_send, axis, pairs)
        overall = jnp.maximum(small_keep[0], small_other[0])
        mine = jnp.exp(small_keep[0] - overall)
        theirs = jnp.exp(small_other[0] - overall)
        numerator = num_keep * mine[..., None] + num_other * theirs[..., None]
        small = jnp.stack([overall, small_keep[1] * mine + small_other[1] * theirs])
        step *= 2
    return (numerator.reshape(rows, -1), small[1].reshape(rows))


CHUNK = 64
EXTRA = 16
VMEM_LIMIT = 24 * 1024 * 1024


def tile_slice(ref, b):
    return ref[:, pl.ds(pl.multiple_of(b * BLOCK, BLOCK), BLOCK)]


def row_slice(ref, r):
    return ref[pl.ds(pl.multiple_of(r * BLOCK, BLOCK), BLOCK), :]


def doubled_source(src_ref, r):
    exact = tile_slice(src_ref, r).astype(jnp.float32)
    return (exact * 2.0).astype(jnp.bfloat16), jnp.sum(exact * exact, axis=0, keepdims=True)


def products(doubled, tgt_ref, b):
    return lax.dot_general(doubled, tile_slice(tgt_ref, b), (((0,), (0,)), ((), ())),
                           preferred_element_type=jnp.float32)


def as_row(column, scratch):
    scratch[...] = jnp.broadcast_to(column, scratch.shape)
    return jnp.transpose(scratch[...])[0:1, :]


def as_column(row, scratch):
    scratch[...] = jnp.broadcast_to(row, scratch.shape)
    return jnp.transpose(scratch[...])[:, 0:1]


def by_count(live, slots, body):
    for count in range(1, slots + 1):
        pl.when(live == count)(functools.partial(body, count))


def over_rows(rows, body):
    lax.fori_loop(0, rows, lambda r, c: (body(r), c)[1], 0)


def fill_shifted(blocks_ref, r, count, doubled, tgt_ref, tnorm_ref, tpot_ref, held):
    for k in range(count):
        b = blocks_ref[r, k]
        shift = tile_slice(tpot_ref, b) - tile_slice(tnorm_ref, b)
        held[k] = products(doubled, tgt_ref, b) + shift


def chunk_peak(held, count, rows):
    peak = held[0, rows, :]
    for k in range(1, count):
        peak = jnp.maximum(peak, held[k, rows, :])
    return jnp.max(peak, axis=1, keepdims=True)


def row_kernel(blocks_ref, count_ref, src_ref, tgt_ref, tnorm_ref, tpot_ref,
               lse_ref, held, tgt_aug, rhs, peak_row, total_row):
    width = tgt_ref.shape[0]
    tgt_aug[0:width, :] = tgt_ref[...]
    tgt_aug[width:, :] = split_rows(tpot_ref[...] - tnorm_ref[...], False)

    def per_row(r):
        doubled, snorm = doubled_source(src_ref, r)
        rhs[0:width, :] = doubled
        rhs[width:, :] = split_rows(snorm, True)
        augmented = rhs[...]

        def body(count):
            for k in range(count):
                held[k] = lax.dot_general(tile_slice(tgt_aug, blocks_ref[r, k]), augmented,
                                          (((0,), (0,)), ((), ())),
                                          preferred_element_type=jnp.float32)
            folded = None
            for chunk in range(BLOCK // CHUNK):
                rows = pl.ds(chunk * CHUNK, CHUNK)
                peak = held[0, rows, :]
                for k in range(1, count):
                    peak = jnp.maximum(peak, held[k, rows, :])
                peak = jnp.max(peak.reshape(CHUNK // 8, 8, BLOCK), axis=0)
                folded = peak if folded is None else jnp.maximum(folded, peak)
            peak = jnp.max(folded, axis=0, keepdims=True)
            folded = None
            for chunk in range(BLOCK // CHUNK):
                rows = pl.ds(chunk * CHUNK, CHUNK)
                acc = jnp.exp2((held[0, rows, :] - peak) * BASE2)
                for k in range(1, count):
                    acc = acc + jnp.exp2((held[k, rows, :] - peak) * BASE2)
                acc = jnp.sum(acc.reshape(CHUNK // 8, 8, BLOCK), axis=0)
                folded = acc if folded is None else folded + acc
            peak_row[...] = peak
            total_row[...] = jnp.sum(folded, axis=0, keepdims=True)

        by_count(count_ref[r], held.shape[0], body)
        lanes = pl.ds(pl.multiple_of(r * BLOCK, BLOCK), BLOCK)
        lse_ref[:, lanes] = (peak_row[...] - snorm) * SCALE + jnp.log(total_row[...])

    over_rows(count_ref.shape[0], per_row)


def split_rows(row, ones):
    high = row.astype(jnp.bfloat16).astype(jnp.float32)
    middle = (row - high).astype(jnp.bfloat16).astype(jnp.float32)
    low = row - high - middle
    index = lax.broadcasted_iota(jnp.int32, (EXTRA, row.shape[1]), 0)
    if ones:
        rows = jnp.where(index < 3, 1.0, 0.0)
    else:
        rows = jnp.where(index == 0, high, jnp.where(index == 1, middle,
                                                     jnp.where(index == 2, low, 0.0)))
    return rows.astype(jnp.bfloat16)


def column_kernel(blocks_ref, count_ref, src_ref, spot_ref, tgt_ref, tnorm_ref,
                  lse_ref, top_ref, sum_ref, lhs):
    top_ref[...] = jnp.full(top_ref.shape, SENTINEL, jnp.float32)
    sum_ref[...] = jnp.zeros(sum_ref.shape, jnp.float32)
    width = src_ref.shape[0]

    def per_row(r):
        doubled, snorm = doubled_source(src_ref, r)
        lhs[0:width, :] = doubled
        lhs[width:, :] = split_rows(tile_slice(spot_ref, r) - snorm, False)
        augmented = lhs[...]

        def body(count):
            for k in range(count):
                b = blocks_ref[r, k]
                lanes = pl.ds(pl.multiple_of(b * BLOCK, BLOCK), BLOCK)
                shifted = products(augmented, tgt_ref, b)
                peak = jnp.max(shifted, axis=0, keepdims=True)
                totals = jnp.sum(jnp.exp2((shifted - peak) * BASE2), axis=0, keepdims=True)
                highest = (peak - tnorm_ref[:, lanes]) * SCALE
                old_top = top_ref[:, lanes]
                new_top = jnp.maximum(old_top, highest)
                sum_ref[:, lanes] = (sum_ref[:, lanes] * jnp.exp(old_top - new_top)
                                     + totals * jnp.exp(highest - new_top))
                top_ref[:, lanes] = new_top

        by_count(count_ref[r], blocks_ref.shape[1], body)

    over_rows(count_ref.shape[0], per_row)
    totals = sum_ref[...]
    lse_ref[...] = jnp.where(totals > 0.0, top_ref[...] + jnp.log(totals), SENTINEL)


def project_kernel(blocks_ref, count_ref, src_ref, tgt_ref, tnorm_ref, tpot_ref, feat_ref,
                   small_ref, num_ref, held, weights, high_col, den_col, wide):
    def per_row(r):
        doubled, snorm = doubled_source(src_ref, r)

        def body(count):
            fill_shifted(blocks_ref, r, count, doubled, tgt_ref, tnorm_ref, tpot_ref, held)
            for chunk in range(BLOCK // CHUNK):
                rows = pl.ds(chunk * CHUNK, CHUNK)
                peak = chunk_peak(held, count, rows)
                acc = jnp.zeros((CHUNK, BLOCK), jnp.float32)
                for k in range(count):
                    rounded = jnp.exp2((held[k, rows, :] - peak) * BASE2).astype(jnp.bfloat16)
                    weights[k, rows, :] = rounded
                    acc = acc + rounded.astype(jnp.float32)
                high_col[rows, :] = peak
                den_col[rows, :] = jnp.sum(acc, axis=1, keepdims=True)
            total = None
            for k in range(count):
                part = lax.dot_general(weights[k], tile_slice(feat_ref, blocks_ref[r, k]),
                                       (((1,), (1,)), ((), ())),
                                       preferred_element_type=jnp.float32)
                total = part if total is None else total + part
            num_ref[pl.ds(pl.multiple_of(r * BLOCK, BLOCK), BLOCK), :] = total

        by_count(count_ref[r], held.shape[0], body)
        lanes = pl.ds(pl.multiple_of(r * BLOCK, BLOCK), BLOCK)
        small_ref[0:1, lanes] = (as_row(high_col[...], wide) - snorm) * SCALE
        small_ref[1:2, lanes] = as_row(den_col[...], wide)

    over_rows(count_ref.shape[0], per_row)


def whole(shape):
    return pl.BlockSpec(shape, lambda r, *_: (0,) * len(shape))


def resident():
    return pl.BlockSpec(memory_space=pltpu.VMEM)


def column_scratch():
    return pltpu.VMEM((BLOCK, 1), jnp.float32)


def local_call(kernel, operands, outs, scratch):
    spec = pltpu.PrefetchScalarGridSpec(
        num_scalar_prefetch=2,
        grid=(1,),
        in_specs=[resident() for x in operands[2:]],
        out_specs=[resident() for o in outs],
        scratch_shapes=scratch,
    )
    return pl.pallas_call(
        kernel, grid_spec=spec, out_shape=outs,
        compiler_params=pltpu.CompilerParams(vmem_limit_bytes=VMEM_LIMIT),
    )(*operands)


def row_pass(blocks, counts, src, tgt, tnorm, tpot):
    slots = blocks.shape[1]
    return local_call(
        row_kernel, (blocks, counts, src, tgt, tnorm, tpot),
        [jax.ShapeDtypeStruct((1, src.shape[1]), jnp.float32)],
        [pltpu.VMEM((slots, BLOCK, BLOCK), jnp.float32),
         pltpu.VMEM((tgt.shape[0] + EXTRA, tgt.shape[1]), jnp.bfloat16),
         pltpu.VMEM((src.shape[0] + EXTRA, BLOCK), jnp.bfloat16),
         pltpu.VMEM((1, BLOCK), jnp.float32), pltpu.VMEM((1, BLOCK), jnp.float32)],
    )


def column_pass(blocks, counts, src, spot, tgt_ones, tnorm):
    return local_call(
        column_kernel, (blocks, counts, src, spot, tgt_ones, tnorm),
        [jax.ShapeDtypeStruct(tnorm.shape, jnp.float32)],
        [pltpu.VMEM(tnorm.shape, jnp.float32), pltpu.VMEM(tnorm.shape, jnp.float32),
         pltpu.VMEM((src.shape[0] + EXTRA, BLOCK), jnp.bfloat16)],
    )


def project_pass(blocks, counts, src, tgt, tnorm, tpot, feat):
    rows = src.shape[1]
    slots = blocks.shape[1]
    return local_call(
        project_kernel, (blocks, counts, src, tgt, tnorm, tpot, feat),
        [jax.ShapeDtypeStruct((2, rows), jnp.float32),
         jax.ShapeDtypeStruct((rows, feat.shape[0]), jnp.float32)],
        [pltpu.VMEM((slots, BLOCK, BLOCK), jnp.float32),
         pltpu.VMEM((slots, BLOCK, BLOCK), jnp.bfloat16),
         column_scratch(), column_scratch(), pltpu.VMEM((BLOCK, 128), jnp.float32)],
    )


def shards(src_emb, tgt_emb, target_features, src_mass, tgt_mass, kept_blocks, kept_count):
    src_rows = src_emb.shape[1]
    tgt_rows = tgt_emb.shape[1]
    src_t = src_emb
    tnorm = jnp.sum(jnp.square(tgt_emb.astype(jnp.float32)), axis=0).reshape(1, tgt_rows)
    counts = kept_count.reshape(-1)
    tgt_ones = jnp.concatenate(
        [tgt_emb, split_rows(jnp.zeros((1, tgt_rows), jnp.float32), True)], axis=0
    )

    tgt_potential = jnp.zeros((tgt_rows,), jnp.float32)
    src_potential = jnp.zeros((src_rows,), jnp.float32)
    for iteration in range(ITERS):
        tpot = tgt_potential.reshape(1, tgt_rows)
        (row_lse,) = row_pass(kept_blocks, counts, src_t, tgt_emb, tnorm, tpot)
        row_lse = butterfly_lse(row_lse.reshape(src_rows), "tgt")
        src_potential = EPSILON * jnp.log(src_mass) - EPSILON * row_lse
        (column_lse,) = column_pass(
            kept_blocks, counts, src_t, src_potential.reshape(1, src_rows), tgt_ones, tnorm
        )
        column_lse = butterfly_lse(column_lse.reshape(tgt_rows), "src")
        tgt_potential = EPSILON * jnp.log(tgt_mass) - EPSILON * column_lse

    tpot = tgt_potential.reshape(1, tgt_rows)
    small, numerator = project_pass(
        kept_blocks, counts, src_t, tgt_emb, tnorm, tpot, target_features
    )
    numerator, denominator = halving_merge(small, numerator, "tgt")
    projected = numerator / denominator[:, None]
    return (projected, src_potential, tgt_potential)


def solution(mesh):
    return jax.shard_map(
        shards,
        mesh=mesh,
        in_specs=(
            P(None, "src"),
            P(None, "tgt"),
            P(None, "tgt"),
            P("src"),
            P("tgt"),
            P("src", "tgt"),
            P("src", "tgt"),
        ),
        out_specs=(P(("src", "tgt"), None), P("src"), P("tgt")),
        check_vma=False,
    )
```

```python
import functools
import math

import jax
import jax.numpy as jnp
from jax import lax
from jax.experimental import pallas as pl
from jax.experimental.pallas import tpu as pltpu
from jax.sharding import PartitionSpec as P

BLOCK = 256
ITERS = 2


SENTINEL = -1e30
EPSILON = 0.1
SCALE = 1.0 / EPSILON
BASE2 = SCALE / math.log(2.0)


def lse_pair(value, other):
    overall = jnp.maximum(value, other)
    return overall + jnp.log(jnp.exp(value - overall) + jnp.exp(other - overall))


def butterfly_lse(value, axis):
    size = lax.axis_size(axis)
    step = 1
    while step < size:
        pairs = [(i, i ^ step) for i in range(size)]
        value = lse_pair(value, lax.ppermute(value, axis, pairs))
        step *= 2
    return value


def halving_merge(small, numerator, axis):
    size = lax.axis_size(axis)
    me = lax.axis_index(axis)
    rows = small.shape[1] // size
    small = small.reshape(2, size, rows)
    numerator = numerator.reshape(size, rows, numerator.shape[-1])
    step = 1
    while step < size:
        pairs = [(i, i ^ step) for i in range(size)]
        keep = (me // step) % 2
        count = numerator.shape[0] // 2

        def split(x, axis_at):
            x = x.reshape(x.shape[:axis_at] + (count, 2) + x.shape[axis_at + 1:])
            return (
                lax.dynamic_index_in_dim(x, keep, axis=axis_at + 1, keepdims=False),
                lax.dynamic_index_in_dim(x, 1 - keep, axis=axis_at + 1, keepdims=False),
            )

        small_keep, small_send = split(small, 1)
        num_keep, num_send = split(numerator, 0)
        small_other = lax.ppermute(small_send, axis, pairs)
        num_other = lax.ppermute(num_send, axis, pairs)
        overall = jnp.maximum(small_keep[0], small_other[0])
        mine = jnp.exp(small_keep[0] - overall)
        theirs = jnp.exp(small_other[0] - overall)
        numerator = num_keep * mine[..., None] + num_other * theirs[..., None]
        small = jnp.stack([overall, small_keep[1] * mine + small_other[1] * theirs])
        step *= 2
    return (numerator.reshape(rows, -1), small[1].reshape(rows))


CHUNK = 64
EXTRA = 16
VMEM_LIMIT = 24 * 1024 * 1024


def tile_slice(ref, b):
    return ref[:, pl.ds(pl.multiple_of(b * BLOCK, BLOCK), BLOCK)]


def row_slice(ref, r):
    return ref[pl.ds(pl.multiple_of(r * BLOCK, BLOCK), BLOCK), :]


def doubled_source(src_ref, r):
    exact = tile_slice(src_ref, r).astype(jnp.float32)
    return (exact * 2.0).astype(jnp.bfloat16), jnp.sum(exact * exact, axis=0, keepdims=True)


def products(doubled, tgt_ref, b):
    return lax.dot_general(doubled, tile_slice(tgt_ref, b), (((0,), (0,)), ((), ())),
                           preferred_element_type=jnp.float32)


def as_row(column, scratch):
    scratch[...] = jnp.broadcast_to(column, scratch.shape)
    return jnp.transpose(scratch[...])[0:1, :]


def as_column(row, scratch):
    scratch[...] = jnp.broadcast_to(row, scratch.shape)
    return jnp.transpose(scratch[...])[:, 0:1]


def by_count(live, slots, body):
    for count in range(1, slots + 1):
        pl.when(live == count)(functools.partial(body, count))


def over_rows(rows, body):
    lax.fori_loop(0, rows, lambda r, c: (body(r), c)[1], 0)


def fill_shifted(blocks_ref, r, count, doubled, tgt_ref, tnorm_ref, tpot_ref, held):
    for k in range(count):
        b = blocks_ref[r, k]
        shift = tile_slice(tpot_ref, b) - tile_slice(tnorm_ref, b)
        held[k] = products(doubled, tgt_ref, b) + shift


def chunk_peak(held, count, rows):
    peak = held[0, rows, :]
    for k in range(1, count):
        peak = jnp.maximum(peak, held[k, rows, :])
    return jnp.max(peak, axis=1, keepdims=True)


def row_kernel(blocks_ref, count_ref, src_ref, tgt_ref, tnorm_ref, tpot_ref,
               lse_ref, held, tgt_aug, rhs, peak_row, total_row):
    width = tgt_ref.shape[0]
    tgt_aug[0:width, :] = tgt_ref[...]
    tgt_aug[width:, :] = split_rows(tpot_ref[...] - tnorm_ref[...], False)

    def per_row(r):
        doubled, snorm = doubled_source(src_ref, r)
        rhs[0:width, :] = doubled
        rhs[width:, :] = split_rows(snorm, True)
        augmented = rhs[...]

        def body(count):
            for k in range(count):
                held[k] = lax.dot_general(tile_slice(tgt_aug, blocks_ref[r, k]), augmented,
                                          (((0,), (0,)), ((), ())),
                                          preferred_element_type=jnp.float32)
            folded = None
            for chunk in range(BLOCK // CHUNK):
                rows = pl.ds(chunk * CHUNK, CHUNK)
                peak = held[0, rows, :]
                for k in range(1, count):
                    peak = jnp.maximum(peak, held[k, rows, :])
                peak = jnp.max(peak.reshape(CHUNK // 8, 8, BLOCK), axis=0)
                folded = peak if folded is None else jnp.maximum(folded, peak)
            peak = jnp.max(folded, axis=0, keepdims=True)
            folded = None
            for chunk in range(BLOCK // CHUNK):
                rows = pl.ds(chunk * CHUNK, CHUNK)
                acc = jnp.exp2((held[0, rows, :] - peak) * BASE2)
                for k in range(1, count):
                    acc = acc + jnp.exp2((held[k, rows, :] - peak) * BASE2)
                acc = jnp.sum(acc.reshape(CHUNK // 8, 8, BLOCK), axis=0)
                folded = acc if folded is None else folded + acc
            peak_row[...] = peak
            total_row[...] = jnp.sum(folded, axis=0, keepdims=True)

        by_count(count_ref[r], held.shape[0], body)
        lanes = pl.ds(pl.multiple_of(r * BLOCK, BLOCK), BLOCK)
        lse_ref[:, lanes] = (peak_row[...] - snorm) * SCALE + jnp.log(total_row[...])

    over_rows(count_ref.shape[0], per_row)


def split_rows(row, ones):
    high = row.astype(jnp.bfloat16).astype(jnp.float32)
    middle = (row - high).astype(jnp.bfloat16).astype(jnp.float32)
    low = row - high - middle
    index = lax.broadcasted_iota(jnp.int32, (EXTRA, row.shape[1]), 0)
    if ones:
        rows = jnp.where(index < 3, 1.0, 0.0)
    else:
        rows = jnp.where(index == 0, high, jnp.where(index == 1, middle,
                                                     jnp.where(index == 2, low, 0.0)))
    return rows.astype(jnp.bfloat16)


def column_kernel(blocks_ref, count_ref, src_ref, spot_ref, tgt_ref, tnorm_ref,
                  lse_ref, top_ref, sum_ref, lhs):
    top_ref[...] = jnp.full(top_ref.shape, SENTINEL, jnp.float32)
    sum_ref[...] = jnp.zeros(sum_ref.shape, jnp.float32)
    width = src_ref.shape[0]

    def per_row(r):
        doubled, snorm = doubled_source(src_ref, r)
        lhs[0:width, :] = doubled
        lhs[width:, :] = split_rows(tile_slice(spot_ref, r) - snorm, False)
        augmented = lhs[...]

        def body(count):
            for k in range(count):
                b = blocks_ref[r, k]
                lanes = pl.ds(pl.multiple_of(b * BLOCK, BLOCK), BLOCK)
                shifted = products(augmented, tgt_ref, b)
                peak = jnp.max(shifted, axis=0, keepdims=True)
                totals = jnp.sum(jnp.exp2((shifted - peak) * BASE2), axis=0, keepdims=True)
                highest = (peak - tnorm_ref[:, lanes]) * SCALE
                old_top = top_ref[:, lanes]
                new_top = jnp.maximum(old_top, highest)
                sum_ref[:, lanes] = (sum_ref[:, lanes] * jnp.exp(old_top - new_top)
                                     + totals * jnp.exp(highest - new_top))
                top_ref[:, lanes] = new_top

        by_count(count_ref[r], blocks_ref.shape[1], body)

    over_rows(count_ref.shape[0], per_row)
    totals = sum_ref[...]
    lse_ref[...] = jnp.where(totals > 0.0, top_ref[...] + jnp.log(totals), SENTINEL)


def project_kernel(blocks_ref, count_ref, src_ref, tgt_ref, tnorm_ref, tpot_ref, feat_ref,
                   small_ref, num_ref, held, weights, tgt_aug, rhs, peak_row, den_row):
    width = tgt_ref.shape[0]
    tgt_aug[0:width, :] = tgt_ref[...]
    tgt_aug[width:, :] = split_rows(tpot_ref[...] - tnorm_ref[...], False)

    def per_row(r):
        doubled, snorm = doubled_source(src_ref, r)
        rhs[0:width, :] = doubled
        rhs[width:, :] = split_rows(snorm, True)
        augmented = rhs[...]

        def body(count):
            for k in range(count):
                held[k] = lax.dot_general(tile_slice(tgt_aug, blocks_ref[r, k]), augmented,
                                          (((0,), (0,)), ((), ())),
                                          preferred_element_type=jnp.float32)
            folded = None
            for chunk in range(BLOCK // CHUNK):
                rows = pl.ds(chunk * CHUNK, CHUNK)
                peak = held[0, rows, :]
                for k in range(1, count):
                    peak = jnp.maximum(peak, held[k, rows, :])
                peak = jnp.max(peak.reshape(CHUNK // 8, 8, BLOCK), axis=0)
                folded = peak if folded is None else jnp.maximum(folded, peak)
            peak = jnp.max(folded, axis=0, keepdims=True)
            folded = None
            for chunk in range(BLOCK // CHUNK):
                rows = pl.ds(chunk * CHUNK, CHUNK)
                acc = jnp.zeros((CHUNK, BLOCK), jnp.float32)
                for k in range(count):
                    rounded = jnp.exp2((held[k, rows, :] - peak) * BASE2).astype(jnp.bfloat16)
                    weights[k, rows, :] = rounded
                    acc = acc + rounded.astype(jnp.float32)
                acc = jnp.sum(acc.reshape(CHUNK // 8, 8, BLOCK), axis=0)
                folded = acc if folded is None else folded + acc
            total = None
            for k in range(count):
                part = jnp.dot(tile_slice(feat_ref, blocks_ref[r, k]), weights[k],
                               preferred_element_type=jnp.float32)
                total = part if total is None else total + part
            num_ref[pl.ds(pl.multiple_of(r * BLOCK, BLOCK), BLOCK), :] = jnp.transpose(total)
            peak_row[...] = peak
            den_row[...] = jnp.sum(folded, axis=0, keepdims=True)

        by_count(count_ref[r], held.shape[0], body)
        lanes = pl.ds(pl.multiple_of(r * BLOCK, BLOCK), BLOCK)
        small_ref[0:1, lanes] = (peak_row[...] - snorm) * SCALE
        small_ref[1:2, lanes] = den_row[...]

    over_rows(count_ref.shape[0], per_row)


def whole(shape):
    return pl.BlockSpec(shape, lambda r, *_: (0,) * len(shape))


def resident():
    return pl.BlockSpec(memory_space=pltpu.VMEM)


def column_scratch():
    return pltpu.VMEM((BLOCK, 1), jnp.float32)


def local_call(kernel, operands, outs, scratch):
    spec = pltpu.PrefetchScalarGridSpec(
        num_scalar_prefetch=2,
        grid=(1,),
        in_specs=[resident() for x in operands[2:]],
        out_specs=[resident() for o in outs],
        scratch_shapes=scratch,
    )
    return pl.pallas_call(
        kernel, grid_spec=spec, out_shape=outs,
        compiler_params=pltpu.CompilerParams(vmem_limit_bytes=VMEM_LIMIT),
    )(*operands)


def row_pass(blocks, counts, src, tgt, tnorm, tpot):
    slots = blocks.shape[1]
    return local_call(
        row_kernel, (blocks, counts, src, tgt, tnorm, tpot),
        [jax.ShapeDtypeStruct((1, src.shape[1]), jnp.float32)],
        [pltpu.VMEM((slots, BLOCK, BLOCK), jnp.float32),
         pltpu.VMEM((tgt.shape[0] + EXTRA, tgt.shape[1]), jnp.bfloat16),
         pltpu.VMEM((src.shape[0] + EXTRA, BLOCK), jnp.bfloat16),
         pltpu.VMEM((1, BLOCK), jnp.float32), pltpu.VMEM((1, BLOCK), jnp.float32)],
    )


def column_pass(blocks, counts, src, spot, tgt_ones, tnorm):
    return local_call(
        column_kernel, (blocks, counts, src, spot, tgt_ones, tnorm),
        [jax.ShapeDtypeStruct(tnorm.shape, jnp.float32)],
        [pltpu.VMEM(tnorm.shape, jnp.float32), pltpu.VMEM(tnorm.shape, jnp.float32),
         pltpu.VMEM((src.shape[0] + EXTRA, BLOCK), jnp.bfloat16)],
    )


def project_pass(blocks, counts, src, tgt, tnorm, tpot, feat):
    rows = src.shape[1]
    slots = blocks.shape[1]
    return local_call(
        project_kernel, (blocks, counts, src, tgt, tnorm, tpot, feat),
        [jax.ShapeDtypeStruct((2, rows), jnp.float32),
         jax.ShapeDtypeStruct((rows, feat.shape[0]), jnp.float32)],
        [pltpu.VMEM((slots, BLOCK, BLOCK), jnp.float32),
         pltpu.VMEM((slots, BLOCK, BLOCK), jnp.bfloat16),
         pltpu.VMEM((tgt.shape[0] + EXTRA, tgt.shape[1]), jnp.bfloat16),
         pltpu.VMEM((src.shape[0] + EXTRA, BLOCK), jnp.bfloat16),
         pltpu.VMEM((1, BLOCK), jnp.float32), pltpu.VMEM((1, BLOCK), jnp.float32)],
    )


def shards(src_emb, tgt_emb, target_features, src_mass, tgt_mass, kept_blocks, kept_count):
    src_rows = src_emb.shape[1]
    tgt_rows = tgt_emb.shape[1]
    src_t = src_emb
    tnorm = jnp.sum(jnp.square(tgt_emb.astype(jnp.float32)), axis=0).reshape(1, tgt_rows)
    counts = kept_count.reshape(-1)
    tgt_ones = jnp.concatenate(
        [tgt_emb, split_rows(jnp.zeros((1, tgt_rows), jnp.float32), True)], axis=0
    )

    tgt_potential = jnp.zeros((tgt_rows,), jnp.float32)
    src_potential = jnp.zeros((src_rows,), jnp.float32)
    for iteration in range(ITERS):
        tpot = tgt_potential.reshape(1, tgt_rows)
        (row_lse,) = row_pass(kept_blocks, counts, src_t, tgt_emb, tnorm, tpot)
        row_lse = butterfly_lse(row_lse.reshape(src_rows), "tgt")
        src_potential = EPSILON * jnp.log(src_mass) - EPSILON * row_lse
        (column_lse,) = column_pass(
            kept_blocks, counts, src_t, src_potential.reshape(1, src_rows), tgt_ones, tnorm
        )
        column_lse = butterfly_lse(column_lse.reshape(tgt_rows), "src")
        tgt_potential = EPSILON * jnp.log(tgt_mass) - EPSILON * column_lse

    tpot = tgt_potential.reshape(1, tgt_rows)
    small, numerator = project_pass(
        kept_blocks, counts, src_t, tgt_emb, tnorm, tpot, target_features
    )
    numerator, denominator = halving_merge(small, numerator, "tgt")
    projected = numerator / denominator[:, None]
    return (projected, src_potential, tgt_potential)


def solution(mesh):
    return jax.shard_map(
        shards,
        mesh=mesh,
        in_specs=(
            P(None, "src"),
            P(None, "tgt"),
            P(None, "tgt"),
            P("src"),
            P("tgt"),
            P("src", "tgt"),
            P("src", "tgt"),
        ),
        out_specs=(P(("src", "tgt"), None), P("src"), P("tgt")),
        check_vma=False,
    )
```

```python
import functools
import math

import jax
import jax.numpy as jnp
from jax import lax
from jax.experimental import pallas as pl
from jax.experimental.pallas import tpu as pltpu
from jax.sharding import PartitionSpec as P

BLOCK = 256
ITERS = 2


SENTINEL = -1e30
EPSILON = 0.1
SCALE = 1.0 / EPSILON
BASE2 = SCALE / math.log(2.0)


def lse_pair(value, other):
    overall = jnp.maximum(value, other)
    return overall + jnp.log(jnp.exp(value - overall) + jnp.exp(other - overall))


def butterfly_lse(value, axis):
    size = lax.axis_size(axis)
    step = 1
    while step < size:
        pairs = [(i, i ^ step) for i in range(size)]
        value = lse_pair(value, lax.ppermute(value, axis, pairs))
        step *= 2
    return value


def halving_merge(small, numerator, axis):
    size = lax.axis_size(axis)
    me = lax.axis_index(axis)
    rows = small.shape[1] // size
    small = small.reshape(2, size, rows)
    numerator = numerator.reshape(size, rows, numerator.shape[-1])
    step = 1
    while step < size:
        pairs = [(i, i ^ step) for i in range(size)]
        keep = (me // step) % 2
        count = numerator.shape[0] // 2

        def split(x, axis_at):
            x = x.reshape(x.shape[:axis_at] + (count, 2) + x.shape[axis_at + 1:])
            return (
                lax.dynamic_index_in_dim(x, keep, axis=axis_at + 1, keepdims=False),
                lax.dynamic_index_in_dim(x, 1 - keep, axis=axis_at + 1, keepdims=False),
            )

        small_keep, small_send = split(small, 1)
        num_keep, num_send = split(numerator, 0)
        small_other = lax.ppermute(small_send, axis, pairs)
        num_other = lax.ppermute(num_send, axis, pairs)
        overall = jnp.maximum(small_keep[0], small_other[0])
        mine = jnp.exp(small_keep[0] - overall)
        theirs = jnp.exp(small_other[0] - overall)
        numerator = num_keep * mine[..., None] + num_other * theirs[..., None]
        denominator = small_keep[1] * mine + small_other[1] * theirs
        step *= 2
        if step < size:
            small = jnp.stack([overall, denominator])
    return (numerator / denominator[..., None]).reshape(rows, -1)


CHUNK = 64
EXTRA = 16
VMEM_LIMIT = 24 * 1024 * 1024


def tile_slice(ref, b):
    return ref[:, pl.ds(pl.multiple_of(b * BLOCK, BLOCK), BLOCK)]


def row_slice(ref, r):
    return ref[pl.ds(pl.multiple_of(r * BLOCK, BLOCK), BLOCK), :]


def doubled_source(src_ref, r):
    exact = tile_slice(src_ref, r).astype(jnp.float32)
    return (exact * 2.0).astype(jnp.bfloat16), jnp.sum(exact * exact, axis=0, keepdims=True)


def products(doubled, tgt_ref, b):
    return lax.dot_general(doubled, tile_slice(tgt_ref, b), (((0,), (0,)), ((), ())),
                           preferred_element_type=jnp.float32)


def as_row(column, scratch):
    scratch[...] = jnp.broadcast_to(column, scratch.shape)
    return jnp.transpose(scratch[...])[0:1, :]


def as_column(row, scratch):
    scratch[...] = jnp.broadcast_to(row, scratch.shape)
    return jnp.transpose(scratch[...])[:, 0:1]


def by_count(live, slots, body):
    for count in range(1, slots + 1):
        pl.when(live == count)(functools.partial(body, count))


def over_rows(rows, body):
    lax.fori_loop(0, rows, lambda r, c: (body(r), c)[1], 0)


def fill_shifted(blocks_ref, r, count, doubled, tgt_ref, tnorm_ref, tpot_ref, held):
    for k in range(count):
        b = blocks_ref[r, k]
        shift = tile_slice(tpot_ref, b) - tile_slice(tnorm_ref, b)
        held[k] = products(doubled, tgt_ref, b) + shift


def chunk_peak(held, count, rows):
    peak = held[0, rows, :]
    for k in range(1, count):
        peak = jnp.maximum(peak, held[k, rows, :])
    return jnp.max(peak, axis=1, keepdims=True)


def row_kernel(blocks_ref, count_ref, src_ref, tgt_ref, tnorm_ref, tpot_ref,
               lse_ref, held, tgt_aug, rhs, peak_row, total_row):
    width = tgt_ref.shape[0]
    tgt_aug[0:width, :] = tgt_ref[...]
    tgt_aug[width:, :] = split_rows(tpot_ref[...] - tnorm_ref[...], False)

    def per_row(r):
        doubled, snorm = doubled_source(src_ref, r)
        rhs[0:width, :] = doubled
        rhs[width:, :] = split_rows(snorm, True)
        augmented = rhs[...]

        def body(count):
            for k in range(count):
                held[k] = lax.dot_general(tile_slice(tgt_aug, blocks_ref[r, k]), augmented,
                                          (((0,), (0,)), ((), ())),
                                          preferred_element_type=jnp.float32)
            folded = None
            for chunk in range(BLOCK // CHUNK):
                rows = pl.ds(chunk * CHUNK, CHUNK)
                peak = held[0, rows, :]
                for k in range(1, count):
                    peak = jnp.maximum(peak, held[k, rows, :])
                peak = jnp.max(peak.reshape(CHUNK // 8, 8, BLOCK), axis=0)
                folded = peak if folded is None else jnp.maximum(folded, peak)
            peak = jnp.max(folded, axis=0, keepdims=True)
            folded = None
            for chunk in range(BLOCK // CHUNK):
                rows = pl.ds(chunk * CHUNK, CHUNK)
                acc = jnp.exp2((held[0, rows, :] - peak) * BASE2)
                for k in range(1, count):
                    acc = acc + jnp.exp2((held[k, rows, :] - peak) * BASE2)
                acc = jnp.sum(acc.reshape(CHUNK // 8, 8, BLOCK), axis=0)
                folded = acc if folded is None else folded + acc
            peak_row[...] = peak
            total_row[...] = jnp.sum(folded, axis=0, keepdims=True)

        by_count(count_ref[r], held.shape[0], body)
        lanes = pl.ds(pl.multiple_of(r * BLOCK, BLOCK), BLOCK)
        lse_ref[:, lanes] = (peak_row[...] - snorm) * SCALE + jnp.log(total_row[...])

    over_rows(count_ref.shape[0], per_row)


def split_rows(row, ones):
    high = row.astype(jnp.bfloat16).astype(jnp.float32)
    middle = (row - high).astype(jnp.bfloat16).astype(jnp.float32)
    low = row - high - middle
    index = lax.broadcasted_iota(jnp.int32, (EXTRA, row.shape[1]), 0)
    if ones:
        rows = jnp.where(index < 3, 1.0, 0.0)
    else:
        rows = jnp.where(index == 0, high, jnp.where(index == 1, middle,
                                                     jnp.where(index == 2, low, 0.0)))
    return rows.astype(jnp.bfloat16)


def column_kernel(blocks_ref, count_ref, src_ref, spot_ref, tgt_ref, tnorm_ref,
                  lse_ref, top_ref, sum_ref, lhs):
    top_ref[...] = jnp.full(top_ref.shape, SENTINEL, jnp.float32)
    sum_ref[...] = jnp.zeros(sum_ref.shape, jnp.float32)
    width = src_ref.shape[0]

    def per_row(r):
        doubled, snorm = doubled_source(src_ref, r)
        lhs[0:width, :] = doubled
        lhs[width:, :] = split_rows(tile_slice(spot_ref, r) - snorm, False)
        augmented = lhs[...]

        def body(count):
            for k in range(count):
                b = blocks_ref[r, k]
                lanes = pl.ds(pl.multiple_of(b * BLOCK, BLOCK), BLOCK)
                shifted = products(augmented, tgt_ref, b)
                peak = jnp.max(shifted, axis=0, keepdims=True)
                totals = jnp.sum(jnp.exp2((shifted - peak) * BASE2), axis=0, keepdims=True)
                highest = (peak - tnorm_ref[:, lanes]) * SCALE
                old_top = top_ref[:, lanes]
                new_top = jnp.maximum(old_top, highest)
                sum_ref[:, lanes] = (sum_ref[:, lanes] * jnp.exp(old_top - new_top)
                                     + totals * jnp.exp(highest - new_top))
                top_ref[:, lanes] = new_top

        by_count(count_ref[r], blocks_ref.shape[1], body)

    over_rows(count_ref.shape[0], per_row)
    totals = sum_ref[...]
    lse_ref[...] = jnp.where(totals > 0.0, top_ref[...] + jnp.log(totals), SENTINEL)


def project_kernel(blocks_ref, count_ref, src_ref, tgt_ref, tnorm_ref, tpot_ref, feat_ref,
                   small_ref, num_ref, held, weights, tgt_aug, rhs, peak_row, den_row):
    width = tgt_ref.shape[0]
    tgt_aug[0:width, :] = tgt_ref[...]
    tgt_aug[width:, :] = split_rows(tpot_ref[...] - tnorm_ref[...], False)

    def per_row(r):
        doubled, snorm = doubled_source(src_ref, r)
        rhs[0:width, :] = doubled
        rhs[width:, :] = split_rows(snorm, True)
        augmented = rhs[...]

        def body(count):
            for k in range(count):
                held[k] = lax.dot_general(tile_slice(tgt_aug, blocks_ref[r, k]), augmented,
                                          (((0,), (0,)), ((), ())),
                                          preferred_element_type=jnp.float32)
            folded = None
            for chunk in range(BLOCK // CHUNK):
                rows = pl.ds(chunk * CHUNK, CHUNK)
                peak = held[0, rows, :]
                for k in range(1, count):
                    peak = jnp.maximum(peak, held[k, rows, :])
                peak = jnp.max(peak.reshape(CHUNK // 8, 8, BLOCK), axis=0)
                folded = peak if folded is None else jnp.maximum(folded, peak)
            peak = jnp.max(folded, axis=0, keepdims=True)
            folded = None
            for chunk in range(BLOCK // CHUNK):
                rows = pl.ds(chunk * CHUNK, CHUNK)
                acc = jnp.zeros((CHUNK, BLOCK), jnp.float32)
                for k in range(count):
                    rounded = jnp.exp2((held[k, rows, :] - peak) * BASE2).astype(jnp.bfloat16)
                    weights[k, rows, :] = rounded
                    acc = acc + rounded.astype(jnp.float32)
                acc = jnp.sum(acc.reshape(CHUNK // 8, 8, BLOCK), axis=0)
                folded = acc if folded is None else folded + acc
            total = None
            for k in range(count):
                part = jnp.dot(tile_slice(feat_ref, blocks_ref[r, k]), weights[k],
                               preferred_element_type=jnp.float32)
                total = part if total is None else total + part
            num_ref[pl.ds(pl.multiple_of(r * BLOCK, BLOCK), BLOCK), :] = jnp.transpose(total)
            peak_row[...] = peak
            den_row[...] = jnp.sum(folded, axis=0, keepdims=True)

        by_count(count_ref[r], held.shape[0], body)
        lanes = pl.ds(pl.multiple_of(r * BLOCK, BLOCK), BLOCK)
        small_ref[0:1, lanes] = (peak_row[...] - snorm) * SCALE
        small_ref[1:2, lanes] = den_row[...]

    over_rows(count_ref.shape[0], per_row)


def whole(shape):
    return pl.BlockSpec(shape, lambda r, *_: (0,) * len(shape))


def resident():
    return pl.BlockSpec(memory_space=pltpu.VMEM)


def column_scratch():
    return pltpu.VMEM((BLOCK, 1), jnp.float32)


def local_call(kernel, operands, outs, scratch):
    spec = pltpu.PrefetchScalarGridSpec(
        num_scalar_prefetch=2,
        grid=(1,),
        in_specs=[resident() for x in operands[2:]],
        out_specs=[resident() for o in outs],
        scratch_shapes=scratch,
    )
    return pl.pallas_call(
        kernel, grid_spec=spec, out_shape=outs,
        compiler_params=pltpu.CompilerParams(vmem_limit_bytes=VMEM_LIMIT),
    )(*operands)


def row_pass(blocks, counts, src, tgt, tnorm, tpot):
    slots = blocks.shape[1]
    return local_call(
        row_kernel, (blocks, counts, src, tgt, tnorm, tpot),
        [jax.ShapeDtypeStruct((1, src.shape[1]), jnp.float32)],
        [pltpu.VMEM((slots, BLOCK, BLOCK), jnp.float32),
         pltpu.VMEM((tgt.shape[0] + EXTRA, tgt.shape[1]), jnp.bfloat16),
         pltpu.VMEM((src.shape[0] + EXTRA, BLOCK), jnp.bfloat16),
         pltpu.VMEM((1, BLOCK), jnp.float32), pltpu.VMEM((1, BLOCK), jnp.float32)],
    )


def column_pass(blocks, counts, src, spot, tgt_ones, tnorm):
    return local_call(
        column_kernel, (blocks, counts, src, spot, tgt_ones, tnorm),
        [jax.ShapeDtypeStruct(tnorm.shape, jnp.float32)],
        [pltpu.VMEM(tnorm.shape, jnp.float32), pltpu.VMEM(tnorm.shape, jnp.float32),
         pltpu.VMEM((src.shape[0] + EXTRA, BLOCK), jnp.bfloat16)],
    )


def project_pass(blocks, counts, src, tgt, tnorm, tpot, feat):
    rows = src.shape[1]
    slots = blocks.shape[1]
    return local_call(
        project_kernel, (blocks, counts, src, tgt, tnorm, tpot, feat),
        [jax.ShapeDtypeStruct((2, rows), jnp.float32),
         jax.ShapeDtypeStruct((rows, feat.shape[0]), jnp.float32)],
        [pltpu.VMEM((slots, BLOCK, BLOCK), jnp.float32),
         pltpu.VMEM((slots, BLOCK, BLOCK), jnp.bfloat16),
         pltpu.VMEM((tgt.shape[0] + EXTRA, tgt.shape[1]), jnp.bfloat16),
         pltpu.VMEM((src.shape[0] + EXTRA, BLOCK), jnp.bfloat16),
         pltpu.VMEM((1, BLOCK), jnp.float32), pltpu.VMEM((1, BLOCK), jnp.float32)],
    )


def shards(src_emb, tgt_emb, target_features, src_mass, tgt_mass, kept_blocks, kept_count):
    src_rows = src_emb.shape[1]
    tgt_rows = tgt_emb.shape[1]
    src_t = src_emb
    tnorm = jnp.sum(jnp.square(tgt_emb.astype(jnp.float32)), axis=0).reshape(1, tgt_rows)
    counts = kept_count.reshape(-1)
    tgt_ones = jnp.concatenate(
        [tgt_emb, split_rows(jnp.zeros((1, tgt_rows), jnp.float32), True)], axis=0
    )

    tgt_potential = jnp.zeros((tgt_rows,), jnp.float32)
    src_potential = jnp.zeros((src_rows,), jnp.float32)
    for iteration in range(ITERS):
        tpot = tgt_potential.reshape(1, tgt_rows)
        (row_lse,) = row_pass(kept_blocks, counts, src_t, tgt_emb, tnorm, tpot)
        row_lse = butterfly_lse(row_lse.reshape(src_rows), "tgt")
        src_potential = EPSILON * jnp.log(src_mass) - EPSILON * row_lse
        (column_lse,) = column_pass(
            kept_blocks, counts, src_t, src_potential.reshape(1, src_rows), tgt_ones, tnorm
        )
        column_lse = butterfly_lse(column_lse.reshape(tgt_rows), "src")
        tgt_potential = EPSILON * jnp.log(tgt_mass) - EPSILON * column_lse

    tpot = tgt_potential.reshape(1, tgt_rows)
    small, numerator = project_pass(
        kept_blocks, counts, src_t, tgt_emb, tnorm, tpot, target_features
    )
    projected = halving_merge(small, numerator, "tgt")
    return (projected, src_potential, tgt_potential)


def solution(mesh):
    return jax.shard_map(
        shards,
        mesh=mesh,
        in_specs=(
            P(None, "src"),
            P(None, "tgt"),
            P(None, "tgt"),
            P("src"),
            P("tgt"),
            P("src", "tgt"),
            P("src", "tgt"),
        ),
        out_specs=(P(("src", "tgt"), None), P("src"), P("tgt")),
        check_vma=False,
    )
```

```python
import functools
import math

import jax
import jax.numpy as jnp
from jax import lax
from jax.experimental import pallas as pl
from jax.experimental.pallas import tpu as pltpu
from jax.sharding import PartitionSpec as P

BLOCK = 256
ITERS = 2


SENTINEL = -1e30
EPSILON = 0.1
SCALE = 1.0 / EPSILON
BASE2 = SCALE / math.log(2.0)


def lse_pair(value, other):
    overall = jnp.maximum(value, other)
    return overall + jnp.log(jnp.exp(value - overall) + jnp.exp(other - overall))


def butterfly_lse(value, axis):
    size = lax.axis_size(axis)
    step = 1
    while step < size:
        pairs = [(i, i ^ step) for i in range(size)]
        value = lse_pair(value, lax.ppermute(value, axis, pairs))
        step *= 2
    return value


def two_round_lse(value, axis):
    size = lax.axis_size(axis)
    if size < 4:
        return butterfly_lse(value, axis)
    value = lse_pair(value, lax.ppermute(value, axis, [(i, i ^ 1) for i in range(size)]))
    others = [lax.ppermute(value, axis, [(i, i ^ mask) for i in range(size)])
              for mask in range(2, size, 2)]
    overall = value
    for other in others:
        overall = jnp.maximum(overall, other)
    total = jnp.exp(value - overall)
    for other in others:
        total = total + jnp.exp(other - overall)
    return overall + jnp.log(total)


def halving_merge(small, numerator, axis):
    size = lax.axis_size(axis)
    me = lax.axis_index(axis)
    rows = small.shape[1] // size
    small = small.reshape(2, size, rows)
    numerator = numerator.reshape(size, rows, numerator.shape[-1])
    step = 1
    while step < size:
        pairs = [(i, i ^ step) for i in range(size)]
        keep = (me // step) % 2
        count = numerator.shape[0] // 2

        def split(x, axis_at):
            x = x.reshape(x.shape[:axis_at] + (count, 2) + x.shape[axis_at + 1:])
            return (
                lax.dynamic_index_in_dim(x, keep, axis=axis_at + 1, keepdims=False),
                lax.dynamic_index_in_dim(x, 1 - keep, axis=axis_at + 1, keepdims=False),
            )

        small_keep, small_send = split(small, 1)
        num_keep, num_send = split(numerator, 0)
        small_other = lax.ppermute(small_send, axis, pairs)
        num_other = lax.ppermute(num_send, axis, pairs)
        overall = jnp.maximum(small_keep[0], small_other[0])
        mine = jnp.exp(small_keep[0] - overall)
        theirs = jnp.exp(small_other[0] - overall)
        numerator = num_keep * mine[..., None] + num_other * theirs[..., None]
        denominator = small_keep[1] * mine + small_other[1] * theirs
        step *= 2
        if step < size:
            small = jnp.stack([overall, denominator])
    return (numerator / denominator[..., None]).reshape(rows, -1)


CHUNK = 64
EXTRA = 16
VMEM_LIMIT = 24 * 1024 * 1024


def tile_slice(ref, b):
    return ref[:, pl.ds(pl.multiple_of(b * BLOCK, BLOCK), BLOCK)]


def row_slice(ref, r):
    return ref[pl.ds(pl.multiple_of(r * BLOCK, BLOCK), BLOCK), :]


def doubled_source(src_ref, r):
    exact = tile_slice(src_ref, r).astype(jnp.float32)
    return (exact * 2.0).astype(jnp.bfloat16), jnp.sum(exact * exact, axis=0, keepdims=True)


def products(doubled, tgt_ref, b):
    return lax.dot_general(doubled, tile_slice(tgt_ref, b), (((0,), (0,)), ((), ())),
                           preferred_element_type=jnp.float32)


def as_row(column, scratch):
    scratch[...] = jnp.broadcast_to(column, scratch.shape)
    return jnp.transpose(scratch[...])[0:1, :]


def as_column(row, scratch):
    scratch[...] = jnp.broadcast_to(row, scratch.shape)
    return jnp.transpose(scratch[...])[:, 0:1]


def by_count(live, slots, body):
    for count in range(1, slots + 1):
        pl.when(live == count)(functools.partial(body, count))


def over_rows(rows, body):
    lax.fori_loop(0, rows, lambda r, c: (body(r), c)[1], 0)


def fill_shifted(blocks_ref, r, count, doubled, tgt_ref, tnorm_ref, tpot_ref, held):
    for k in range(count):
        b = blocks_ref[r, k]
        shift = tile_slice(tpot_ref, b) - tile_slice(tnorm_ref, b)
        held[k] = products(doubled, tgt_ref, b) + shift


def chunk_peak(held, count, rows):
    peak = held[0, rows, :]
    for k in range(1, count):
        peak = jnp.maximum(peak, held[k, rows, :])
    return jnp.max(peak, axis=1, keepdims=True)


def row_kernel(blocks_ref, count_ref, src_ref, tgt_ref, tnorm_ref, tpot_ref,
               lse_ref, held, tgt_aug, rhs, peak_row, total_row):
    width = tgt_ref.shape[0]
    tgt_aug[0:width, :] = tgt_ref[...]
    tgt_aug[width:, :] = split_rows(tpot_ref[...] - tnorm_ref[...], False)

    def per_row(r):
        doubled, snorm = doubled_source(src_ref, r)
        rhs[0:width, :] = doubled
        rhs[width:, :] = split_rows(snorm, True)
        augmented = rhs[...]

        def body(count):
            for k in range(count):
                held[k] = lax.dot_general(tile_slice(tgt_aug, blocks_ref[r, k]), augmented,
                                          (((0,), (0,)), ((), ())),
                                          preferred_element_type=jnp.float32)
            folded = None
            for chunk in range(BLOCK // CHUNK):
                rows = pl.ds(chunk * CHUNK, CHUNK)
                peak = held[0, rows, :]
                for k in range(1, count):
                    peak = jnp.maximum(peak, held[k, rows, :])
                peak = jnp.max(peak.reshape(CHUNK // 8, 8, BLOCK), axis=0)
                folded = peak if folded is None else jnp.maximum(folded, peak)
            peak = jnp.max(folded, axis=0, keepdims=True)
            folded = None
            for chunk in range(BLOCK // CHUNK):
                rows = pl.ds(chunk * CHUNK, CHUNK)
                acc = jnp.exp2((held[0, rows, :] - peak) * BASE2)
                for k in range(1, count):
                    acc = acc + jnp.exp2((held[k, rows, :] - peak) * BASE2)
                acc = jnp.sum(acc.reshape(CHUNK // 8, 8, BLOCK), axis=0)
                folded = acc if folded is None else folded + acc
            peak_row[...] = peak
            total_row[...] = jnp.sum(folded, axis=0, keepdims=True)

        by_count(count_ref[r], held.shape[0], body)
        lanes = pl.ds(pl.multiple_of(r * BLOCK, BLOCK), BLOCK)
        lse_ref[:, lanes] = (peak_row[...] - snorm) * SCALE + jnp.log(total_row[...])

    over_rows(count_ref.shape[0], per_row)


def split_rows(row, ones):
    high = row.astype(jnp.bfloat16).astype(jnp.float32)
    middle = (row - high).astype(jnp.bfloat16).astype(jnp.float32)
    low = row - high - middle
    index = lax.broadcasted_iota(jnp.int32, (EXTRA, row.shape[1]), 0)
    if ones:
        rows = jnp.where(index < 3, 1.0, 0.0)
    else:
        rows = jnp.where(index == 0, high, jnp.where(index == 1, middle,
                                                     jnp.where(index == 2, low, 0.0)))
    return rows.astype(jnp.bfloat16)


def column_kernel(blocks_ref, count_ref, src_ref, spot_ref, tgt_ref, tnorm_ref,
                  lse_ref, top_ref, sum_ref, lhs):
    top_ref[...] = jnp.full(top_ref.shape, SENTINEL, jnp.float32)
    sum_ref[...] = jnp.zeros(sum_ref.shape, jnp.float32)
    width = src_ref.shape[0]

    def per_row(r):
        doubled, snorm = doubled_source(src_ref, r)
        lhs[0:width, :] = doubled
        lhs[width:, :] = split_rows(tile_slice(spot_ref, r) - snorm, False)
        augmented = lhs[...]

        def body(count):
            for k in range(count):
                b = blocks_ref[r, k]
                lanes = pl.ds(pl.multiple_of(b * BLOCK, BLOCK), BLOCK)
                shifted = products(augmented, tgt_ref, b)
                peak = jnp.max(shifted, axis=0, keepdims=True)
                totals = jnp.sum(jnp.exp2((shifted - peak) * BASE2), axis=0, keepdims=True)
                highest = (peak - tnorm_ref[:, lanes]) * SCALE
                old_top = top_ref[:, lanes]
                new_top = jnp.maximum(old_top, highest)
                sum_ref[:, lanes] = (sum_ref[:, lanes] * jnp.exp(old_top - new_top)
                                     + totals * jnp.exp(highest - new_top))
                top_ref[:, lanes] = new_top

        by_count(count_ref[r], blocks_ref.shape[1], body)

    over_rows(count_ref.shape[0], per_row)
    totals = sum_ref[...]
    lse_ref[...] = jnp.where(totals > 0.0, top_ref[...] + jnp.log(totals), SENTINEL)


def project_kernel(blocks_ref, count_ref, src_ref, tgt_ref, tnorm_ref, tpot_ref, feat_ref,
                   small_ref, num_ref, held, weights, tgt_aug, rhs, peak_row, den_row):
    width = tgt_ref.shape[0]
    tgt_aug[0:width, :] = tgt_ref[...]
    tgt_aug[width:, :] = split_rows(tpot_ref[...] - tnorm_ref[...], False)

    def per_row(r):
        doubled, snorm = doubled_source(src_ref, r)
        rhs[0:width, :] = doubled
        rhs[width:, :] = split_rows(snorm, True)
        augmented = rhs[...]

        def body(count):
            for k in range(count):
                held[k] = lax.dot_general(tile_slice(tgt_aug, blocks_ref[r, k]), augmented,
                                          (((0,), (0,)), ((), ())),
                                          preferred_element_type=jnp.float32)
            folded = None
            for chunk in range(BLOCK // CHUNK):
                rows = pl.ds(chunk * CHUNK, CHUNK)
                peak = held[0, rows, :]
                for k in range(1, count):
                    peak = jnp.maximum(peak, held[k, rows, :])
                peak = jnp.max(peak.reshape(CHUNK // 8, 8, BLOCK), axis=0)
                folded = peak if folded is None else jnp.maximum(folded, peak)
            peak = jnp.max(folded, axis=0, keepdims=True)
            folded = None
            for chunk in range(BLOCK // CHUNK):
                rows = pl.ds(chunk * CHUNK, CHUNK)
                acc = jnp.zeros((CHUNK, BLOCK), jnp.float32)
                for k in range(count):
                    rounded = jnp.exp2((held[k, rows, :] - peak) * BASE2).astype(jnp.bfloat16)
                    weights[k, rows, :] = rounded
                    acc = acc + rounded.astype(jnp.float32)
                acc = jnp.sum(acc.reshape(CHUNK // 8, 8, BLOCK), axis=0)
                folded = acc if folded is None else folded + acc
            total = None
            for k in range(count):
                part = jnp.dot(tile_slice(feat_ref, blocks_ref[r, k]), weights[k],
                               preferred_element_type=jnp.float32)
                total = part if total is None else total + part
            num_ref[pl.ds(pl.multiple_of(r * BLOCK, BLOCK), BLOCK), :] = jnp.transpose(total)
            peak_row[...] = peak
            den_row[...] = jnp.sum(folded, axis=0, keepdims=True)

        by_count(count_ref[r], held.shape[0], body)
        lanes = pl.ds(pl.multiple_of(r * BLOCK, BLOCK), BLOCK)
        small_ref[0:1, lanes] = (peak_row[...] - snorm) * SCALE
        small_ref[1:2, lanes] = den_row[...]

    over_rows(count_ref.shape[0], per_row)


def whole(shape):
    return pl.BlockSpec(shape, lambda r, *_: (0,) * len(shape))


def resident():
    return pl.BlockSpec(memory_space=pltpu.VMEM)


def column_scratch():
    return pltpu.VMEM((BLOCK, 1), jnp.float32)


def local_call(kernel, operands, outs, scratch):
    spec = pltpu.PrefetchScalarGridSpec(
        num_scalar_prefetch=2,
        grid=(1,),
        in_specs=[resident() for x in operands[2:]],
        out_specs=[resident() for o in outs],
        scratch_shapes=scratch,
    )
    return pl.pallas_call(
        kernel, grid_spec=spec, out_shape=outs,
        compiler_params=pltpu.CompilerParams(vmem_limit_bytes=VMEM_LIMIT),
    )(*operands)


def row_pass(blocks, counts, src, tgt, tnorm, tpot):
    slots = blocks.shape[1]
    return local_call(
        row_kernel, (blocks, counts, src, tgt, tnorm, tpot),
        [jax.ShapeDtypeStruct((1, src.shape[1]), jnp.float32)],
        [pltpu.VMEM((slots, BLOCK, BLOCK), jnp.float32),
         pltpu.VMEM((tgt.shape[0] + EXTRA, tgt.shape[1]), jnp.bfloat16),
         pltpu.VMEM((src.shape[0] + EXTRA, BLOCK), jnp.bfloat16),
         pltpu.VMEM((1, BLOCK), jnp.float32), pltpu.VMEM((1, BLOCK), jnp.float32)],
    )


def column_pass(blocks, counts, src, spot, tgt_ones, tnorm):
    return local_call(
        column_kernel, (blocks, counts, src, spot, tgt_ones, tnorm),
        [jax.ShapeDtypeStruct(tnorm.shape, jnp.float32)],
        [pltpu.VMEM(tnorm.shape, jnp.float32), pltpu.VMEM(tnorm.shape, jnp.float32),
         pltpu.VMEM((src.shape[0] + EXTRA, BLOCK), jnp.bfloat16)],
    )


def project_pass(blocks, counts, src, tgt, tnorm, tpot, feat):
    rows = src.shape[1]
    slots = blocks.shape[1]
    return local_call(
        project_kernel, (blocks, counts, src, tgt, tnorm, tpot, feat),
        [jax.ShapeDtypeStruct((2, rows), jnp.float32),
         jax.ShapeDtypeStruct((rows, feat.shape[0]), jnp.float32)],
        [pltpu.VMEM((slots, BLOCK, BLOCK), jnp.float32),
         pltpu.VMEM((slots, BLOCK, BLOCK), jnp.bfloat16),
         pltpu.VMEM((tgt.shape[0] + EXTRA, tgt.shape[1]), jnp.bfloat16),
         pltpu.VMEM((src.shape[0] + EXTRA, BLOCK), jnp.bfloat16),
         pltpu.VMEM((1, BLOCK), jnp.float32), pltpu.VMEM((1, BLOCK), jnp.float32)],
    )


def shards(src_emb, tgt_emb, target_features, src_mass, tgt_mass, kept_blocks, kept_count):
    src_rows = src_emb.shape[1]
    tgt_rows = tgt_emb.shape[1]
    src_t = src_emb
    tnorm = jnp.sum(jnp.square(tgt_emb.astype(jnp.float32)), axis=0).reshape(1, tgt_rows)
    counts = kept_count.reshape(-1)
    tgt_ones = jnp.concatenate(
        [tgt_emb, split_rows(jnp.zeros((1, tgt_rows), jnp.float32), True)], axis=0
    )

    tgt_potential = jnp.zeros((tgt_rows,), jnp.float32)
    src_potential = jnp.zeros((src_rows,), jnp.float32)
    for iteration in range(ITERS):
        tpot = tgt_potential.reshape(1, tgt_rows)
        (row_lse,) = row_pass(kept_blocks, counts, src_t, tgt_emb, tnorm, tpot)
        row_lse = butterfly_lse(row_lse.reshape(src_rows), "tgt")
        src_potential = EPSILON * jnp.log(src_mass) - EPSILON * row_lse
        (column_lse,) = column_pass(
            kept_blocks, counts, src_t, src_potential.reshape(1, src_rows), tgt_ones, tnorm
        )
        column_lse = two_round_lse(column_lse.reshape(tgt_rows), "src")
        tgt_potential = EPSILON * jnp.log(tgt_mass) - EPSILON * column_lse

    tpot = tgt_potential.reshape(1, tgt_rows)
    small, numerator = project_pass(
        kept_blocks, counts, src_t, tgt_emb, tnorm, tpot, target_features
    )
    projected = halving_merge(small, numerator, "tgt")
    return (projected, src_potential, tgt_potential)


def solution(mesh):
    return jax.shard_map(
        shards,
        mesh=mesh,
        in_specs=(
            P(None, "src"),
            P(None, "tgt"),
            P(None, "tgt"),
            P("src"),
            P("tgt"),
            P("src", "tgt"),
            P("src", "tgt"),
        ),
        out_specs=(P(("src", "tgt"), None), P("src"), P("tgt")),
        check_vma=False,
    )
```

```python
import functools
import math

import jax
import jax.numpy as jnp
from jax import lax
from jax.experimental import pallas as pl
from jax.experimental.pallas import tpu as pltpu
from jax.sharding import PartitionSpec as P

BLOCK = 256
ITERS = 2


SENTINEL = -1e30
EPSILON = 0.1
SCALE = 1.0 / EPSILON
BASE2 = SCALE / math.log(2.0)


def lse_pair(value, other):
    overall = jnp.maximum(value, other)
    return overall + jnp.log(jnp.exp(value - overall) + jnp.exp(other - overall))


def butterfly_lse(value, axis):
    size = lax.axis_size(axis)
    step = 1
    while step < size:
        pairs = [(i, i ^ step) for i in range(size)]
        value = lse_pair(value, lax.ppermute(value, axis, pairs))
        step *= 2
    return value


def merge_many(value, others):
    overall = value
    for other in others:
        overall = jnp.maximum(overall, other)
    total = jnp.exp(value - overall)
    for other in others:
        total = total + jnp.exp(other - overall)
    return overall + jnp.log(total)


def exchange(value, axis, masks):
    size = lax.axis_size(axis)
    return [lax.ppermute(value, axis, [(i, i ^ mask) for i in range(size)]) for mask in masks]


def two_round_lse(value, axis):
    size = lax.axis_size(axis)
    if size < 4:
        return butterfly_lse(value, axis)
    value = lse_pair(value, exchange(value, axis, [1])[0])
    return merge_many(value, exchange(value, axis, range(2, size, 2)))


def one_round_lse(value, axis):
    size = lax.axis_size(axis)
    if size > 4:
        return two_round_lse(value, axis)
    return merge_many(value, exchange(value, axis, range(1, size)))


def halving_merge(small, numerator, axis):
    size = lax.axis_size(axis)
    me = lax.axis_index(axis)
    rows = small.shape[1] // size
    small = small.reshape(2, size, rows)
    numerator = numerator.reshape(size, rows, numerator.shape[-1])
    step = 1
    while step < size:
        pairs = [(i, i ^ step) for i in range(size)]
        keep = (me // step) % 2
        count = numerator.shape[0] // 2

        def split(x, axis_at):
            x = x.reshape(x.shape[:axis_at] + (count, 2) + x.shape[axis_at + 1:])
            return (
                lax.dynamic_index_in_dim(x, keep, axis=axis_at + 1, keepdims=False),
                lax.dynamic_index_in_dim(x, 1 - keep, axis=axis_at + 1, keepdims=False),
            )

        small_keep, small_send = split(small, 1)
        num_keep, num_send = split(numerator, 0)
        small_other = lax.ppermute(small_send, axis, pairs)
        num_other = lax.ppermute(num_send, axis, pairs)
        overall = jnp.maximum(small_keep[0], small_other[0])
        mine = jnp.exp(small_keep[0] - overall)
        theirs = jnp.exp(small_other[0] - overall)
        numerator = num_keep * mine[..., None] + num_other * theirs[..., None]
        denominator = small_keep[1] * mine + small_other[1] * theirs
        step *= 2
        if step < size:
            small = jnp.stack([overall, denominator])
    return (numerator / denominator[..., None]).reshape(rows, -1)


CHUNK = 64
EXTRA = 16
VMEM_LIMIT = 24 * 1024 * 1024


def tile_slice(ref, b):
    return ref[:, pl.ds(pl.multiple_of(b * BLOCK, BLOCK), BLOCK)]


def row_slice(ref, r):
    return ref[pl.ds(pl.multiple_of(r * BLOCK, BLOCK), BLOCK), :]


def doubled_source(src_ref, r):
    exact = tile_slice(src_ref, r).astype(jnp.float32)
    return (exact * 2.0).astype(jnp.bfloat16), jnp.sum(exact * exact, axis=0, keepdims=True)


def products(doubled, tgt_ref, b):
    return lax.dot_general(doubled, tile_slice(tgt_ref, b), (((0,), (0,)), ((), ())),
                           preferred_element_type=jnp.float32)


def as_row(column, scratch):
    scratch[...] = jnp.broadcast_to(column, scratch.shape)
    return jnp.transpose(scratch[...])[0:1, :]


def as_column(row, scratch):
    scratch[...] = jnp.broadcast_to(row, scratch.shape)
    return jnp.transpose(scratch[...])[:, 0:1]


def by_count(live, slots, body):
    for count in range(1, slots + 1):
        pl.when(live == count)(functools.partial(body, count))


def over_rows(rows, body):
    lax.fori_loop(0, rows, lambda r, c: (body(r), c)[1], 0)


def fill_shifted(blocks_ref, r, count, doubled, tgt_ref, tnorm_ref, tpot_ref, held):
    for k in range(count):
        b = blocks_ref[r, k]
        shift = tile_slice(tpot_ref, b) - tile_slice(tnorm_ref, b)
        held[k] = products(doubled, tgt_ref, b) + shift


def chunk_peak(held, count, rows):
    peak = held[0, rows, :]
    for k in range(1, count):
        peak = jnp.maximum(peak, held[k, rows, :])
    return jnp.max(peak, axis=1, keepdims=True)


def row_kernel(blocks_ref, count_ref, src_ref, tgt_ref, tnorm_ref, tpot_ref,
               lse_ref, held, tgt_aug, rhs, peak_row, total_row):
    width = tgt_ref.shape[0]
    tgt_aug[0:width, :] = tgt_ref[...]
    tgt_aug[width:, :] = split_rows(tpot_ref[...] - tnorm_ref[...], False)

    def per_row(r):
        doubled, snorm = doubled_source(src_ref, r)
        rhs[0:width, :] = doubled
        rhs[width:, :] = split_rows(snorm, True)
        augmented = rhs[...]

        def body(count):
            for k in range(count):
                held[k] = lax.dot_general(tile_slice(tgt_aug, blocks_ref[r, k]), augmented,
                                          (((0,), (0,)), ((), ())),
                                          preferred_element_type=jnp.float32)
            folded = None
            for chunk in range(BLOCK // CHUNK):
                rows = pl.ds(chunk * CHUNK, CHUNK)
                peak = held[0, rows, :]
                for k in range(1, count):
                    peak = jnp.maximum(peak, held[k, rows, :])
                peak = jnp.max(peak.reshape(CHUNK // 8, 8, BLOCK), axis=0)
                folded = peak if folded is None else jnp.maximum(folded, peak)
            peak = jnp.max(folded, axis=0, keepdims=True)
            folded = None
            for chunk in range(BLOCK // CHUNK):
                rows = pl.ds(chunk * CHUNK, CHUNK)
                acc = jnp.exp2((held[0, rows, :] - peak) * BASE2)
                for k in range(1, count):
                    acc = acc + jnp.exp2((held[k, rows, :] - peak) * BASE2)
                acc = jnp.sum(acc.reshape(CHUNK // 8, 8, BLOCK), axis=0)
                folded = acc if folded is None else folded + acc
            peak_row[...] = peak
            total_row[...] = jnp.sum(folded, axis=0, keepdims=True)

        by_count(count_ref[r], held.shape[0], body)
        lanes = pl.ds(pl.multiple_of(r * BLOCK, BLOCK), BLOCK)
        lse_ref[:, lanes] = (peak_row[...] - snorm) * SCALE + jnp.log(total_row[...])

    over_rows(count_ref.shape[0], per_row)


def split_rows(row, ones):
    high = row.astype(jnp.bfloat16).astype(jnp.float32)
    middle = (row - high).astype(jnp.bfloat16).astype(jnp.float32)
    low = row - high - middle
    index = lax.broadcasted_iota(jnp.int32, (EXTRA, row.shape[1]), 0)
    if ones:
        rows = jnp.where(index < 3, 1.0, 0.0)
    else:
        rows = jnp.where(index == 0, high, jnp.where(index == 1, middle,
                                                     jnp.where(index == 2, low, 0.0)))
    return rows.astype(jnp.bfloat16)


def column_kernel(blocks_ref, count_ref, src_ref, spot_ref, tgt_ref, tnorm_ref,
                  lse_ref, top_ref, sum_ref, lhs):
    top_ref[...] = jnp.full(top_ref.shape, SENTINEL, jnp.float32)
    sum_ref[...] = jnp.zeros(sum_ref.shape, jnp.float32)
    width = src_ref.shape[0]

    def per_row(r):
        doubled, snorm = doubled_source(src_ref, r)
        lhs[0:width, :] = doubled
        lhs[width:, :] = split_rows(tile_slice(spot_ref, r) - snorm, False)
        augmented = lhs[...]

        def body(count):
            for k in range(count):
                b = blocks_ref[r, k]
                lanes = pl.ds(pl.multiple_of(b * BLOCK, BLOCK), BLOCK)
                shifted = products(augmented, tgt_ref, b)
                peak = jnp.max(shifted, axis=0, keepdims=True)
                totals = jnp.sum(jnp.exp2((shifted - peak) * BASE2), axis=0, keepdims=True)
                highest = (peak - tnorm_ref[:, lanes]) * SCALE
                old_top = top_ref[:, lanes]
                new_top = jnp.maximum(old_top, highest)
                sum_ref[:, lanes] = (sum_ref[:, lanes] * jnp.exp(old_top - new_top)
                                     + totals * jnp.exp(highest - new_top))
                top_ref[:, lanes] = new_top

        by_count(count_ref[r], blocks_ref.shape[1], body)

    over_rows(count_ref.shape[0], per_row)
    totals = sum_ref[...]
    lse_ref[...] = jnp.where(totals > 0.0, top_ref[...] + jnp.log(totals), SENTINEL)


def project_kernel(blocks_ref, count_ref, src_ref, tgt_ref, tnorm_ref, tpot_ref, feat_ref,
                   small_ref, num_ref, held, weights, tgt_aug, rhs, peak_row, den_row):
    width = tgt_ref.shape[0]
    tgt_aug[0:width, :] = tgt_ref[...]
    tgt_aug[width:, :] = split_rows(tpot_ref[...] - tnorm_ref[...], False)

    def per_row(r):
        doubled, snorm = doubled_source(src_ref, r)
        rhs[0:width, :] = doubled
        rhs[width:, :] = split_rows(snorm, True)
        augmented = rhs[...]

        def body(count):
            for k in range(count):
                held[k] = lax.dot_general(tile_slice(tgt_aug, blocks_ref[r, k]), augmented,
                                          (((0,), (0,)), ((), ())),
                                          preferred_element_type=jnp.float32)
            folded = None
            for chunk in range(BLOCK // CHUNK):
                rows = pl.ds(chunk * CHUNK, CHUNK)
                peak = held[0, rows, :]
                for k in range(1, count):
                    peak = jnp.maximum(peak, held[k, rows, :])
                peak = jnp.max(peak.reshape(CHUNK // 8, 8, BLOCK), axis=0)
                folded = peak if folded is None else jnp.maximum(folded, peak)
            peak = jnp.max(folded, axis=0, keepdims=True)
            folded = None
            for chunk in range(BLOCK // CHUNK):
                rows = pl.ds(chunk * CHUNK, CHUNK)
                acc = jnp.zeros((CHUNK, BLOCK), jnp.float32)
                for k in range(count):
                    rounded = jnp.exp2((held[k, rows, :] - peak) * BASE2).astype(jnp.bfloat16)
                    weights[k, rows, :] = rounded
                    acc = acc + rounded.astype(jnp.float32)
                acc = jnp.sum(acc.reshape(CHUNK // 8, 8, BLOCK), axis=0)
                folded = acc if folded is None else folded + acc
            total = None
            for k in range(count):
                part = jnp.dot(tile_slice(feat_ref, blocks_ref[r, k]), weights[k],
                               preferred_element_type=jnp.float32)
                total = part if total is None else total + part
            num_ref[pl.ds(pl.multiple_of(r * BLOCK, BLOCK), BLOCK), :] = jnp.transpose(total)
            peak_row[...] = peak
            den_row[...] = jnp.sum(folded, axis=0, keepdims=True)

        by_count(count_ref[r], held.shape[0], body)
        lanes = pl.ds(pl.multiple_of(r * BLOCK, BLOCK), BLOCK)
        small_ref[0:1, lanes] = (peak_row[...] - snorm) * SCALE
        small_ref[1:2, lanes] = den_row[...]

    over_rows(count_ref.shape[0], per_row)


def whole(shape):
    return pl.BlockSpec(shape, lambda r, *_: (0,) * len(shape))


def resident():
    return pl.BlockSpec(memory_space=pltpu.VMEM)


def column_scratch():
    return pltpu.VMEM((BLOCK, 1), jnp.float32)


def local_call(kernel, operands, outs, scratch):
    spec = pltpu.PrefetchScalarGridSpec(
        num_scalar_prefetch=2,
        grid=(1,),
        in_specs=[resident() for x in operands[2:]],
        out_specs=[resident() for o in outs],
        scratch_shapes=scratch,
    )
    return pl.pallas_call(
        kernel, grid_spec=spec, out_shape=outs,
        compiler_params=pltpu.CompilerParams(vmem_limit_bytes=VMEM_LIMIT),
    )(*operands)


def row_pass(blocks, counts, src, tgt, tnorm, tpot):
    slots = blocks.shape[1]
    return local_call(
        row_kernel, (blocks, counts, src, tgt, tnorm, tpot),
        [jax.ShapeDtypeStruct((1, src.shape[1]), jnp.float32)],
        [pltpu.VMEM((slots, BLOCK, BLOCK), jnp.float32),
         pltpu.VMEM((tgt.shape[0] + EXTRA, tgt.shape[1]), jnp.bfloat16),
         pltpu.VMEM((src.shape[0] + EXTRA, BLOCK), jnp.bfloat16),
         pltpu.VMEM((1, BLOCK), jnp.float32), pltpu.VMEM((1, BLOCK), jnp.float32)],
    )


def column_pass(blocks, counts, src, spot, tgt_ones, tnorm):
    return local_call(
        column_kernel, (blocks, counts, src, spot, tgt_ones, tnorm),
        [jax.ShapeDtypeStruct(tnorm.shape, jnp.float32)],
        [pltpu.VMEM(tnorm.shape, jnp.float32), pltpu.VMEM(tnorm.shape, jnp.float32),
         pltpu.VMEM((src.shape[0] + EXTRA, BLOCK), jnp.bfloat16)],
    )


def project_pass(blocks, counts, src, tgt, tnorm, tpot, feat):
    rows = src.shape[1]
    slots = blocks.shape[1]
    return local_call(
        project_kernel, (blocks, counts, src, tgt, tnorm, tpot, feat),
        [jax.ShapeDtypeStruct((2, rows), jnp.float32),
         jax.ShapeDtypeStruct((rows, feat.shape[0]), jnp.float32)],
        [pltpu.VMEM((slots, BLOCK, BLOCK), jnp.float32),
         pltpu.VMEM((slots, BLOCK, BLOCK), jnp.bfloat16),
         pltpu.VMEM((tgt.shape[0] + EXTRA, tgt.shape[1]), jnp.bfloat16),
         pltpu.VMEM((src.shape[0] + EXTRA, BLOCK), jnp.bfloat16),
         pltpu.VMEM((1, BLOCK), jnp.float32), pltpu.VMEM((1, BLOCK), jnp.float32)],
    )


def shards(src_emb, tgt_emb, target_features, src_mass, tgt_mass, kept_blocks, kept_count):
    src_rows = src_emb.shape[1]
    tgt_rows = tgt_emb.shape[1]
    src_t = src_emb
    tnorm = jnp.sum(jnp.square(tgt_emb.astype(jnp.float32)), axis=0).reshape(1, tgt_rows)
    counts = kept_count.reshape(-1)
    tgt_ones = jnp.concatenate(
        [tgt_emb, split_rows(jnp.zeros((1, tgt_rows), jnp.float32), True)], axis=0
    )

    tgt_potential = jnp.zeros((tgt_rows,), jnp.float32)
    src_potential = jnp.zeros((src_rows,), jnp.float32)
    for iteration in range(ITERS):
        tpot = tgt_potential.reshape(1, tgt_rows)
        (row_lse,) = row_pass(kept_blocks, counts, src_t, tgt_emb, tnorm, tpot)
        row_lse = one_round_lse(row_lse.reshape(src_rows), "tgt")
        src_potential = EPSILON * jnp.log(src_mass) - EPSILON * row_lse
        (column_lse,) = column_pass(
            kept_blocks, counts, src_t, src_potential.reshape(1, src_rows), tgt_ones, tnorm
        )
        column_lse = two_round_lse(column_lse.reshape(tgt_rows), "src")
        tgt_potential = EPSILON * jnp.log(tgt_mass) - EPSILON * column_lse

    tpot = tgt_potential.reshape(1, tgt_rows)
    small, numerator = project_pass(
        kept_blocks, counts, src_t, tgt_emb, tnorm, tpot, target_features
    )
    projected = halving_merge(small, numerator, "tgt")
    return (projected, src_potential, tgt_potential)


def solution(mesh):
    return jax.shard_map(
        shards,
        mesh=mesh,
        in_specs=(
            P(None, "src"),
            P(None, "tgt"),
            P(None, "tgt"),
            P("src"),
            P("tgt"),
            P("src", "tgt"),
            P("src", "tgt"),
        ),
        out_specs=(P(("src", "tgt"), None), P("src"), P("tgt")),
        check_vma=False,
    )
```

```python
import functools
import math

import jax
import jax.numpy as jnp
from jax import lax
from jax.experimental import pallas as pl
from jax.experimental.pallas import tpu as pltpu
from jax.sharding import PartitionSpec as P

BLOCK = 256
ITERS = 2


SENTINEL = -1e30
EPSILON = 0.1
SCALE = 1.0 / EPSILON
BASE2 = SCALE / math.log(2.0)


def lse_pair(value, other):
    overall = jnp.maximum(value, other)
    return overall + jnp.log(jnp.exp(value - overall) + jnp.exp(other - overall))


def butterfly_lse(value, axis):
    size = lax.axis_size(axis)
    step = 1
    while step < size:
        pairs = [(i, i ^ step) for i in range(size)]
        value = lse_pair(value, lax.ppermute(value, axis, pairs))
        step *= 2
    return value


def merge_many(value, others):
    overall = value
    for other in others:
        overall = jnp.maximum(overall, other)
    total = jnp.exp(value - overall)
    for other in others:
        total = total + jnp.exp(other - overall)
    return overall + jnp.log(total)


def exchange(value, axis, masks):
    size = lax.axis_size(axis)
    return [lax.ppermute(value, axis, [(i, i ^ mask) for i in range(size)]) for mask in masks]


def two_round_lse(value, axis):
    size = lax.axis_size(axis)
    if size < 4:
        return butterfly_lse(value, axis)
    value = lse_pair(value, exchange(value, axis, [1])[0])
    return merge_many(value, exchange(value, axis, range(2, size, 2)))


def one_round_lse(value, axis):
    size = lax.axis_size(axis)
    if size > 8:
        return two_round_lse(value, axis)
    return merge_many(value, exchange(value, axis, range(1, size)))


def halving_merge(small, numerator, axis):
    size = lax.axis_size(axis)
    me = lax.axis_index(axis)
    rows = small.shape[1] // size
    small = small.reshape(2, size, rows)
    numerator = numerator.reshape(size, rows, numerator.shape[-1])
    step = 1
    while step < size:
        pairs = [(i, i ^ step) for i in range(size)]
        keep = (me // step) % 2
        count = numerator.shape[0] // 2

        def split(x, axis_at):
            x = x.reshape(x.shape[:axis_at] + (count, 2) + x.shape[axis_at + 1:])
            return (
                lax.dynamic_index_in_dim(x, keep, axis=axis_at + 1, keepdims=False),
                lax.dynamic_index_in_dim(x, 1 - keep, axis=axis_at + 1, keepdims=False),
            )

        small_keep, small_send = split(small, 1)
        num_keep, num_send = split(numerator, 0)
        small_other = lax.ppermute(small_send, axis, pairs)
        num_other = lax.ppermute(num_send, axis, pairs)
        overall = jnp.maximum(small_keep[0], small_other[0])
        mine = jnp.exp(small_keep[0] - overall)
        theirs = jnp.exp(small_other[0] - overall)
        numerator = num_keep * mine[..., None] + num_other * theirs[..., None]
        denominator = small_keep[1] * mine + small_other[1] * theirs
        step *= 2
        if step < size:
            small = jnp.stack([overall, denominator])
    return (numerator / denominator[..., None]).reshape(rows, -1)


CHUNK = 64
EXTRA = 16
VMEM_LIMIT = 24 * 1024 * 1024


def tile_slice(ref, b):
    return ref[:, pl.ds(pl.multiple_of(b * BLOCK, BLOCK), BLOCK)]


def row_slice(ref, r):
    return ref[pl.ds(pl.multiple_of(r * BLOCK, BLOCK), BLOCK), :]


def doubled_source(src_ref, r):
    exact = tile_slice(src_ref, r).astype(jnp.float32)
    return (exact * 2.0).astype(jnp.bfloat16), jnp.sum(exact * exact, axis=0, keepdims=True)


def products(doubled, tgt_ref, b):
    return lax.dot_general(doubled, tile_slice(tgt_ref, b), (((0,), (0,)), ((), ())),
                           preferred_element_type=jnp.float32)


def as_row(column, scratch):
    scratch[...] = jnp.broadcast_to(column, scratch.shape)
    return jnp.transpose(scratch[...])[0:1, :]


def as_column(row, scratch):
    scratch[...] = jnp.broadcast_to(row, scratch.shape)
    return jnp.transpose(scratch[...])[:, 0:1]


def by_count(live, slots, body):
    for count in range(1, slots + 1):
        pl.when(live == count)(functools.partial(body, count))


def over_rows(rows, body):
    lax.fori_loop(0, rows, lambda r, c: (body(r), c)[1], 0)


def fill_shifted(blocks_ref, r, count, doubled, tgt_ref, tnorm_ref, tpot_ref, held):
    for k in range(count):
        b = blocks_ref[r, k]
        shift = tile_slice(tpot_ref, b) - tile_slice(tnorm_ref, b)
        held[k] = products(doubled, tgt_ref, b) + shift


def chunk_peak(held, count, rows):
    peak = held[0, rows, :]
    for k in range(1, count):
        peak = jnp.maximum(peak, held[k, rows, :])
    return jnp.max(peak, axis=1, keepdims=True)


def row_kernel(blocks_ref, count_ref, src_ref, tgt_ref, tnorm_ref, tpot_ref,
               lse_ref, held, tgt_aug, rhs, peak_row, total_row):
    width = tgt_ref.shape[0]
    tgt_aug[0:width, :] = tgt_ref[...]
    tgt_aug[width:, :] = split_rows(tpot_ref[...] - tnorm_ref[...], False)

    def per_row(r):
        doubled, snorm = doubled_source(src_ref, r)
        rhs[0:width, :] = doubled
        rhs[width:, :] = split_rows(snorm, True)
        augmented = rhs[...]

        def body(count):
            for k in range(count):
                held[k] = lax.dot_general(tile_slice(tgt_aug, blocks_ref[r, k]), augmented,
                                          (((0,), (0,)), ((), ())),
                                          preferred_element_type=jnp.float32)
            folded = None
            for chunk in range(BLOCK // CHUNK):
                rows = pl.ds(chunk * CHUNK, CHUNK)
                peak = held[0, rows, :]
                for k in range(1, count):
                    peak = jnp.maximum(peak, held[k, rows, :])
                peak = jnp.max(peak.reshape(CHUNK // 8, 8, BLOCK), axis=0)
                folded = peak if folded is None else jnp.maximum(folded, peak)
            peak = jnp.max(folded, axis=0, keepdims=True)
            folded = None
            for chunk in range(BLOCK // CHUNK):
                rows = pl.ds(chunk * CHUNK, CHUNK)
                acc = jnp.exp2((held[0, rows, :] - peak) * BASE2)
                for k in range(1, count):
                    acc = acc + jnp.exp2((held[k, rows, :] - peak) * BASE2)
                acc = jnp.sum(acc.reshape(CHUNK // 8, 8, BLOCK), axis=0)
                folded = acc if folded is None else folded + acc
            peak_row[...] = peak
            total_row[...] = jnp.sum(folded, axis=0, keepdims=True)

        by_count(count_ref[r], held.shape[0], body)
        lanes = pl.ds(pl.multiple_of(r * BLOCK, BLOCK), BLOCK)
        lse_ref[:, lanes] = (peak_row[...] - snorm) * SCALE + jnp.log(total_row[...])

    over_rows(count_ref.shape[0], per_row)


def split_rows(row, ones):
    high = row.astype(jnp.bfloat16).astype(jnp.float32)
    middle = (row - high).astype(jnp.bfloat16).astype(jnp.float32)
    low = row - high - middle
    index = lax.broadcasted_iota(jnp.int32, (EXTRA, row.shape[1]), 0)
    if ones:
        rows = jnp.where(index < 3, 1.0, 0.0)
    else:
        rows = jnp.where(index == 0, high, jnp.where(index == 1, middle,
                                                     jnp.where(index == 2, low, 0.0)))
    return rows.astype(jnp.bfloat16)


def column_kernel(blocks_ref, count_ref, src_ref, spot_ref, tgt_ref, tnorm_ref,
                  lse_ref, top_ref, sum_ref, lhs):
    top_ref[...] = jnp.full(top_ref.shape, SENTINEL, jnp.float32)
    sum_ref[...] = jnp.zeros(sum_ref.shape, jnp.float32)
    width = src_ref.shape[0]

    def per_row(r):
        doubled, snorm = doubled_source(src_ref, r)
        lhs[0:width, :] = doubled
        lhs[width:, :] = split_rows(tile_slice(spot_ref, r) - snorm, False)
        augmented = lhs[...]

        def body(count):
            for k in range(count):
                b = blocks_ref[r, k]
                lanes = pl.ds(pl.multiple_of(b * BLOCK, BLOCK), BLOCK)
                shifted = products(augmented, tgt_ref, b)
                peak = jnp.max(shifted, axis=0, keepdims=True)
                totals = jnp.sum(jnp.exp2((shifted - peak) * BASE2), axis=0, keepdims=True)
                highest = (peak - tnorm_ref[:, lanes]) * SCALE
                old_top = top_ref[:, lanes]
                new_top = jnp.maximum(old_top, highest)
                sum_ref[:, lanes] = (sum_ref[:, lanes] * jnp.exp(old_top - new_top)
                                     + totals * jnp.exp(highest - new_top))
                top_ref[:, lanes] = new_top

        by_count(count_ref[r], blocks_ref.shape[1], body)

    over_rows(count_ref.shape[0], per_row)
    totals = sum_ref[...]
    lse_ref[...] = jnp.where(totals > 0.0, top_ref[...] + jnp.log(totals), SENTINEL)


def project_kernel(blocks_ref, count_ref, src_ref, tgt_ref, tnorm_ref, tpot_ref, feat_ref,
                   small_ref, num_ref, held, weights, tgt_aug, rhs, peak_row, den_row):
    width = tgt_ref.shape[0]
    tgt_aug[0:width, :] = tgt_ref[...]
    tgt_aug[width:, :] = split_rows(tpot_ref[...] - tnorm_ref[...], False)

    def per_row(r):
        doubled, snorm = doubled_source(src_ref, r)
        rhs[0:width, :] = doubled
        rhs[width:, :] = split_rows(snorm, True)
        augmented = rhs[...]

        def body(count):
            for k in range(count):
                held[k] = lax.dot_general(tile_slice(tgt_aug, blocks_ref[r, k]), augmented,
                                          (((0,), (0,)), ((), ())),
                                          preferred_element_type=jnp.float32)
            folded = None
            for chunk in range(BLOCK // CHUNK):
                rows = pl.ds(chunk * CHUNK, CHUNK)
                peak = held[0, rows, :]
                for k in range(1, count):
                    peak = jnp.maximum(peak, held[k, rows, :])
                peak = jnp.max(peak.reshape(CHUNK // 8, 8, BLOCK), axis=0)
                folded = peak if folded is None else jnp.maximum(folded, peak)
            peak = jnp.max(folded, axis=0, keepdims=True)
            folded = None
            for chunk in range(BLOCK // CHUNK):
                rows = pl.ds(chunk * CHUNK, CHUNK)
                acc = jnp.zeros((CHUNK, BLOCK), jnp.float32)
                for k in range(count):
                    rounded = jnp.exp2((held[k, rows, :] - peak) * BASE2).astype(jnp.bfloat16)
                    weights[k, rows, :] = rounded
                    acc = acc + rounded.astype(jnp.float32)
                acc = jnp.sum(acc.reshape(CHUNK // 8, 8, BLOCK), axis=0)
                folded = acc if folded is None else folded + acc
            total = None
            for k in range(count):
                part = jnp.dot(tile_slice(feat_ref, blocks_ref[r, k]), weights[k],
                               preferred_element_type=jnp.float32)
                total = part if total is None else total + part
            num_ref[pl.ds(pl.multiple_of(r * BLOCK, BLOCK), BLOCK), :] = jnp.transpose(total)
            peak_row[...] = peak
            den_row[...] = jnp.sum(folded, axis=0, keepdims=True)

        by_count(count_ref[r], held.shape[0], body)
        lanes = pl.ds(pl.multiple_of(r * BLOCK, BLOCK), BLOCK)
        small_ref[0:1, lanes] = (peak_row[...] - snorm) * SCALE
        small_ref[1:2, lanes] = den_row[...]

    over_rows(count_ref.shape[0], per_row)


def whole(shape):
    return pl.BlockSpec(shape, lambda r, *_: (0,) * len(shape))


def resident():
    return pl.BlockSpec(memory_space=pltpu.VMEM)


def column_scratch():
    return pltpu.VMEM((BLOCK, 1), jnp.float32)


def local_call(kernel, operands, outs, scratch):
    spec = pltpu.PrefetchScalarGridSpec(
        num_scalar_prefetch=2,
        grid=(1,),
        in_specs=[resident() for x in operands[2:]],
        out_specs=[resident() for o in outs],
        scratch_shapes=scratch,
    )
    return pl.pallas_call(
        kernel, grid_spec=spec, out_shape=outs,
        compiler_params=pltpu.CompilerParams(vmem_limit_bytes=VMEM_LIMIT),
    )(*operands)


def row_pass(blocks, counts, src, tgt, tnorm, tpot):
    slots = blocks.shape[1]
    return local_call(
        row_kernel, (blocks, counts, src, tgt, tnorm, tpot),
        [jax.ShapeDtypeStruct((1, src.shape[1]), jnp.float32)],
        [pltpu.VMEM((slots, BLOCK, BLOCK), jnp.float32),
         pltpu.VMEM((tgt.shape[0] + EXTRA, tgt.shape[1]), jnp.bfloat16),
         pltpu.VMEM((src.shape[0] + EXTRA, BLOCK), jnp.bfloat16),
         pltpu.VMEM((1, BLOCK), jnp.float32), pltpu.VMEM((1, BLOCK), jnp.float32)],
    )


def column_pass(blocks, counts, src, spot, tgt_ones, tnorm):
    return local_call(
        column_kernel, (blocks, counts, src, spot, tgt_ones, tnorm),
        [jax.ShapeDtypeStruct(tnorm.shape, jnp.float32)],
        [pltpu.VMEM(tnorm.shape, jnp.float32), pltpu.VMEM(tnorm.shape, jnp.float32),
         pltpu.VMEM((src.shape[0] + EXTRA, BLOCK), jnp.bfloat16)],
    )


def project_pass(blocks, counts, src, tgt, tnorm, tpot, feat):
    rows = src.shape[1]
    slots = blocks.shape[1]
    return local_call(
        project_kernel, (blocks, counts, src, tgt, tnorm, tpot, feat),
        [jax.ShapeDtypeStruct((2, rows), jnp.float32),
         jax.ShapeDtypeStruct((rows, feat.shape[0]), jnp.float32)],
        [pltpu.VMEM((slots, BLOCK, BLOCK), jnp.float32),
         pltpu.VMEM((slots, BLOCK, BLOCK), jnp.bfloat16),
         pltpu.VMEM((tgt.shape[0] + EXTRA, tgt.shape[1]), jnp.bfloat16),
         pltpu.VMEM((src.shape[0] + EXTRA, BLOCK), jnp.bfloat16),
         pltpu.VMEM((1, BLOCK), jnp.float32), pltpu.VMEM((1, BLOCK), jnp.float32)],
    )


def shards(src_emb, tgt_emb, target_features, src_mass, tgt_mass, kept_blocks, kept_count):
    src_rows = src_emb.shape[1]
    tgt_rows = tgt_emb.shape[1]
    src_t = src_emb
    tnorm = jnp.sum(jnp.square(tgt_emb.astype(jnp.float32)), axis=0).reshape(1, tgt_rows)
    counts = kept_count.reshape(-1)
    tgt_ones = jnp.concatenate(
        [tgt_emb, split_rows(jnp.zeros((1, tgt_rows), jnp.float32), True)], axis=0
    )

    tgt_potential = jnp.zeros((tgt_rows,), jnp.float32)
    src_potential = jnp.zeros((src_rows,), jnp.float32)
    for iteration in range(ITERS):
        tpot = tgt_potential.reshape(1, tgt_rows)
        (row_lse,) = row_pass(kept_blocks, counts, src_t, tgt_emb, tnorm, tpot)
        row_lse = one_round_lse(row_lse.reshape(src_rows), "tgt")
        src_potential = EPSILON * jnp.log(src_mass) - EPSILON * row_lse
        (column_lse,) = column_pass(
            kept_blocks, counts, src_t, src_potential.reshape(1, src_rows), tgt_ones, tnorm
        )
        column_lse = one_round_lse(column_lse.reshape(tgt_rows), "src")
        tgt_potential = EPSILON * jnp.log(tgt_mass) - EPSILON * column_lse

    tpot = tgt_potential.reshape(1, tgt_rows)
    small, numerator = project_pass(
        kept_blocks, counts, src_t, tgt_emb, tnorm, tpot, target_features
    )
    projected = halving_merge(small, numerator, "tgt")
    return (projected, src_potential, tgt_potential)


def solution(mesh):
    return jax.shard_map(
        shards,
        mesh=mesh,
        in_specs=(
            P(None, "src"),
            P(None, "tgt"),
            P(None, "tgt"),
            P("src"),
            P("tgt"),
            P("src", "tgt"),
            P("src", "tgt"),
        ),
        out_specs=(P(("src", "tgt"), None), P("src"), P("tgt")),
        check_vma=False,
    )
```

```python
import functools
import math

import jax
import jax.numpy as jnp
from jax import lax
from jax.experimental import pallas as pl
from jax.experimental.pallas import tpu as pltpu
from jax.sharding import PartitionSpec as P

BLOCK = 256
ITERS = 2


SENTINEL = -1e30
EPSILON = 0.1
SCALE = 1.0 / EPSILON
BASE2 = SCALE / math.log(2.0)


def lse_pair(value, other):
    overall = jnp.maximum(value, other)
    return overall + jnp.log(jnp.exp(value - overall) + jnp.exp(other - overall))


def butterfly_lse(value, axis):
    size = lax.axis_size(axis)
    step = 1
    while step < size:
        pairs = [(i, i ^ step) for i in range(size)]
        value = lse_pair(value, lax.ppermute(value, axis, pairs))
        step *= 2
    return value


def merge_many(value, others):
    overall = value
    for other in others:
        overall = jnp.maximum(overall, other)
    total = jnp.exp(value - overall)
    for other in others:
        total = total + jnp.exp(other - overall)
    return overall + jnp.log(total)


def exchange(value, axis, masks):
    size = lax.axis_size(axis)
    return [lax.ppermute(value, axis, [(i, i ^ mask) for i in range(size)]) for mask in masks]


def two_round_lse(value, axis):
    size = lax.axis_size(axis)
    if size < 4:
        return butterfly_lse(value, axis)
    value = lse_pair(value, exchange(value, axis, [1])[0])
    return merge_many(value, exchange(value, axis, range(2, size, 2)))


def one_round_lse(value, axis):
    size = lax.axis_size(axis)
    if size > 4:
        return two_round_lse(value, axis)
    return merge_many(value, exchange(value, axis, range(1, size)))


def halving_merge(small, numerator, axis):
    size = lax.axis_size(axis)
    me = lax.axis_index(axis)
    rows = small.shape[1] // size
    small = small.reshape(2, size, rows)
    numerator = numerator.reshape(size, rows, numerator.shape[-1])
    step = 1
    while step < size:
        pairs = [(i, i ^ step) for i in range(size)]
        keep = (me // step) % 2
        count = numerator.shape[0] // 2

        def split(x, axis_at):
            x = x.reshape(x.shape[:axis_at] + (count, 2) + x.shape[axis_at + 1:])
            return (
                lax.dynamic_index_in_dim(x, keep, axis=axis_at + 1, keepdims=False),
                lax.dynamic_index_in_dim(x, 1 - keep, axis=axis_at + 1, keepdims=False),
            )

        small_keep, small_send = split(small, 1)
        num_keep, num_send = split(numerator, 0)
        small_other = lax.ppermute(small_send, axis, pairs)
        num_other = lax.ppermute(num_send, axis, pairs)
        overall = jnp.maximum(small_keep[0], small_other[0])
        mine = jnp.exp(small_keep[0] - overall)
        theirs = jnp.exp(small_other[0] - overall)
        numerator = num_keep * mine[..., None] + num_other * theirs[..., None]
        denominator = small_keep[1] * mine + small_other[1] * theirs
        step *= 2
        if step < size:
            small = jnp.stack([overall, denominator])
    return (numerator / denominator[..., None]).reshape(rows, -1)


def direct_merge(small, numerator, axis):
    size = lax.axis_size(axis)
    if size > 4:
        return halving_merge(small, numerator, axis)
    me = lax.axis_index(axis)
    rows = small.shape[1] // size
    small = small.reshape(2, size, rows)
    numerator = numerator.reshape(size, rows, numerator.shape[-1])
    parts = [(lax.dynamic_index_in_dim(small, me, axis=1, keepdims=False),
              lax.dynamic_index_in_dim(numerator, me, axis=0, keepdims=False))]
    for mask in range(1, size):
        pairs = [(i, i ^ mask) for i in range(size)]
        owner = me ^ mask
        parts.append((
            lax.ppermute(lax.dynamic_index_in_dim(small, owner, axis=1, keepdims=False), axis, pairs),
            lax.ppermute(lax.dynamic_index_in_dim(numerator, owner, axis=0, keepdims=False), axis,
                         pairs),
        ))
    overall = parts[0][0][0]
    for part in parts[1:]:
        overall = jnp.maximum(overall, part[0][0])
    total_num = None
    total_den = None
    for part_small, part_num in parts:
        factor = jnp.exp(part_small[0] - overall)
        num = part_num * factor[:, None]
        den = part_small[1] * factor
        total_num = num if total_num is None else total_num + num
        total_den = den if total_den is None else total_den + den
    return total_num / total_den[:, None]


CHUNK = 64
EXTRA = 16
VMEM_LIMIT = 24 * 1024 * 1024


def tile_slice(ref, b):
    return ref[:, pl.ds(pl.multiple_of(b * BLOCK, BLOCK), BLOCK)]


def row_slice(ref, r):
    return ref[pl.ds(pl.multiple_of(r * BLOCK, BLOCK), BLOCK), :]


def doubled_source(src_ref, r):
    exact = tile_slice(src_ref, r).astype(jnp.float32)
    return (exact * 2.0).astype(jnp.bfloat16), jnp.sum(exact * exact, axis=0, keepdims=True)


def products(doubled, tgt_ref, b):
    return lax.dot_general(doubled, tile_slice(tgt_ref, b), (((0,), (0,)), ((), ())),
                           preferred_element_type=jnp.float32)


def as_row(column, scratch):
    scratch[...] = jnp.broadcast_to(column, scratch.shape)
    return jnp.transpose(scratch[...])[0:1, :]


def as_column(row, scratch):
    scratch[...] = jnp.broadcast_to(row, scratch.shape)
    return jnp.transpose(scratch[...])[:, 0:1]


def by_count(live, slots, body):
    for count in range(1, slots + 1):
        pl.when(live == count)(functools.partial(body, count))


def over_rows(rows, body):
    lax.fori_loop(0, rows, lambda r, c: (body(r), c)[1], 0)


def fill_shifted(blocks_ref, r, count, doubled, tgt_ref, tnorm_ref, tpot_ref, held):
    for k in range(count):
        b = blocks_ref[r, k]
        shift = tile_slice(tpot_ref, b) - tile_slice(tnorm_ref, b)
        held[k] = products(doubled, tgt_ref, b) + shift


def chunk_peak(held, count, rows):
    peak = held[0, rows, :]
    for k in range(1, count):
        peak = jnp.maximum(peak, held[k, rows, :])
    return jnp.max(peak, axis=1, keepdims=True)


def row_kernel(blocks_ref, count_ref, src_ref, tgt_ref, tnorm_ref, tpot_ref,
               lse_ref, held, tgt_aug, rhs, peak_row, total_row):
    width = tgt_ref.shape[0]
    tgt_aug[0:width, :] = tgt_ref[...]
    tgt_aug[width:, :] = split_rows(tpot_ref[...] - tnorm_ref[...], False)

    def per_row(r):
        doubled, snorm = doubled_source(src_ref, r)
        rhs[0:width, :] = doubled
        rhs[width:, :] = split_rows(snorm, True)
        augmented = rhs[...]

        def body(count):
            for k in range(count):
                held[k] = lax.dot_general(tile_slice(tgt_aug, blocks_ref[r, k]), augmented,
                                          (((0,), (0,)), ((), ())),
                                          preferred_element_type=jnp.float32)
            folded = None
            for chunk in range(BLOCK // CHUNK):
                rows = pl.ds(chunk * CHUNK, CHUNK)
                peak = held[0, rows, :]
                for k in range(1, count):
                    peak = jnp.maximum(peak, held[k, rows, :])
                peak = jnp.max(peak.reshape(CHUNK // 8, 8, BLOCK), axis=0)
                folded = peak if folded is None else jnp.maximum(folded, peak)
            peak = jnp.max(folded, axis=0, keepdims=True)
            folded = None
            for chunk in range(BLOCK // CHUNK):
                rows = pl.ds(chunk * CHUNK, CHUNK)
                acc = jnp.exp2((held[0, rows, :] - peak) * BASE2)
                for k in range(1, count):
                    acc = acc + jnp.exp2((held[k, rows, :] - peak) * BASE2)
                acc = jnp.sum(acc.reshape(CHUNK // 8, 8, BLOCK), axis=0)
                folded = acc if folded is None else folded + acc
            peak_row[...] = peak
            total_row[...] = jnp.sum(folded, axis=0, keepdims=True)

        by_count(count_ref[r], held.shape[0], body)
        lanes = pl.ds(pl.multiple_of(r * BLOCK, BLOCK), BLOCK)
        lse_ref[:, lanes] = (peak_row[...] - snorm) * SCALE + jnp.log(total_row[...])

    over_rows(count_ref.shape[0], per_row)


def split_rows(row, ones):
    high = row.astype(jnp.bfloat16).astype(jnp.float32)
    middle = (row - high).astype(jnp.bfloat16).astype(jnp.float32)
    low = row - high - middle
    index = lax.broadcasted_iota(jnp.int32, (EXTRA, row.shape[1]), 0)
    if ones:
        rows = jnp.where(index < 3, 1.0, 0.0)
    else:
        rows = jnp.where(index == 0, high, jnp.where(index == 1, middle,
                                                     jnp.where(index == 2, low, 0.0)))
    return rows.astype(jnp.bfloat16)


def column_kernel(blocks_ref, count_ref, src_ref, spot_ref, tgt_ref, tnorm_ref,
                  lse_ref, top_ref, sum_ref, lhs):
    top_ref[...] = jnp.full(top_ref.shape, SENTINEL, jnp.float32)
    sum_ref[...] = jnp.zeros(sum_ref.shape, jnp.float32)
    width = src_ref.shape[0]

    def per_row(r):
        doubled, snorm = doubled_source(src_ref, r)
        lhs[0:width, :] = doubled
        lhs[width:, :] = split_rows(tile_slice(spot_ref, r) - snorm, False)
        augmented = lhs[...]

        def body(count):
            for k in range(count):
                b = blocks_ref[r, k]
                lanes = pl.ds(pl.multiple_of(b * BLOCK, BLOCK), BLOCK)
                shifted = products(augmented, tgt_ref, b)
                peak = jnp.max(shifted, axis=0, keepdims=True)
                totals = jnp.sum(jnp.exp2((shifted - peak) * BASE2), axis=0, keepdims=True)
                highest = (peak - tnorm_ref[:, lanes]) * SCALE
                old_top = top_ref[:, lanes]
                new_top = jnp.maximum(old_top, highest)
                sum_ref[:, lanes] = (sum_ref[:, lanes] * jnp.exp(old_top - new_top)
                                     + totals * jnp.exp(highest - new_top))
                top_ref[:, lanes] = new_top

        by_count(count_ref[r], blocks_ref.shape[1], body)

    over_rows(count_ref.shape[0], per_row)
    totals = sum_ref[...]
    lse_ref[...] = jnp.where(totals > 0.0, top_ref[...] + jnp.log(totals), SENTINEL)


def project_kernel(blocks_ref, count_ref, src_ref, tgt_ref, tnorm_ref, tpot_ref, feat_ref,
                   small_ref, num_ref, held, weights, tgt_aug, rhs, peak_row, den_row):
    width = tgt_ref.shape[0]
    tgt_aug[0:width, :] = tgt_ref[...]
    tgt_aug[width:, :] = split_rows(tpot_ref[...] - tnorm_ref[...], False)

    def per_row(r):
        doubled, snorm = doubled_source(src_ref, r)
        rhs[0:width, :] = doubled
        rhs[width:, :] = split_rows(snorm, True)
        augmented = rhs[...]

        def body(count):
            for k in range(count):
                held[k] = lax.dot_general(tile_slice(tgt_aug, blocks_ref[r, k]), augmented,
                                          (((0,), (0,)), ((), ())),
                                          preferred_element_type=jnp.float32)
            folded = None
            for chunk in range(BLOCK // CHUNK):
                rows = pl.ds(chunk * CHUNK, CHUNK)
                peak = held[0, rows, :]
                for k in range(1, count):
                    peak = jnp.maximum(peak, held[k, rows, :])
                peak = jnp.max(peak.reshape(CHUNK // 8, 8, BLOCK), axis=0)
                folded = peak if folded is None else jnp.maximum(folded, peak)
            peak = jnp.max(folded, axis=0, keepdims=True)
            folded = None
            for chunk in range(BLOCK // CHUNK):
                rows = pl.ds(chunk * CHUNK, CHUNK)
                acc = jnp.zeros((CHUNK, BLOCK), jnp.float32)
                for k in range(count):
                    rounded = jnp.exp2((held[k, rows, :] - peak) * BASE2).astype(jnp.bfloat16)
                    weights[k, rows, :] = rounded
                    acc = acc + rounded.astype(jnp.float32)
                acc = jnp.sum(acc.reshape(CHUNK // 8, 8, BLOCK), axis=0)
                folded = acc if folded is None else folded + acc
            total = None
            for k in range(count):
                part = jnp.dot(tile_slice(feat_ref, blocks_ref[r, k]), weights[k],
                               preferred_element_type=jnp.float32)
                total = part if total is None else total + part
            num_ref[pl.ds(pl.multiple_of(r * BLOCK, BLOCK), BLOCK), :] = jnp.transpose(total)
            peak_row[...] = peak
            den_row[...] = jnp.sum(folded, axis=0, keepdims=True)

        by_count(count_ref[r], held.shape[0], body)
        lanes = pl.ds(pl.multiple_of(r * BLOCK, BLOCK), BLOCK)
        small_ref[0:1, lanes] = (peak_row[...] - snorm) * SCALE
        small_ref[1:2, lanes] = den_row[...]

    over_rows(count_ref.shape[0], per_row)


def whole(shape):
    return pl.BlockSpec(shape, lambda r, *_: (0,) * len(shape))


def resident():
    return pl.BlockSpec(memory_space=pltpu.VMEM)


def column_scratch():
    return pltpu.VMEM((BLOCK, 1), jnp.float32)


def local_call(kernel, operands, outs, scratch):
    spec = pltpu.PrefetchScalarGridSpec(
        num_scalar_prefetch=2,
        grid=(1,),
        in_specs=[resident() for x in operands[2:]],
        out_specs=[resident() for o in outs],
        scratch_shapes=scratch,
    )
    return pl.pallas_call(
        kernel, grid_spec=spec, out_shape=outs,
        compiler_params=pltpu.CompilerParams(vmem_limit_bytes=VMEM_LIMIT),
    )(*operands)


def row_pass(blocks, counts, src, tgt, tnorm, tpot):
    slots = blocks.shape[1]
    return local_call(
        row_kernel, (blocks, counts, src, tgt, tnorm, tpot),
        [jax.ShapeDtypeStruct((1, src.shape[1]), jnp.float32)],
        [pltpu.VMEM((slots, BLOCK, BLOCK), jnp.float32),
         pltpu.VMEM((tgt.shape[0] + EXTRA, tgt.shape[1]), jnp.bfloat16),
         pltpu.VMEM((src.shape[0] + EXTRA, BLOCK), jnp.bfloat16),
         pltpu.VMEM((1, BLOCK), jnp.float32), pltpu.VMEM((1, BLOCK), jnp.float32)],
    )


def column_pass(blocks, counts, src, spot, tgt_ones, tnorm):
    return local_call(
        column_kernel, (blocks, counts, src, spot, tgt_ones, tnorm),
        [jax.ShapeDtypeStruct(tnorm.shape, jnp.float32)],
        [pltpu.VMEM(tnorm.shape, jnp.float32), pltpu.VMEM(tnorm.shape, jnp.float32),
         pltpu.VMEM((src.shape[0] + EXTRA, BLOCK), jnp.bfloat16)],
    )


def project_pass(blocks, counts, src, tgt, tnorm, tpot, feat):
    rows = src.shape[1]
    slots = blocks.shape[1]
    return local_call(
        project_kernel, (blocks, counts, src, tgt, tnorm, tpot, feat),
        [jax.ShapeDtypeStruct((2, rows), jnp.float32),
         jax.ShapeDtypeStruct((rows, feat.shape[0]), jnp.float32)],
        [pltpu.VMEM((slots, BLOCK, BLOCK), jnp.float32),
         pltpu.VMEM((slots, BLOCK, BLOCK), jnp.bfloat16),
         pltpu.VMEM((tgt.shape[0] + EXTRA, tgt.shape[1]), jnp.bfloat16),
         pltpu.VMEM((src.shape[0] + EXTRA, BLOCK), jnp.bfloat16),
         pltpu.VMEM((1, BLOCK), jnp.float32), pltpu.VMEM((1, BLOCK), jnp.float32)],
    )


def shards(src_emb, tgt_emb, target_features, src_mass, tgt_mass, kept_blocks, kept_count):
    src_rows = src_emb.shape[1]
    tgt_rows = tgt_emb.shape[1]
    src_t = src_emb
    tnorm = jnp.sum(jnp.square(tgt_emb.astype(jnp.float32)), axis=0).reshape(1, tgt_rows)
    counts = kept_count.reshape(-1)
    tgt_ones = jnp.concatenate(
        [tgt_emb, split_rows(jnp.zeros((1, tgt_rows), jnp.float32), True)], axis=0
    )

    tgt_potential = jnp.zeros((tgt_rows,), jnp.float32)
    src_potential = jnp.zeros((src_rows,), jnp.float32)
    for iteration in range(ITERS):
        tpot = tgt_potential.reshape(1, tgt_rows)
        (row_lse,) = row_pass(kept_blocks, counts, src_t, tgt_emb, tnorm, tpot)
        row_lse = one_round_lse(row_lse.reshape(src_rows), "tgt")
        src_potential = EPSILON * jnp.log(src_mass) - EPSILON * row_lse
        (column_lse,) = column_pass(
            kept_blocks, counts, src_t, src_potential.reshape(1, src_rows), tgt_ones, tnorm
        )
        column_lse = two_round_lse(column_lse.reshape(tgt_rows), "src")
        tgt_potential = EPSILON * jnp.log(tgt_mass) - EPSILON * column_lse

    tpot = tgt_potential.reshape(1, tgt_rows)
    small, numerator = project_pass(
        kept_blocks, counts, src_t, tgt_emb, tnorm, tpot, target_features
    )
    projected = direct_merge(small, numerator, "tgt")
    return (projected, src_potential, tgt_potential)


def solution(mesh):
    return jax.shard_map(
        shards,
        mesh=mesh,
        in_specs=(
            P(None, "src"),
            P(None, "tgt"),
            P(None, "tgt"),
            P("src"),
            P("tgt"),
            P("src", "tgt"),
            P("src", "tgt"),
        ),
        out_specs=(P(("src", "tgt"), None), P("src"), P("tgt")),
        check_vma=False,
    )
```

```python
import functools
import math

import jax
import jax.numpy as jnp
from jax import lax
from jax.experimental import pallas as pl
from jax.experimental.pallas import tpu as pltpu
from jax.sharding import PartitionSpec as P

BLOCK = 256
ITERS = 2


SENTINEL = -1e30
EPSILON = 0.1
SCALE = 1.0 / EPSILON
BASE2 = SCALE / math.log(2.0)


def lse_pair(value, other):
    overall = jnp.maximum(value, other)
    return overall + jnp.log(jnp.exp(value - overall) + jnp.exp(other - overall))


def butterfly_lse(value, axis):
    size = lax.axis_size(axis)
    step = 1
    while step < size:
        pairs = [(i, i ^ step) for i in range(size)]
        value = lse_pair(value, lax.ppermute(value, axis, pairs))
        step *= 2
    return value


def merge_many(value, others):
    overall = value
    for other in others:
        overall = jnp.maximum(overall, other)
    total = jnp.exp(value - overall)
    for other in others:
        total = total + jnp.exp(other - overall)
    return overall + jnp.log(total)


def exchange(value, axis, masks):
    size = lax.axis_size(axis)
    return [lax.ppermute(value, axis, [(i, i ^ mask) for i in range(size)]) for mask in masks]


def two_round_lse(value, axis):
    size = lax.axis_size(axis)
    if size == 8:
        value = merge_many(value, exchange(value, axis, [1, 2, 3]))
        return lse_pair(value, exchange(value, axis, [4])[0])
    if size < 4:
        return butterfly_lse(value, axis)
    value = lse_pair(value, exchange(value, axis, [1])[0])
    return merge_many(value, exchange(value, axis, range(2, size, 2)))


def one_round_lse(value, axis):
    size = lax.axis_size(axis)
    if size > 4:
        return two_round_lse(value, axis)
    return merge_many(value, exchange(value, axis, range(1, size)))


def halving_merge(small, numerator, axis):
    size = lax.axis_size(axis)
    me = lax.axis_index(axis)
    rows = small.shape[1] // size
    small = small.reshape(2, size, rows)
    numerator = numerator.reshape(size, rows, numerator.shape[-1])
    step = 1
    while step < size:
        pairs = [(i, i ^ step) for i in range(size)]
        keep = (me // step) % 2
        count = numerator.shape[0] // 2

        def split(x, axis_at):
            x = x.reshape(x.shape[:axis_at] + (count, 2) + x.shape[axis_at + 1:])
            return (
                lax.dynamic_index_in_dim(x, keep, axis=axis_at + 1, keepdims=False),
                lax.dynamic_index_in_dim(x, 1 - keep, axis=axis_at + 1, keepdims=False),
            )

        small_keep, small_send = split(small, 1)
        num_keep, num_send = split(numerator, 0)
        small_other = lax.ppermute(small_send, axis, pairs)
        num_other = lax.ppermute(num_send, axis, pairs)
        overall = jnp.maximum(small_keep[0], small_other[0])
        mine = jnp.exp(small_keep[0] - overall)
        theirs = jnp.exp(small_other[0] - overall)
        numerator = num_keep * mine[..., None] + num_other * theirs[..., None]
        denominator = small_keep[1] * mine + small_other[1] * theirs
        step *= 2
        if step < size:
            small = jnp.stack([overall, denominator])
    return (numerator / denominator[..., None]).reshape(rows, -1)


CHUNK = 64
EXTRA = 16
VMEM_LIMIT = 24 * 1024 * 1024


def tile_slice(ref, b):
    return ref[:, pl.ds(pl.multiple_of(b * BLOCK, BLOCK), BLOCK)]


def row_slice(ref, r):
    return ref[pl.ds(pl.multiple_of(r * BLOCK, BLOCK), BLOCK), :]


def doubled_source(src_ref, r):
    exact = tile_slice(src_ref, r).astype(jnp.float32)
    return (exact * 2.0).astype(jnp.bfloat16), jnp.sum(exact * exact, axis=0, keepdims=True)


def products(doubled, tgt_ref, b):
    return lax.dot_general(doubled, tile_slice(tgt_ref, b), (((0,), (0,)), ((), ())),
                           preferred_element_type=jnp.float32)


def as_row(column, scratch):
    scratch[...] = jnp.broadcast_to(column, scratch.shape)
    return jnp.transpose(scratch[...])[0:1, :]


def as_column(row, scratch):
    scratch[...] = jnp.broadcast_to(row, scratch.shape)
    return jnp.transpose(scratch[...])[:, 0:1]


def by_count(live, slots, body):
    for count in range(1, slots + 1):
        pl.when(live == count)(functools.partial(body, count))


def over_rows(rows, body):
    lax.fori_loop(0, rows, lambda r, c: (body(r), c)[1], 0)


def fill_shifted(blocks_ref, r, count, doubled, tgt_ref, tnorm_ref, tpot_ref, held):
    for k in range(count):
        b = blocks_ref[r, k]
        shift = tile_slice(tpot_ref, b) - tile_slice(tnorm_ref, b)
        held[k] = products(doubled, tgt_ref, b) + shift


def chunk_peak(held, count, rows):
    peak = held[0, rows, :]
    for k in range(1, count):
        peak = jnp.maximum(peak, held[k, rows, :])
    return jnp.max(peak, axis=1, keepdims=True)


def row_kernel(blocks_ref, count_ref, src_ref, tgt_ref, tnorm_ref, tpot_ref,
               lse_ref, held, tgt_aug, rhs, peak_row, total_row):
    width = tgt_ref.shape[0]
    tgt_aug[0:width, :] = tgt_ref[...]
    tgt_aug[width:, :] = split_rows(tpot_ref[...] - tnorm_ref[...], False)

    def per_row(r):
        doubled, snorm = doubled_source(src_ref, r)
        rhs[0:width, :] = doubled
        rhs[width:, :] = split_rows(snorm, True)
        augmented = rhs[...]

        def body(count):
            for k in range(count):
                held[k] = lax.dot_general(tile_slice(tgt_aug, blocks_ref[r, k]), augmented,
                                          (((0,), (0,)), ((), ())),
                                          preferred_element_type=jnp.float32)
            folded = None
            for chunk in range(BLOCK // CHUNK):
                rows = pl.ds(chunk * CHUNK, CHUNK)
                peak = held[0, rows, :]
                for k in range(1, count):
                    peak = jnp.maximum(peak, held[k, rows, :])
                peak = jnp.max(peak.reshape(CHUNK // 8, 8, BLOCK), axis=0)
                folded = peak if folded is None else jnp.maximum(folded, peak)
            peak = jnp.max(folded, axis=0, keepdims=True)
            folded = None
            for chunk in range(BLOCK // CHUNK):
                rows = pl.ds(chunk * CHUNK, CHUNK)
                acc = jnp.exp2((held[0, rows, :] - peak) * BASE2)
                for k in range(1, count):
                    acc = acc + jnp.exp2((held[k, rows, :] - peak) * BASE2)
                acc = jnp.sum(acc.reshape(CHUNK // 8, 8, BLOCK), axis=0)
                folded = acc if folded is None else folded + acc
            peak_row[...] = peak
            total_row[...] = jnp.sum(folded, axis=0, keepdims=True)

        by_count(count_ref[r], held.shape[0], body)
        lanes = pl.ds(pl.multiple_of(r * BLOCK, BLOCK), BLOCK)
        lse_ref[:, lanes] = (peak_row[...] - snorm) * SCALE + jnp.log(total_row[...])

    over_rows(count_ref.shape[0], per_row)


def split_rows(row, ones):
    high = row.astype(jnp.bfloat16).astype(jnp.float32)
    middle = (row - high).astype(jnp.bfloat16).astype(jnp.float32)
    low = row - high - middle
    index = lax.broadcasted_iota(jnp.int32, (EXTRA, row.shape[1]), 0)
    if ones:
        rows = jnp.where(index < 3, 1.0, 0.0)
    else:
        rows = jnp.where(index == 0, high, jnp.where(index == 1, middle,
                                                     jnp.where(index == 2, low, 0.0)))
    return rows.astype(jnp.bfloat16)


def column_kernel(blocks_ref, count_ref, src_ref, spot_ref, tgt_ref, tnorm_ref,
                  lse_ref, top_ref, sum_ref, lhs):
    top_ref[...] = jnp.full(top_ref.shape, SENTINEL, jnp.float32)
    sum_ref[...] = jnp.zeros(sum_ref.shape, jnp.float32)
    width = src_ref.shape[0]

    def per_row(r):
        doubled, snorm = doubled_source(src_ref, r)
        lhs[0:width, :] = doubled
        lhs[width:, :] = split_rows(tile_slice(spot_ref, r) - snorm, False)
        augmented = lhs[...]

        def body(count):
            for k in range(count):
                b = blocks_ref[r, k]
                lanes = pl.ds(pl.multiple_of(b * BLOCK, BLOCK), BLOCK)
                shifted = products(augmented, tgt_ref, b)
                peak = jnp.max(shifted, axis=0, keepdims=True)
                totals = jnp.sum(jnp.exp2((shifted - peak) * BASE2), axis=0, keepdims=True)
                highest = (peak - tnorm_ref[:, lanes]) * SCALE
                old_top = top_ref[:, lanes]
                new_top = jnp.maximum(old_top, highest)
                sum_ref[:, lanes] = (sum_ref[:, lanes] * jnp.exp(old_top - new_top)
                                     + totals * jnp.exp(highest - new_top))
                top_ref[:, lanes] = new_top

        by_count(count_ref[r], blocks_ref.shape[1], body)

    over_rows(count_ref.shape[0], per_row)
    totals = sum_ref[...]
    lse_ref[...] = jnp.where(totals > 0.0, top_ref[...] + jnp.log(totals), SENTINEL)


def project_kernel(blocks_ref, count_ref, src_ref, tgt_ref, tnorm_ref, tpot_ref, feat_ref,
                   small_ref, num_ref, held, weights, tgt_aug, rhs, peak_row, den_row):
    width = tgt_ref.shape[0]
    tgt_aug[0:width, :] = tgt_ref[...]
    tgt_aug[width:, :] = split_rows(tpot_ref[...] - tnorm_ref[...], False)

    def per_row(r):
        doubled, snorm = doubled_source(src_ref, r)
        rhs[0:width, :] = doubled
        rhs[width:, :] = split_rows(snorm, True)
        augmented = rhs[...]

        def body(count):
            for k in range(count):
                held[k] = lax.dot_general(tile_slice(tgt_aug, blocks_ref[r, k]), augmented,
                                          (((0,), (0,)), ((), ())),
                                          preferred_element_type=jnp.float32)
            folded = None
            for chunk in range(BLOCK // CHUNK):
                rows = pl.ds(chunk * CHUNK, CHUNK)
                peak = held[0, rows, :]
                for k in range(1, count):
                    peak = jnp.maximum(peak, held[k, rows, :])
                peak = jnp.max(peak.reshape(CHUNK // 8, 8, BLOCK), axis=0)
                folded = peak if folded is None else jnp.maximum(folded, peak)
            peak = jnp.max(folded, axis=0, keepdims=True)
            folded = None
            for chunk in range(BLOCK // CHUNK):
                rows = pl.ds(chunk * CHUNK, CHUNK)
                acc = jnp.zeros((CHUNK, BLOCK), jnp.float32)
                for k in range(count):
                    rounded = jnp.exp2((held[k, rows, :] - peak) * BASE2).astype(jnp.bfloat16)
                    weights[k, rows, :] = rounded
                    acc = acc + rounded.astype(jnp.float32)
                acc = jnp.sum(acc.reshape(CHUNK // 8, 8, BLOCK), axis=0)
                folded = acc if folded is None else folded + acc
            total = None
            for k in range(count):
                part = jnp.dot(tile_slice(feat_ref, blocks_ref[r, k]), weights[k],
                               preferred_element_type=jnp.float32)
                total = part if total is None else total + part
            num_ref[pl.ds(pl.multiple_of(r * BLOCK, BLOCK), BLOCK), :] = jnp.transpose(total)
            peak_row[...] = peak
            den_row[...] = jnp.sum(folded, axis=0, keepdims=True)

        by_count(count_ref[r], held.shape[0], body)
        lanes = pl.ds(pl.multiple_of(r * BLOCK, BLOCK), BLOCK)
        small_ref[0:1, lanes] = (peak_row[...] - snorm) * SCALE
        small_ref[1:2, lanes] = den_row[...]

    over_rows(count_ref.shape[0], per_row)


def whole(shape):
    return pl.BlockSpec(shape, lambda r, *_: (0,) * len(shape))


def resident():
    return pl.BlockSpec(memory_space=pltpu.VMEM)


def column_scratch():
    return pltpu.VMEM((BLOCK, 1), jnp.float32)


def local_call(kernel, operands, outs, scratch):
    spec = pltpu.PrefetchScalarGridSpec(
        num_scalar_prefetch=2,
        grid=(1,),
        in_specs=[resident() for x in operands[2:]],
        out_specs=[resident() for o in outs],
        scratch_shapes=scratch,
    )
    return pl.pallas_call(
        kernel, grid_spec=spec, out_shape=outs,
        compiler_params=pltpu.CompilerParams(vmem_limit_bytes=VMEM_LIMIT),
    )(*operands)


def row_pass(blocks, counts, src, tgt, tnorm, tpot):
    slots = blocks.shape[1]
    return local_call(
        row_kernel, (blocks, counts, src, tgt, tnorm, tpot),
        [jax.ShapeDtypeStruct((1, src.shape[1]), jnp.float32)],
        [pltpu.VMEM((slots, BLOCK, BLOCK), jnp.float32),
         pltpu.VMEM((tgt.shape[0] + EXTRA, tgt.shape[1]), jnp.bfloat16),
         pltpu.VMEM((src.shape[0] + EXTRA, BLOCK), jnp.bfloat16),
         pltpu.VMEM((1, BLOCK), jnp.float32), pltpu.VMEM((1, BLOCK), jnp.float32)],
    )


def column_pass(blocks, counts, src, spot, tgt_ones, tnorm):
    return local_call(
        column_kernel, (blocks, counts, src, spot, tgt_ones, tnorm),
        [jax.ShapeDtypeStruct(tnorm.shape, jnp.float32)],
        [pltpu.VMEM(tnorm.shape, jnp.float32), pltpu.VMEM(tnorm.shape, jnp.float32),
         pltpu.VMEM((src.shape[0] + EXTRA, BLOCK), jnp.bfloat16)],
    )


def project_pass(blocks, counts, src, tgt, tnorm, tpot, feat):
    rows = src.shape[1]
    slots = blocks.shape[1]
    return local_call(
        project_kernel, (blocks, counts, src, tgt, tnorm, tpot, feat),
        [jax.ShapeDtypeStruct((2, rows), jnp.float32),
         jax.ShapeDtypeStruct((rows, feat.shape[0]), jnp.float32)],
        [pltpu.VMEM((slots, BLOCK, BLOCK), jnp.float32),
         pltpu.VMEM((slots, BLOCK, BLOCK), jnp.bfloat16),
         pltpu.VMEM((tgt.shape[0] + EXTRA, tgt.shape[1]), jnp.bfloat16),
         pltpu.VMEM((src.shape[0] + EXTRA, BLOCK), jnp.bfloat16),
         pltpu.VMEM((1, BLOCK), jnp.float32), pltpu.VMEM((1, BLOCK), jnp.float32)],
    )


def shards(src_emb, tgt_emb, target_features, src_mass, tgt_mass, kept_blocks, kept_count):
    src_rows = src_emb.shape[1]
    tgt_rows = tgt_emb.shape[1]
    src_t = src_emb
    tnorm = jnp.sum(jnp.square(tgt_emb.astype(jnp.float32)), axis=0).reshape(1, tgt_rows)
    counts = kept_count.reshape(-1)
    tgt_ones = jnp.concatenate(
        [tgt_emb, split_rows(jnp.zeros((1, tgt_rows), jnp.float32), True)], axis=0
    )

    tgt_potential = jnp.zeros((tgt_rows,), jnp.float32)
    src_potential = jnp.zeros((src_rows,), jnp.float32)
    for iteration in range(ITERS):
        tpot = tgt_potential.reshape(1, tgt_rows)
        (row_lse,) = row_pass(kept_blocks, counts, src_t, tgt_emb, tnorm, tpot)
        row_lse = one_round_lse(row_lse.reshape(src_rows), "tgt")
        src_potential = EPSILON * jnp.log(src_mass) - EPSILON * row_lse
        (column_lse,) = column_pass(
            kept_blocks, counts, src_t, src_potential.reshape(1, src_rows), tgt_ones, tnorm
        )
        column_lse = two_round_lse(column_lse.reshape(tgt_rows), "src")
        tgt_potential = EPSILON * jnp.log(tgt_mass) - EPSILON * column_lse

    tpot = tgt_potential.reshape(1, tgt_rows)
    small, numerator = project_pass(
        kept_blocks, counts, src_t, tgt_emb, tnorm, tpot, target_features
    )
    projected = halving_merge(small, numerator, "tgt")
    return (projected, src_potential, tgt_potential)


def solution(mesh):
    return jax.shard_map(
        shards,
        mesh=mesh,
        in_specs=(
            P(None, "src"),
            P(None, "tgt"),
            P(None, "tgt"),
            P("src"),
            P("tgt"),
            P("src", "tgt"),
            P("src", "tgt"),
        ),
        out_specs=(P(("src", "tgt"), None), P("src"), P("tgt")),
        check_vma=False,
    )
```

```python
import functools
import math

import jax
import jax.numpy as jnp
from jax import lax
from jax.experimental import pallas as pl
from jax.experimental.pallas import tpu as pltpu
from jax.sharding import PartitionSpec as P

BLOCK = 256
ITERS = 2


SENTINEL = -1e30
EPSILON = 0.1
SCALE = 1.0 / EPSILON
BASE2 = SCALE / math.log(2.0)


def lse_pair(value, other):
    overall = jnp.maximum(value, other)
    return overall + jnp.log(jnp.exp(value - overall) + jnp.exp(other - overall))


def butterfly_lse(value, axis):
    size = lax.axis_size(axis)
    step = 1
    while step < size:
        pairs = [(i, i ^ step) for i in range(size)]
        value = lse_pair(value, lax.ppermute(value, axis, pairs))
        step *= 2
    return value


def merge_many(value, others):
    overall = value
    for other in others:
        overall = jnp.maximum(overall, other)
    total = jnp.exp(value - overall)
    for other in others:
        total = total + jnp.exp(other - overall)
    return overall + jnp.log(total)


def exchange(value, axis, masks):
    size = lax.axis_size(axis)
    return [lax.ppermute(value, axis, [(i, i ^ mask) for i in range(size)]) for mask in masks]


def two_round_lse(value, axis):
    size = lax.axis_size(axis)
    if size < 4:
        return butterfly_lse(value, axis)
    value = lse_pair(value, exchange(value, axis, [1])[0])
    return merge_many(value, exchange(value, axis, range(2, size, 2)))


def one_round_lse(value, axis):
    size = lax.axis_size(axis)
    if size > 4:
        return two_round_lse(value, axis)
    return merge_many(value, exchange(value, axis, range(1, size)))


def halving_merge(small, numerator, axis):
    size = lax.axis_size(axis)
    me = lax.axis_index(axis)
    rows = small.shape[1] // size
    small = small.reshape(2, size, rows)
    numerator = numerator.reshape(size, rows, numerator.shape[-1])
    step = 1
    while step < size:
        pairs = [(i, i ^ step) for i in range(size)]
        keep = (me // step) % 2
        count = numerator.shape[0] // 2

        def split(x, axis_at):
            x = x.reshape(x.shape[:axis_at] + (count, 2) + x.shape[axis_at + 1:])
            return (
                lax.dynamic_index_in_dim(x, keep, axis=axis_at + 1, keepdims=False),
                lax.dynamic_index_in_dim(x, 1 - keep, axis=axis_at + 1, keepdims=False),
            )

        small_keep, small_send = split(small, 1)
        num_keep, num_send = split(numerator, 0)
        small_other = lax.ppermute(small_send, axis, pairs)
        num_other = lax.ppermute(num_send, axis, pairs)
        overall = jnp.maximum(small_keep[0], small_other[0])
        mine = jnp.exp(small_keep[0] - overall)
        theirs = jnp.exp(small_other[0] - overall)
        numerator = num_keep * mine[..., None] + num_other * theirs[..., None]
        denominator = small_keep[1] * mine + small_other[1] * theirs
        step *= 2
        if step < size:
            small = jnp.stack([overall, denominator])
    return (numerator / denominator[..., None]).reshape(rows, -1)


CHUNK = 128
EXTRA = 16
VMEM_LIMIT = 24 * 1024 * 1024


def tile_slice(ref, b):
    return ref[:, pl.ds(pl.multiple_of(b * BLOCK, BLOCK), BLOCK)]


def row_slice(ref, r):
    return ref[pl.ds(pl.multiple_of(r * BLOCK, BLOCK), BLOCK), :]


def doubled_source(src_ref, r):
    exact = tile_slice(src_ref, r).astype(jnp.float32)
    return (exact * 2.0).astype(jnp.bfloat16), jnp.sum(exact * exact, axis=0, keepdims=True)


def products(doubled, tgt_ref, b):
    return lax.dot_general(doubled, tile_slice(tgt_ref, b), (((0,), (0,)), ((), ())),
                           preferred_element_type=jnp.float32)


def as_row(column, scratch):
    scratch[...] = jnp.broadcast_to(column, scratch.shape)
    return jnp.transpose(scratch[...])[0:1, :]


def as_column(row, scratch):
    scratch[...] = jnp.broadcast_to(row, scratch.shape)
    return jnp.transpose(scratch[...])[:, 0:1]


def by_count(live, slots, body):
    for count in range(1, slots + 1):
        pl.when(live == count)(functools.partial(body, count))


def over_rows(rows, body):
    lax.fori_loop(0, rows, lambda r, c: (body(r), c)[1], 0)


def fill_shifted(blocks_ref, r, count, doubled, tgt_ref, tnorm_ref, tpot_ref, held):
    for k in range(count):
        b = blocks_ref[r, k]
        shift = tile_slice(tpot_ref, b) - tile_slice(tnorm_ref, b)
        held[k] = products(doubled, tgt_ref, b) + shift


def chunk_peak(held, count, rows):
    peak = held[0, rows, :]
    for k in range(1, count):
        peak = jnp.maximum(peak, held[k, rows, :])
    return jnp.max(peak, axis=1, keepdims=True)


def row_kernel(blocks_ref, count_ref, src_ref, tgt_ref, tnorm_ref, tpot_ref,
               lse_ref, held, tgt_aug, rhs, peak_row, total_row):
    width = tgt_ref.shape[0]
    tgt_aug[0:width, :] = tgt_ref[...]
    tgt_aug[width:, :] = split_rows(tpot_ref[...] - tnorm_ref[...], False)

    def per_row(r):
        doubled, snorm = doubled_source(src_ref, r)
        rhs[0:width, :] = doubled
        rhs[width:, :] = split_rows(snorm, True)
        augmented = rhs[...]

        def body(count):
            for k in range(count):
                held[k] = lax.dot_general(tile_slice(tgt_aug, blocks_ref[r, k]), augmented,
                                          (((0,), (0,)), ((), ())),
                                          preferred_element_type=jnp.float32)
            folded = None
            for chunk in range(BLOCK // CHUNK):
                rows = pl.ds(chunk * CHUNK, CHUNK)
                peak = held[0, rows, :]
                for k in range(1, count):
                    peak = jnp.maximum(peak, held[k, rows, :])
                peak = jnp.max(peak.reshape(CHUNK // 8, 8, BLOCK), axis=0)
                folded = peak if folded is None else jnp.maximum(folded, peak)
            peak = jnp.max(folded, axis=0, keepdims=True)
            folded = None
            for chunk in range(BLOCK // CHUNK):
                rows = pl.ds(chunk * CHUNK, CHUNK)
                acc = jnp.exp2((held[0, rows, :] - peak) * BASE2)
                for k in range(1, count):
                    acc = acc + jnp.exp2((held[k, rows, :] - peak) * BASE2)
                acc = jnp.sum(acc.reshape(CHUNK // 8, 8, BLOCK), axis=0)
                folded = acc if folded is None else folded + acc
            peak_row[...] = peak
            total_row[...] = jnp.sum(folded, axis=0, keepdims=True)

        by_count(count_ref[r], held.shape[0], body)
        lanes = pl.ds(pl.multiple_of(r * BLOCK, BLOCK), BLOCK)
        lse_ref[:, lanes] = (peak_row[...] - snorm) * SCALE + jnp.log(total_row[...])

    over_rows(count_ref.shape[0], per_row)


def split_rows(row, ones):
    high = row.astype(jnp.bfloat16).astype(jnp.float32)
    middle = (row - high).astype(jnp.bfloat16).astype(jnp.float32)
    low = row - high - middle
    index = lax.broadcasted_iota(jnp.int32, (EXTRA, row.shape[1]), 0)
    if ones:
        rows = jnp.where(index < 3, 1.0, 0.0)
    else:
        rows = jnp.where(index == 0, high, jnp.where(index == 1, middle,
                                                     jnp.where(index == 2, low, 0.0)))
    return rows.astype(jnp.bfloat16)


def column_kernel(blocks_ref, count_ref, src_ref, spot_ref, tgt_ref, tnorm_ref,
                  lse_ref, top_ref, sum_ref, lhs):
    top_ref[...] = jnp.full(top_ref.shape, SENTINEL, jnp.float32)
    sum_ref[...] = jnp.zeros(sum_ref.shape, jnp.float32)
    width = src_ref.shape[0]

    def per_row(r):
        doubled, snorm = doubled_source(src_ref, r)
        lhs[0:width, :] = doubled
        lhs[width:, :] = split_rows(tile_slice(spot_ref, r) - snorm, False)
        augmented = lhs[...]

        def body(count):
            for k in range(count):
                b = blocks_ref[r, k]
                lanes = pl.ds(pl.multiple_of(b * BLOCK, BLOCK), BLOCK)
                shifted = products(augmented, tgt_ref, b)
                peak = jnp.max(shifted, axis=0, keepdims=True)
                totals = jnp.sum(jnp.exp2((shifted - peak) * BASE2), axis=0, keepdims=True)
                highest = (peak - tnorm_ref[:, lanes]) * SCALE
                old_top = top_ref[:, lanes]
                new_top = jnp.maximum(old_top, highest)
                sum_ref[:, lanes] = (sum_ref[:, lanes] * jnp.exp(old_top - new_top)
                                     + totals * jnp.exp(highest - new_top))
                top_ref[:, lanes] = new_top

        by_count(count_ref[r], blocks_ref.shape[1], body)

    over_rows(count_ref.shape[0], per_row)
    totals = sum_ref[...]
    lse_ref[...] = jnp.where(totals > 0.0, top_ref[...] + jnp.log(totals), SENTINEL)


def project_kernel(blocks_ref, count_ref, src_ref, tgt_ref, tnorm_ref, tpot_ref, feat_ref,
                   small_ref, num_ref, held, weights, tgt_aug, rhs, peak_row, den_row):
    width = tgt_ref.shape[0]
    tgt_aug[0:width, :] = tgt_ref[...]
    tgt_aug[width:, :] = split_rows(tpot_ref[...] - tnorm_ref[...], False)

    def per_row(r):
        doubled, snorm = doubled_source(src_ref, r)
        rhs[0:width, :] = doubled
        rhs[width:, :] = split_rows(snorm, True)
        augmented = rhs[...]

        def body(count):
            for k in range(count):
                held[k] = lax.dot_general(tile_slice(tgt_aug, blocks_ref[r, k]), augmented,
                                          (((0,), (0,)), ((), ())),
                                          preferred_element_type=jnp.float32)
            folded = None
            for chunk in range(BLOCK // CHUNK):
                rows = pl.ds(chunk * CHUNK, CHUNK)
                peak = held[0, rows, :]
                for k in range(1, count):
                    peak = jnp.maximum(peak, held[k, rows, :])
                peak = jnp.max(peak.reshape(CHUNK // 8, 8, BLOCK), axis=0)
                folded = peak if folded is None else jnp.maximum(folded, peak)
            peak = jnp.max(folded, axis=0, keepdims=True)
            folded = None
            for chunk in range(BLOCK // CHUNK):
                rows = pl.ds(chunk * CHUNK, CHUNK)
                acc = jnp.zeros((CHUNK, BLOCK), jnp.float32)
                for k in range(count):
                    rounded = jnp.exp2((held[k, rows, :] - peak) * BASE2).astype(jnp.bfloat16)
                    weights[k, rows, :] = rounded
                    acc = acc + rounded.astype(jnp.float32)
                acc = jnp.sum(acc.reshape(CHUNK // 8, 8, BLOCK), axis=0)
                folded = acc if folded is None else folded + acc
            total = None
            for k in range(count):
                part = jnp.dot(tile_slice(feat_ref, blocks_ref[r, k]), weights[k],
                               preferred_element_type=jnp.float32)
                total = part if total is None else total + part
            num_ref[pl.ds(pl.multiple_of(r * BLOCK, BLOCK), BLOCK), :] = jnp.transpose(total)
            peak_row[...] = peak
            den_row[...] = jnp.sum(folded, axis=0, keepdims=True)

        by_count(count_ref[r], held.shape[0], body)
        lanes = pl.ds(pl.multiple_of(r * BLOCK, BLOCK), BLOCK)
        small_ref[0:1, lanes] = (peak_row[...] - snorm) * SCALE
        small_ref[1:2, lanes] = den_row[...]

    over_rows(count_ref.shape[0], per_row)


def whole(shape):
    return pl.BlockSpec(shape, lambda r, *_: (0,) * len(shape))


def resident():
    return pl.BlockSpec(memory_space=pltpu.VMEM)


def column_scratch():
    return pltpu.VMEM((BLOCK, 1), jnp.float32)


def local_call(kernel, operands, outs, scratch):
    spec = pltpu.PrefetchScalarGridSpec(
        num_scalar_prefetch=2,
        grid=(1,),
        in_specs=[resident() for x in operands[2:]],
        out_specs=[resident() for o in outs],
        scratch_shapes=scratch,
    )
    return pl.pallas_call(
        kernel, grid_spec=spec, out_shape=outs,
        compiler_params=pltpu.CompilerParams(vmem_limit_bytes=VMEM_LIMIT),
    )(*operands)


def row_pass(blocks, counts, src, tgt, tnorm, tpot):
    slots = blocks.shape[1]
    return local_call(
        row_kernel, (blocks, counts, src, tgt, tnorm, tpot),
        [jax.ShapeDtypeStruct((1, src.shape[1]), jnp.float32)],
        [pltpu.VMEM((slots, BLOCK, BLOCK), jnp.float32),
         pltpu.VMEM((tgt.shape[0] + EXTRA, tgt.shape[1]), jnp.bfloat16),
         pltpu.VMEM((src.shape[0] + EXTRA, BLOCK), jnp.bfloat16),
         pltpu.VMEM((1, BLOCK), jnp.float32), pltpu.VMEM((1, BLOCK), jnp.float32)],
    )


def column_pass(blocks, counts, src, spot, tgt_ones, tnorm):
    return local_call(
        column_kernel, (blocks, counts, src, spot, tgt_ones, tnorm),
        [jax.ShapeDtypeStruct(tnorm.shape, jnp.float32)],
        [pltpu.VMEM(tnorm.shape, jnp.float32), pltpu.VMEM(tnorm.shape, jnp.float32),
         pltpu.VMEM((src.shape[0] + EXTRA, BLOCK), jnp.bfloat16)],
    )


def project_pass(blocks, counts, src, tgt, tnorm, tpot, feat):
    rows = src.shape[1]
    slots = blocks.shape[1]
    return local_call(
        project_kernel, (blocks, counts, src, tgt, tnorm, tpot, feat),
        [jax.ShapeDtypeStruct((2, rows), jnp.float32),
         jax.ShapeDtypeStruct((rows, feat.shape[0]), jnp.float32)],
        [pltpu.VMEM((slots, BLOCK, BLOCK), jnp.float32),
         pltpu.VMEM((slots, BLOCK, BLOCK), jnp.bfloat16),
         pltpu.VMEM((tgt.shape[0] + EXTRA, tgt.shape[1]), jnp.bfloat16),
         pltpu.VMEM((src.shape[0] + EXTRA, BLOCK), jnp.bfloat16),
         pltpu.VMEM((1, BLOCK), jnp.float32), pltpu.VMEM((1, BLOCK), jnp.float32)],
    )


def shards(src_emb, tgt_emb, target_features, src_mass, tgt_mass, kept_blocks, kept_count):
    src_rows = src_emb.shape[1]
    tgt_rows = tgt_emb.shape[1]
    src_t = src_emb
    tnorm = jnp.sum(jnp.square(tgt_emb.astype(jnp.float32)), axis=0).reshape(1, tgt_rows)
    counts = kept_count.reshape(-1)
    tgt_ones = jnp.concatenate(
        [tgt_emb, split_rows(jnp.zeros((1, tgt_rows), jnp.float32), True)], axis=0
    )

    tgt_potential = jnp.zeros((tgt_rows,), jnp.float32)
    src_potential = jnp.zeros((src_rows,), jnp.float32)
    for iteration in range(ITERS):
        tpot = tgt_potential.reshape(1, tgt_rows)
        (row_lse,) = row_pass(kept_blocks, counts, src_t, tgt_emb, tnorm, tpot)
        row_lse = one_round_lse(row_lse.reshape(src_rows), "tgt")
        src_potential = EPSILON * jnp.log(src_mass) - EPSILON * row_lse
        (column_lse,) = column_pass(
            kept_blocks, counts, src_t, src_potential.reshape(1, src_rows), tgt_ones, tnorm
        )
        column_lse = two_round_lse(column_lse.reshape(tgt_rows), "src")
        tgt_potential = EPSILON * jnp.log(tgt_mass) - EPSILON * column_lse

    tpot = tgt_potential.reshape(1, tgt_rows)
    small, numerator = project_pass(
        kept_blocks, counts, src_t, tgt_emb, tnorm, tpot, target_features
    )
    projected = halving_merge(small, numerator, "tgt")
    return (projected, src_potential, tgt_potential)


def solution(mesh):
    return jax.shard_map(
        shards,
        mesh=mesh,
        in_specs=(
            P(None, "src"),
            P(None, "tgt"),
            P(None, "tgt"),
            P("src"),
            P("tgt"),
            P("src", "tgt"),
            P("src", "tgt"),
        ),
        out_specs=(P(("src", "tgt"), None), P("src"), P("tgt")),
        check_vma=False,
    )
```

```python
import functools
import math

import jax
import jax.numpy as jnp
from jax import lax
from jax.experimental import pallas as pl
from jax.experimental.pallas import tpu as pltpu
from jax.sharding import PartitionSpec as P

BLOCK = 256
ITERS = 2


SENTINEL = -1e30
EPSILON = 0.1
SCALE = 1.0 / EPSILON
BASE2 = SCALE / math.log(2.0)


def lse_pair(value, other):
    overall = jnp.maximum(value, other)
    return overall + jnp.log(jnp.exp(value - overall) + jnp.exp(other - overall))


def butterfly_lse(value, axis):
    size = lax.axis_size(axis)
    step = 1
    while step < size:
        pairs = [(i, i ^ step) for i in range(size)]
        value = lse_pair(value, lax.ppermute(value, axis, pairs))
        step *= 2
    return value


def merge_many(value, others):
    overall = value
    for other in others:
        overall = jnp.maximum(overall, other)
    total = jnp.exp(value - overall)
    for other in others:
        total = total + jnp.exp(other - overall)
    return overall + jnp.log(total)


def exchange(value, axis, masks):
    size = lax.axis_size(axis)
    return [lax.ppermute(value, axis, [(i, i ^ mask) for i in range(size)]) for mask in masks]


def two_round_lse(value, axis):
    size = lax.axis_size(axis)
    if size < 4:
        return butterfly_lse(value, axis)
    value = lse_pair(value, exchange(value, axis, [1])[0])
    return merge_many(value, exchange(value, axis, range(2, size, 2)))


def one_round_lse(value, axis):
    size = lax.axis_size(axis)
    if size > 4:
        return two_round_lse(value, axis)
    return merge_many(value, exchange(value, axis, range(1, size)))


def halving_merge(small, numerator, axis):
    size = lax.axis_size(axis)
    me = lax.axis_index(axis)
    rows = small.shape[1] // size
    small = small.reshape(2, size, rows)
    numerator = numerator.reshape(size, rows, numerator.shape[-1])
    step = 1
    while step < size:
        pairs = [(i, i ^ step) for i in range(size)]
        keep = (me // step) % 2
        count = numerator.shape[0] // 2

        def split(x, axis_at):
            x = x.reshape(x.shape[:axis_at] + (count, 2) + x.shape[axis_at + 1:])
            return (
                lax.dynamic_index_in_dim(x, keep, axis=axis_at + 1, keepdims=False),
                lax.dynamic_index_in_dim(x, 1 - keep, axis=axis_at + 1, keepdims=False),
            )

        small_keep, small_send = split(small, 1)
        num_keep, num_send = split(numerator, 0)
        small_other = lax.ppermute(small_send, axis, pairs)
        num_other = lax.ppermute(num_send, axis, pairs)
        overall = jnp.maximum(small_keep[0], small_other[0])
        mine = jnp.exp(small_keep[0] - overall)
        theirs = jnp.exp(small_other[0] - overall)
        numerator = num_keep * mine[..., None] + num_other * theirs[..., None]
        denominator = small_keep[1] * mine + small_other[1] * theirs
        step *= 2
        if step < size:
            small = jnp.stack([overall, denominator])
    return (numerator / denominator[..., None]).reshape(rows, -1)


CHUNK = 32
EXTRA = 16
VMEM_LIMIT = 24 * 1024 * 1024


def tile_slice(ref, b):
    return ref[:, pl.ds(pl.multiple_of(b * BLOCK, BLOCK), BLOCK)]


def row_slice(ref, r):
    return ref[pl.ds(pl.multiple_of(r * BLOCK, BLOCK), BLOCK), :]


def doubled_source(src_ref, r):
    exact = tile_slice(src_ref, r).astype(jnp.float32)
    return (exact * 2.0).astype(jnp.bfloat16), jnp.sum(exact * exact, axis=0, keepdims=True)


def products(doubled, tgt_ref, b):
    return lax.dot_general(doubled, tile_slice(tgt_ref, b), (((0,), (0,)), ((), ())),
                           preferred_element_type=jnp.float32)


def as_row(column, scratch):
    scratch[...] = jnp.broadcast_to(column, scratch.shape)
    return jnp.transpose(scratch[...])[0:1, :]


def as_column(row, scratch):
    scratch[...] = jnp.broadcast_to(row, scratch.shape)
    return jnp.transpose(scratch[...])[:, 0:1]


def by_count(live, slots, body):
    for count in range(1, slots + 1):
        pl.when(live == count)(functools.partial(body, count))


def over_rows(rows, body):
    lax.fori_loop(0, rows, lambda r, c: (body(r), c)[1], 0)


def fill_shifted(blocks_ref, r, count, doubled, tgt_ref, tnorm_ref, tpot_ref, held):
    for k in range(count):
        b = blocks_ref[r, k]
        shift = tile_slice(tpot_ref, b) - tile_slice(tnorm_ref, b)
        held[k] = products(doubled, tgt_ref, b) + shift


def chunk_peak(held, count, rows):
    peak = held[0, rows, :]
    for k in range(1, count):
        peak = jnp.maximum(peak, held[k, rows, :])
    return jnp.max(peak, axis=1, keepdims=True)


def row_kernel(blocks_ref, count_ref, src_ref, tgt_ref, tnorm_ref, tpot_ref,
               lse_ref, held, tgt_aug, rhs, peak_row, total_row):
    width = tgt_ref.shape[0]
    tgt_aug[0:width, :] = tgt_ref[...]
    tgt_aug[width:, :] = split_rows(tpot_ref[...] - tnorm_ref[...], False)

    def per_row(r):
        doubled, snorm = doubled_source(src_ref, r)
        rhs[0:width, :] = doubled
        rhs[width:, :] = split_rows(snorm, True)
        augmented = rhs[...]

        def body(count):
            for k in range(count):
                held[k] = lax.dot_general(tile_slice(tgt_aug, blocks_ref[r, k]), augmented,
                                          (((0,), (0,)), ((), ())),
                                          preferred_element_type=jnp.float32)
            folded = None
            for chunk in range(BLOCK // CHUNK):
                rows = pl.ds(chunk * CHUNK, CHUNK)
                peak = held[0, rows, :]
                for k in range(1, count):
                    peak = jnp.maximum(peak, held[k, rows, :])
                peak = jnp.max(peak.reshape(CHUNK // 8, 8, BLOCK), axis=0)
                folded = peak if folded is None else jnp.maximum(folded, peak)
            peak = jnp.max(folded, axis=0, keepdims=True)
            folded = None
            for chunk in range(BLOCK // CHUNK):
                rows = pl.ds(chunk * CHUNK, CHUNK)
                acc = jnp.exp2((held[0, rows, :] - peak) * BASE2)
                for k in range(1, count):
                    acc = acc + jnp.exp2((held[k, rows, :] - peak) * BASE2)
                acc = jnp.sum(acc.reshape(CHUNK // 8, 8, BLOCK), axis=0)
                folded = acc if folded is None else folded + acc
            peak_row[...] = peak
            total_row[...] = jnp.sum(folded, axis=0, keepdims=True)

        by_count(count_ref[r], held.shape[0], body)
        lanes = pl.ds(pl.multiple_of(r * BLOCK, BLOCK), BLOCK)
        lse_ref[:, lanes] = (peak_row[...] - snorm) * SCALE + jnp.log(total_row[...])

    over_rows(count_ref.shape[0], per_row)


def split_rows(row, ones):
    high = row.astype(jnp.bfloat16).astype(jnp.float32)
    middle = (row - high).astype(jnp.bfloat16).astype(jnp.float32)
    low = row - high - middle
    index = lax.broadcasted_iota(jnp.int32, (EXTRA, row.shape[1]), 0)
    if ones:
        rows = jnp.where(index < 3, 1.0, 0.0)
    else:
        rows = jnp.where(index == 0, high, jnp.where(index == 1, middle,
                                                     jnp.where(index == 2, low, 0.0)))
    return rows.astype(jnp.bfloat16)


def column_kernel(blocks_ref, count_ref, src_ref, spot_ref, tgt_ref, tnorm_ref,
                  lse_ref, top_ref, sum_ref, lhs):
    top_ref[...] = jnp.full(top_ref.shape, SENTINEL, jnp.float32)
    sum_ref[...] = jnp.zeros(sum_ref.shape, jnp.float32)
    width = src_ref.shape[0]

    def per_row(r):
        doubled, snorm = doubled_source(src_ref, r)
        lhs[0:width, :] = doubled
        lhs[width:, :] = split_rows(tile_slice(spot_ref, r) - snorm, False)
        augmented = lhs[...]

        def body(count):
            for k in range(count):
                b = blocks_ref[r, k]
                lanes = pl.ds(pl.multiple_of(b * BLOCK, BLOCK), BLOCK)
                shifted = products(augmented, tgt_ref, b)
                peak = jnp.max(shifted, axis=0, keepdims=True)
                totals = jnp.sum(jnp.exp2((shifted - peak) * BASE2), axis=0, keepdims=True)
                highest = (peak - tnorm_ref[:, lanes]) * SCALE
                old_top = top_ref[:, lanes]
                new_top = jnp.maximum(old_top, highest)
                sum_ref[:, lanes] = (sum_ref[:, lanes] * jnp.exp(old_top - new_top)
                                     + totals * jnp.exp(highest - new_top))
                top_ref[:, lanes] = new_top

        by_count(count_ref[r], blocks_ref.shape[1], body)

    over_rows(count_ref.shape[0], per_row)
    totals = sum_ref[...]
    lse_ref[...] = jnp.where(totals > 0.0, top_ref[...] + jnp.log(totals), SENTINEL)


def project_kernel(blocks_ref, count_ref, src_ref, tgt_ref, tnorm_ref, tpot_ref, feat_ref,
                   small_ref, num_ref, held, weights, tgt_aug, rhs, peak_row, den_row):
    width = tgt_ref.shape[0]
    tgt_aug[0:width, :] = tgt_ref[...]
    tgt_aug[width:, :] = split_rows(tpot_ref[...] - tnorm_ref[...], False)

    def per_row(r):
        doubled, snorm = doubled_source(src_ref, r)
        rhs[0:width, :] = doubled
        rhs[width:, :] = split_rows(snorm, True)
        augmented = rhs[...]

        def body(count):
            for k in range(count):
                held[k] = lax.dot_general(tile_slice(tgt_aug, blocks_ref[r, k]), augmented,
                                          (((0,), (0,)), ((), ())),
                                          preferred_element_type=jnp.float32)
            folded = None
            for chunk in range(BLOCK // CHUNK):
                rows = pl.ds(chunk * CHUNK, CHUNK)
                peak = held[0, rows, :]
                for k in range(1, count):
                    peak = jnp.maximum(peak, held[k, rows, :])
                peak = jnp.max(peak.reshape(CHUNK // 8, 8, BLOCK), axis=0)
                folded = peak if folded is None else jnp.maximum(folded, peak)
            peak = jnp.max(folded, axis=0, keepdims=True)
            folded = None
            for chunk in range(BLOCK // CHUNK):
                rows = pl.ds(chunk * CHUNK, CHUNK)
                acc = jnp.zeros((CHUNK, BLOCK), jnp.float32)
                for k in range(count):
                    rounded = jnp.exp2((held[k, rows, :] - peak) * BASE2).astype(jnp.bfloat16)
                    weights[k, rows, :] = rounded
                    acc = acc + rounded.astype(jnp.float32)
                acc = jnp.sum(acc.reshape(CHUNK // 8, 8, BLOCK), axis=0)
                folded = acc if folded is None else folded + acc
            total = None
            for k in range(count):
                part = jnp.dot(tile_slice(feat_ref, blocks_ref[r, k]), weights[k],
                               preferred_element_type=jnp.float32)
                total = part if total is None else total + part
            num_ref[pl.ds(pl.multiple_of(r * BLOCK, BLOCK), BLOCK), :] = jnp.transpose(total)
            peak_row[...] = peak
            den_row[...] = jnp.sum(folded, axis=0, keepdims=True)

        by_count(count_ref[r], held.shape[0], body)
        lanes = pl.ds(pl.multiple_of(r * BLOCK, BLOCK), BLOCK)
        small_ref[0:1, lanes] = (peak_row[...] - snorm) * SCALE
        small_ref[1:2, lanes] = den_row[...]

    over_rows(count_ref.shape[0], per_row)


def whole(shape):
    return pl.BlockSpec(shape, lambda r, *_: (0,) * len(shape))


def resident():
    return pl.BlockSpec(memory_space=pltpu.VMEM)


def column_scratch():
    return pltpu.VMEM((BLOCK, 1), jnp.float32)


def local_call(kernel, operands, outs, scratch):
    spec = pltpu.PrefetchScalarGridSpec(
        num_scalar_prefetch=2,
        grid=(1,),
        in_specs=[resident() for x in operands[2:]],
        out_specs=[resident() for o in outs],
        scratch_shapes=scratch,
    )
    return pl.pallas_call(
        kernel, grid_spec=spec, out_shape=outs,
        compiler_params=pltpu.CompilerParams(vmem_limit_bytes=VMEM_LIMIT),
    )(*operands)


def row_pass(blocks, counts, src, tgt, tnorm, tpot):
    slots = blocks.shape[1]
    return local_call(
        row_kernel, (blocks, counts, src, tgt, tnorm, tpot),
        [jax.ShapeDtypeStruct((1, src.shape[1]), jnp.float32)],
        [pltpu.VMEM((slots, BLOCK, BLOCK), jnp.float32),
         pltpu.VMEM((tgt.shape[0] + EXTRA, tgt.shape[1]), jnp.bfloat16),
         pltpu.VMEM((src.shape[0] + EXTRA, BLOCK), jnp.bfloat16),
         pltpu.VMEM((1, BLOCK), jnp.float32), pltpu.VMEM((1, BLOCK), jnp.float32)],
    )


def column_pass(blocks, counts, src, spot, tgt_ones, tnorm):
    return local_call(
        column_kernel, (blocks, counts, src, spot, tgt_ones, tnorm),
        [jax.ShapeDtypeStruct(tnorm.shape, jnp.float32)],
        [pltpu.VMEM(tnorm.shape, jnp.float32), pltpu.VMEM(tnorm.shape, jnp.float32),
         pltpu.VMEM((src.shape[0] + EXTRA, BLOCK), jnp.bfloat16)],
    )


def project_pass(blocks, counts, src, tgt, tnorm, tpot, feat):
    rows = src.shape[1]
    slots = blocks.shape[1]
    return local_call(
        project_kernel, (blocks, counts, src, tgt, tnorm, tpot, feat),
        [jax.ShapeDtypeStruct((2, rows), jnp.float32),
         jax.ShapeDtypeStruct((rows, feat.shape[0]), jnp.float32)],
        [pltpu.VMEM((slots, BLOCK, BLOCK), jnp.float32),
         pltpu.VMEM((slots, BLOCK, BLOCK), jnp.bfloat16),
         pltpu.VMEM((tgt.shape[0] + EXTRA, tgt.shape[1]), jnp.bfloat16),
         pltpu.VMEM((src.shape[0] + EXTRA, BLOCK), jnp.bfloat16),
         pltpu.VMEM((1, BLOCK), jnp.float32), pltpu.VMEM((1, BLOCK), jnp.float32)],
    )


def shards(src_emb, tgt_emb, target_features, src_mass, tgt_mass, kept_blocks, kept_count):
    src_rows = src_emb.shape[1]
    tgt_rows = tgt_emb.shape[1]
    src_t = src_emb
    tnorm = jnp.sum(jnp.square(tgt_emb.astype(jnp.float32)), axis=0).reshape(1, tgt_rows)
    counts = kept_count.reshape(-1)
    tgt_ones = jnp.concatenate(
        [tgt_emb, split_rows(jnp.zeros((1, tgt_rows), jnp.float32), True)], axis=0
    )

    tgt_potential = jnp.zeros((tgt_rows,), jnp.float32)
    src_potential = jnp.zeros((src_rows,), jnp.float32)
    for iteration in range(ITERS):
        tpot = tgt_potential.reshape(1, tgt_rows)
        (row_lse,) = row_pass(kept_blocks, counts, src_t, tgt_emb, tnorm, tpot)
        row_lse = one_round_lse(row_lse.reshape(src_rows), "tgt")
        src_potential = EPSILON * jnp.log(src_mass) - EPSILON * row_lse
        (column_lse,) = column_pass(
            kept_blocks, counts, src_t, src_potential.reshape(1, src_rows), tgt_ones, tnorm
        )
        column_lse = two_round_lse(column_lse.reshape(tgt_rows), "src")
        tgt_potential = EPSILON * jnp.log(tgt_mass) - EPSILON * column_lse

    tpot = tgt_potential.reshape(1, tgt_rows)
    small, numerator = project_pass(
        kept_blocks, counts, src_t, tgt_emb, tnorm, tpot, target_features
    )
    projected = halving_merge(small, numerator, "tgt")
    return (projected, src_potential, tgt_potential)


def solution(mesh):
    return jax.shard_map(
        shards,
        mesh=mesh,
        in_specs=(
            P(None, "src"),
            P(None, "tgt"),
            P(None, "tgt"),
            P("src"),
            P("tgt"),
            P("src", "tgt"),
            P("src", "tgt"),
        ),
        out_specs=(P(("src", "tgt"), None), P("src"), P("tgt")),
        check_vma=False,
    )
```
